256 devices in a mesh: dp: 4 (over y), ctx: 32 (over x, z_lo, core), tp: 2 (over z_hi).
Axes of the slice: x: 4, y: 4, z: 8 (z_hi: 2, z_lo: 4; z = z_hi * 4 + z_lo), core: 2. Of those that a mesh axis runs over, the one named last changes fastest.
Arguments:
- projected: bfloat16 [4, 3, 4096, 8192], P('dp', None, 'tp', 'ctx'), may hold values from -6 to 6
- cotangent: bfloat16 [4, 4096, 8192], P('dp', None, ('ctx', 'tp')), may hold values from -6 to 6
- short_filter: float32 [3, 3, 4096], P(None, None, 'tp'), may hold values from -3 to 3
- residues: float32 [4096, 16], P('tp'), may hold values from -3 to 3
- decay_rate: float32 [4096, 16], P('tp'), may hold values from 3.0517578e-05 to 0.035
- skip_gain: float32 [4096], P('tp'), may hold values from -1 to 1
Outputs:
- hyena_out: bfloat16 [4, 4096, 8192], P('dp', 'tp', 'ctx')
- input_grad: bfloat16 [4, 3, 4096, 8192], P('dp', None, 'tp', 'ctx')
- residue_grad: float32 [4096, 16], P('tp')
- skip_grad: float32 [4096], P('tp')
The draws below stay inside these ranges and needn't reach their ends.
All inputs are finite; a program needn't handle non-finite values.
Results may differ from the reference program's by a relative error of at most 0.0076.
Values may be sent and summed in bfloat16 or wider, within the bound.
No kernel may reach another device: no remote copies, remote signals or barrier semaphores. Data moves between devices by JAX's collectives and lax.ppermute only.
A program may use at most 128 MiB of HBM per device.

```python
import math
import jax
import jax.numpy as jnp
from jax import lax

D = 4096
ORDER = 16
SHORT = 3
SEQ = 8192
SAMPLES = 4


def block_levels(own_key, dims, cuts, low, top_value):
    def one(dim, shards_of):
        draws = jax.random.uniform(jax.random.fold_in(jax.random.fold_in(own_key, 6), dim), (shards_of,), jnp.float32, low / len(cuts), top_value / len(cuts))
        return jnp.repeat(jnp.exp(draws), dims[dim] // shards_of).reshape((-1,) + (1,) * (len(dims) - dim - 1))

    level = one(*cuts[0])
    for cut in cuts[1:]:
        level = level * one(*cut)
    return level


def bell_draw(stream_key, shape, width, most, split=(), held_as=jnp.bfloat16):
    entries = jax.random.normal(stream_key, shape, jnp.float32) * width
    if len(split) > 0:
        entries = block_levels(stream_key, shape, split, -0.22, 0.18) * entries
    return jnp.clip(entries, min=-most, max=most).astype(held_as)


def setup_inputs(seed: int = 0) -> dict:
    arg_keys = jax.random.split(jax.random.key(seed), 7)
    return {
        "projected": bell_draw(arg_keys[0], (SAMPLES, 3, D, SEQ), 1.0, 6.0, ((0, 4), (2, 2), (3, 32))),
        "cotangent": bell_draw(arg_keys[1], (SAMPLES, D, SEQ), 1.0, 6.0, ((0, 4), (2, 64))),
        "short_filter": bell_draw(arg_keys[2], (3, SHORT, D), 0.6, 3.0, ((2, 2),), jnp.float32),
        "residues": bell_draw(arg_keys[3], (D, ORDER), 0.35, 3.0, ((0, 2),), jnp.float32),
        "decay_rate": jnp.clip(jnp.exp(math.log(0.035) - 7.0448005 * jax.random.uniform(arg_keys[4], (D, ORDER), jnp.float32) ** block_levels(arg_keys[4], (D, ORDER), ((0, 2),), -0.2, 0.2)), 3.0517578125e-05, 0.035),
        "skip_gain": jnp.clip(jax.random.uniform(arg_keys[5], (D,), jnp.float32, -1.0, 1.0) * block_levels(arg_keys[5], (D,), ((0, 2),), -0.4, 0.0), -1.0, 1.0),
    }


exact_mode = lax.Precision.HIGHEST

def rounded(values):
    return lax.optimization_barrier(values.astype(jnp.bfloat16)).astype(jnp.float32)

def causal_taps(signal, tap_weights):
    length = signal.shape[2]
    result = tap_weights[:, 0, :, None] * signal
    for lag_index in range(1, SHORT):
        shifted = jnp.pad(signal, ((0, 0), (0, 0), (lag_index, 0)))[:, :, :length]
        result = result + tap_weights[:, lag_index, :, None] * shifted
    return result

def anticausal_taps(signal, tap_weights):
    result = tap_weights[:, 0, :, None] * signal
    for lag_index in range(1, SHORT):
        shifted = jnp.pad(signal, ((0, 0), (0, 0), (0, lag_index)))[:, :, lag_index:]
        result = result + tap_weights[:, lag_index, :, None] * shifted
    return result

def long_block(group_items):
    product, adjoint, rate_rows, residue_rows, gain_rows = group_items
    length = product.shape[1]
    lag_values = jnp.arange(length).astype(rate_rows.dtype)
    falloff = jnp.exp(-rate_rows[:, :, None] * lag_values)
    root_rate = jnp.sqrt(2.0 * rate_rows)
    kernel = jnp.einsum('cn,cnl->cl', residue_rows * root_rate, falloff, precision=exact_mode)
    padded = 2 * length
    product_freq = jnp.fft.rfft(product, padded, axis=1)
    adjoint_freq = jnp.fft.rfft(adjoint, padded, axis=1)
    kernel_freq = jnp.fft.rfft(kernel, padded, axis=1)
    forward = jnp.fft.irfft(product_freq * kernel_freq, padded, axis=1)[:, :length]
    forward = forward + gain_rows[:, None] * product
    backward = jnp.fft.irfft(adjoint_freq * jnp.conj(kernel_freq), padded, axis=1)[:, :length]
    backward = backward + gain_rows[:, None] * adjoint
    lagged = jnp.fft.irfft(adjoint_freq * jnp.conj(product_freq), padded, axis=1)[:, :length]
    mode_raw = root_rate * jnp.einsum('cl,cnl->cn', lagged, falloff, precision=exact_mode)
    skip_raw = lax.optimization_barrier(jnp.sum(adjoint * product, axis=1))
    return (forward.astype(jnp.bfloat16), backward.astype(jnp.bfloat16), mode_raw, skip_raw)

def reference(projected, cotangent, short_filter, residues, decay_rate, skip_gain):
    block_total = D // 64

    def one_sample(sample_items):
        proj_rows, grad_rows = sample_items
        featured = rounded(causal_taps(proj_rows.astype(jnp.float32), short_filter))
        query_feat = featured[0]
        key_feat = featured[1]
        value_feat = featured[2]
        product = rounded(key_feat * value_feat)
        grad_out = grad_rows.astype(jnp.float32)
        adjoint = rounded(grad_out * query_feat)
        stacked = (product.reshape(block_total, 64, SEQ), adjoint.reshape(block_total, 64, SEQ), decay_rate.reshape(block_total, 64, ORDER), residues.reshape(block_total, 64, ORDER), skip_gain.reshape(block_total, 64))
        forward, backward, mode_raw, skip_raw = lax.map(long_block, stacked)
        forward = forward.reshape(D, SEQ).astype(jnp.float32)
        backward = backward.reshape(D, SEQ).astype(jnp.float32)
        hyena_out = (query_feat * forward).astype(jnp.bfloat16)
        feature_grad = rounded(jnp.stack([grad_out * forward, backward * value_feat, backward * key_feat]))
        input_grad = anticausal_taps(feature_grad, short_filter).astype(jnp.bfloat16)
        return (hyena_out, input_grad, mode_raw.reshape(D, ORDER), skip_raw.reshape(D))
    outputs = lax.map(one_sample, (projected, cotangent))
    grad_scale = 1.0 / jnp.sqrt(jnp.asarray(SEQ * SAMPLES, dtype=residues.dtype))
    residue_grad = lax.optimization_barrier(jnp.sum(outputs[2], axis=0)) * grad_scale
    skip_grad = lax.optimization_barrier(jnp.sum(outputs[3], axis=0)) * grad_scale
    return (outputs[0], outputs[1], residue_grad, skip_grad)
```

```python
from functools import partial
import math

import jax
import jax.numpy as jnp
from jax import lax
from jax.sharding import PartitionSpec as P

exact_mode = lax.Precision.HIGHEST
data_mode = lax.Precision.HIGH


def from_behind(shard, axis, by):
    count = lax.axis_size(axis)
    pairs = [(i, i + by) for i in range(count) if 0 <= i + by < count]
    return lax.ppermute(shard, axis, pairs)


def causal_short(proj_rows, prev_rim, tap_weights):
    rim_width = prev_rim.shape[2]
    token_count = proj_rows.shape[2]
    extended = jnp.concatenate([prev_rim, proj_rows], axis=2).astype(jnp.float32)
    result = tap_weights[:, 0, :, None] * extended[:, :, rim_width : rim_width + token_count]
    for lag_index in range(1, rim_width + 1):
        start_at = rim_width - lag_index
        result = (
            result
            + tap_weights[:, lag_index, :, None] * extended[:, :, start_at : start_at + token_count]
        )
    return result


def anticausal_short(grad_rows, next_rim, tap_weights):
    rim_width = next_rim.shape[2]
    token_count = grad_rows.shape[2]
    extended = jnp.concatenate([grad_rows, next_rim], axis=2).astype(jnp.float32)
    result = tap_weights[:, 0, :, None] * extended[:, :, :token_count]
    for lag_index in range(1, rim_width + 1):
        result = (
            result
            + tap_weights[:, lag_index, :, None]
            * extended[:, :, lag_index : lag_index + token_count]
        )
    return result


def make_tables(rate_rows, block_len):
    offsets = jnp.arange(block_len, dtype=jnp.float32)
    fall_now = jnp.exp(-rate_rows[:, :, None] * offsets)
    rise_now = jnp.exp(rate_rows[:, :, None] * offsets)
    fall_next = jnp.exp(-rate_rows[:, :, None] * (offsets + 1.0))
    fall_tail = jnp.exp(-rate_rows[:, :, None] * (block_len - 1.0 - offsets))
    lower_mask = offsets[:, None] >= offsets[None, :]
    return (fall_now, rise_now, fall_next, fall_tail, lower_mask)


def chain_link(earlier, later):
    return (earlier[0] * later[0], later[0] * earlier[1] + later[1])


def modal_pass(signal, rate_rows, weights, incoming, tables):
    fall_now, rise_now, fall_next, fall_tail, lower_mask = tables
    block_len = fall_now.shape[2]
    chan_count, length = signal.shape
    block_count = length // block_len
    pieces = signal.reshape(chan_count, block_count, block_len)
    kernel = jnp.einsum(
        "cnt,cns->cts", weights[:, :, None] * fall_now, rise_now, precision=exact_mode
    )
    kernel = jnp.where(lower_mask[None], kernel, 0.0)
    inside = jnp.einsum("cts,cbs->cbt", kernel, pieces, precision=data_mode)
    block_ends = jnp.einsum("cns,cbs->cnb", fall_tail, pieces, precision=data_mode)
    span_decay = jnp.exp(-rate_rows * block_len)
    block_mults = jnp.broadcast_to(span_decay[:, :, None], block_ends.shape)
    _, running = lax.associative_scan(chain_link, (block_mults, block_ends), axis=2)
    block_steps = jnp.arange(block_count, dtype=jnp.float32)
    before = jnp.concatenate([jnp.zeros_like(running[:, :, :1]), running[:, :, :-1]], axis=2)
    before = (
        before + jnp.exp(-rate_rows[:, :, None] * block_len * block_steps) * incoming[:, :, None]
    )
    carry_in = jnp.einsum(
        "cnt,cnb->cbt", weights[:, :, None] * fall_next, before, precision=exact_mode
    )
    return ((inside + carry_in).reshape(chan_count, length), before)


def mode_products(signal, adjoint, before, tables):
    fall_now, rise_now, fall_next, fall_tail, lower_mask = tables
    block_len = fall_now.shape[2]
    chan_count, length = signal.shape
    block_count = length // block_len
    pieces = signal.reshape(chan_count, block_count, block_len)
    dual_pieces = adjoint.reshape(chan_count, block_count, block_len)
    crossed = jnp.einsum("cbt,cbs->cts", dual_pieces, pieces, precision=data_mode)
    crossed = jnp.where(lower_mask[None], crossed, 0.0)
    weighted = jnp.einsum("cts,cnt->cns", crossed, fall_now, precision=exact_mode)
    inside = jnp.sum(weighted * rise_now, axis=2)
    carried = jnp.einsum("cbt,cnt->cnb", dual_pieces, fall_next, precision=data_mode)
    return inside + jnp.sum(carried * before, axis=2)


def channel_group(group_items, block_len):
    (
        forward_narrow,
        backward_narrow,
        rate_rows,
        weights,
        gain_rows,
        enter_forward,
        enter_backward,
    ) = group_items
    forward_rows = forward_narrow.astype(jnp.float32)
    backward_rows = backward_narrow.astype(jnp.float32)
    tables = make_tables(rate_rows, block_len)
    carried, before = modal_pass(forward_rows, rate_rows, weights, enter_forward, tables)
    returned, _ = modal_pass(jnp.flip(backward_rows, 1), rate_rows, weights, enter_backward, tables)
    signal = (carried + gain_rows[:, None] * forward_rows).astype(jnp.bfloat16)
    back_signal = (jnp.flip(returned, 1) + gain_rows[:, None] * backward_rows).astype(jnp.bfloat16)
    mode_raw = mode_products(forward_rows, backward_rows, before, tables)
    skip_raw = jnp.sum(backward_rows * forward_rows, axis=1)
    return (signal, back_signal, mode_raw, skip_raw)


def grouped(function, arrays, group_size):
    stacked = tuple(
        (
            item.reshape((item.shape[0] // group_size, group_size) + item.shape[1:])
            for item in arrays
        )
    )
    results = lax.map(function, stacked)
    return tuple(
        (item.reshape((item.shape[0] * item.shape[1],) + item.shape[2:]) for item in results)
    )


def on_device(projected, cotangent, short_filter, residues, decay_rate, skip_gain):
    proj_rows = projected[0]
    token_count = proj_rows.shape[2]
    chans_tp = proj_rows.shape[1]
    rim_width = short_filter.shape[1] - 1
    grad_out = lax.all_to_all(cotangent[0], "tp", split_axis=0, concat_axis=1, tiled=True).astype(
        jnp.float32
    )
    prev_rim = from_behind(proj_rows[:, :, token_count - rim_width :], "ctx", 1)
    featured = lax.optimization_barrier(
        causal_short(proj_rows, prev_rim, short_filter).astype(jnp.bfloat16)
    )
    query_feat = featured[0].astype(jnp.float32)
    key_feat = featured[1].astype(jnp.float32)
    value_feat = featured[2].astype(jnp.float32)
    product = (key_feat * value_feat).astype(jnp.bfloat16)
    adjoint = (grad_out * query_feat).astype(jnp.bfloat16)
    ctx_count = lax.axis_size("ctx")
    token_total = token_count * ctx_count * lax.axis_size("dp")
    weight_all = residues * jnp.sqrt(2.0 * decay_rate)
    product_all, adjoint_all = (
        lax.all_to_all(product, "ctx", split_axis=0, concat_axis=1, tiled=True),
        lax.all_to_all(adjoint, "ctx", split_axis=0, concat_axis=1, tiled=True),
    )
    chan_count = chans_tp // ctx_count
    chan_start = lax.axis_index("ctx") * chan_count
    rate_rows = lax.dynamic_slice_in_dim(decay_rate, chan_start, chan_count, 0)
    weight_rows = lax.dynamic_slice_in_dim(weight_all, chan_start, chan_count, 0)
    gain_rows = lax.dynamic_slice_in_dim(skip_gain, chan_start, chan_count, 0)
    length = product_all.shape[1]
    block_len = math.gcd(256, length)
    group_size = math.gcd(chan_count, 2**21 // (block_len * block_len))
    zero_state = jnp.zeros(rate_rows.shape, jnp.float32)
    conv_rows, back_rows, mode_part, skip_part = grouped(
        partial(channel_group, block_len=block_len),
        (product_all, adjoint_all, rate_rows, weight_rows, gain_rows, zero_state, zero_state),
        group_size,
    )
    signal, back_signal = (
        lax.all_to_all(conv_rows, "ctx", split_axis=1, concat_axis=0, tiled=True),
        lax.all_to_all(back_rows, "ctx", split_axis=1, concat_axis=0, tiled=True),
    )
    grad_scale = 1.0 / math.sqrt(token_total)
    local_grads = jnp.concatenate(
        [mode_part * jnp.sqrt(2.0 * rate_rows) * grad_scale, skip_part[:, None] * grad_scale], axis=1
    )
    local_grads = lax.psum(local_grads, "dp")
    spread = jnp.broadcast_to(local_grads[None], (ctx_count,) + local_grads.shape)
    gathered = lax.all_to_all(spread, "ctx", split_axis=0, concat_axis=0, tiled=True)
    gathered = gathered.reshape(chans_tp, local_grads.shape[1])
    residue_grad = gathered[:, : mode_part.shape[1]]
    skip_grad = gathered[:, mode_part.shape[1]]
    conv_wide = signal.astype(jnp.float32)
    back_wide = back_signal.astype(jnp.float32)
    hyena_out = (query_feat * conv_wide).astype(jnp.bfloat16)
    feature_grad = jnp.stack(
        [grad_out * conv_wide, back_wide * value_feat, back_wide * key_feat]
    ).astype(jnp.bfloat16)
    next_rim = from_behind(feature_grad[:, :, :rim_width], "ctx", -1)
    input_grad = anticausal_short(feature_grad, next_rim, short_filter).astype(jnp.bfloat16)
    return (hyena_out[None], input_grad[None], residue_grad, skip_grad)


def solution(mesh):
    placed = (
        P("dp", None, "tp", "ctx"),
        P("dp", None, ("ctx", "tp")),
        P(None, None, "tp"),
        P("tp", None),
        P("tp", None),
        P("tp"),
    )
    return jax.shard_map(
        on_device,
        mesh=mesh,
        in_specs=placed,
        out_specs=(P("dp", "tp", "ctx"), P("dp", None, "tp", "ctx"), P("tp", None), P("tp")),
        check_vma=False,
    )
```

```python
from functools import partial
import math

import jax
import jax.numpy as jnp
from jax import lax
from jax.sharding import PartitionSpec as P
from jax.experimental import pallas as pl
from jax.experimental.pallas import tpu as pltpu

exact_mode = lax.Precision.HIGHEST
data_mode = lax.Precision.HIGH


def from_behind(shard, axis, by):
    count = lax.axis_size(axis)
    pairs = [(i, i + by) for i in range(count) if 0 <= i + by < count]
    return lax.ppermute(shard, axis, pairs)


def causal_short(proj_rows, prev_rim, tap_weights):
    rim_width = prev_rim.shape[2]
    token_count = proj_rows.shape[2]
    extended = jnp.concatenate([prev_rim, proj_rows], axis=2).astype(jnp.float32)
    result = tap_weights[:, 0, :, None] * extended[:, :, rim_width : rim_width + token_count]
    for lag_index in range(1, rim_width + 1):
        start_at = rim_width - lag_index
        result = (
            result
            + tap_weights[:, lag_index, :, None] * extended[:, :, start_at : start_at + token_count]
        )
    return result


def anticausal_short(grad_rows, next_rim, tap_weights):
    rim_width = next_rim.shape[2]
    token_count = grad_rows.shape[2]
    extended = jnp.concatenate([grad_rows, next_rim], axis=2).astype(jnp.float32)
    result = tap_weights[:, 0, :, None] * extended[:, :, :token_count]
    for lag_index in range(1, rim_width + 1):
        result = (
            result
            + tap_weights[:, lag_index, :, None]
            * extended[:, :, lag_index : lag_index + token_count]
        )
    return result


def make_tables(rate_rows, block_len):
    offsets = jnp.arange(block_len, dtype=jnp.float32)
    fall_now = jnp.exp(-rate_rows[:, :, None] * offsets)
    rise_now = jnp.exp(rate_rows[:, :, None] * offsets)
    fall_next = jnp.exp(-rate_rows[:, :, None] * (offsets + 1.0))
    fall_tail = jnp.exp(-rate_rows[:, :, None] * (block_len - 1.0 - offsets))
    lower_mask = offsets[:, None] >= offsets[None, :]
    return (fall_now, rise_now, fall_next, fall_tail, lower_mask)


def chain_link(earlier, later):
    return (earlier[0] * later[0], later[0] * earlier[1] + later[1])


def modal_pass(signal, rate_rows, weights, incoming, tables):
    fall_now, rise_now, fall_next, fall_tail, lower_mask = tables
    block_len = fall_now.shape[2]
    chan_count, length = signal.shape
    block_count = length // block_len
    pieces = signal.reshape(chan_count, block_count, block_len)
    kernel = jnp.einsum(
        "cnt,cns->cts", weights[:, :, None] * fall_now, rise_now, precision=exact_mode
    )
    kernel = jnp.where(lower_mask[None], kernel, 0.0)
    inside = jnp.einsum("cts,cbs->cbt", kernel, pieces, precision=data_mode)
    block_ends = jnp.einsum("cns,cbs->cnb", fall_tail, pieces, precision=data_mode)
    span_decay = jnp.exp(-rate_rows * block_len)
    block_mults = jnp.broadcast_to(span_decay[:, :, None], block_ends.shape)
    _, running = lax.associative_scan(chain_link, (block_mults, block_ends), axis=2)
    block_steps = jnp.arange(block_count, dtype=jnp.float32)
    before = jnp.concatenate([jnp.zeros_like(running[:, :, :1]), running[:, :, :-1]], axis=2)
    before = (
        before + jnp.exp(-rate_rows[:, :, None] * block_len * block_steps) * incoming[:, :, None]
    )
    carry_in = jnp.einsum(
        "cnt,cnb->cbt", weights[:, :, None] * fall_next, before, precision=exact_mode
    )
    return ((inside + carry_in).reshape(chan_count, length), before)


def mode_products(signal, adjoint, before, tables):
    fall_now, rise_now, fall_next, fall_tail, lower_mask = tables
    block_len = fall_now.shape[2]
    chan_count, length = signal.shape
    block_count = length // block_len
    pieces = signal.reshape(chan_count, block_count, block_len)
    dual_pieces = adjoint.reshape(chan_count, block_count, block_len)
    crossed = jnp.einsum("cbt,cbs->cts", dual_pieces, pieces, precision=data_mode)
    crossed = jnp.where(lower_mask[None], crossed, 0.0)
    weighted = jnp.einsum("cts,cnt->cns", crossed, fall_now, precision=exact_mode)
    inside = jnp.sum(weighted * rise_now, axis=2)
    carried = jnp.einsum("cbt,cnt->cnb", dual_pieces, fall_next, precision=data_mode)
    return inside + jnp.sum(carried * before, axis=2)


def channel_group(group_items, block_len):
    (
        forward_narrow,
        backward_narrow,
        rate_rows,
        weights,
        gain_rows,
        enter_forward,
        enter_backward,
    ) = group_items
    forward_rows = forward_narrow.astype(jnp.float32)
    backward_rows = backward_narrow.astype(jnp.float32)
    tables = make_tables(rate_rows, block_len)
    carried, before = modal_pass(forward_rows, rate_rows, weights, enter_forward, tables)
    returned, _ = modal_pass(jnp.flip(backward_rows, 1), rate_rows, weights, enter_backward, tables)
    signal = (carried + gain_rows[:, None] * forward_rows).astype(jnp.bfloat16)
    back_signal = (jnp.flip(returned, 1) + gain_rows[:, None] * backward_rows).astype(jnp.bfloat16)
    mode_raw = mode_products(forward_rows, backward_rows, before, tables)
    skip_raw = jnp.sum(backward_rows * forward_rows, axis=1)
    return (signal, back_signal, mode_raw, skip_raw)


def split_pair(values):
    high = values.astype(jnp.bfloat16)
    low = (values - high.astype(jnp.float32)).astype(jnp.bfloat16)
    return high, low


def mat_nn(a, b):
    return jnp.dot(a, b, preferred_element_type=jnp.float32)


def mat_nt(a, b):
    return lax.dot_general(a, b, (((1,), (1,)), ((), ())), preferred_element_type=jnp.float32)


def mat_tn(a, b):
    return lax.dot_general(a, b, (((0,), (0,)), ((), ())), preferred_element_type=jnp.float32)


def wide_nn(a, b_pair):
    a_high, a_low = split_pair(a)
    return mat_nn(a_high, b_pair[0]) + mat_nn(a_high, b_pair[1]) + mat_nn(a_low, b_pair[0])


def shifted(values, by, lanes_rows):
    rows = values.shape[0]
    rolled = pltpu.roll(values, by % rows, 0)
    index = lax.broadcasted_iota(jnp.int32, values.shape, 0)
    keep = (index >= by) if by > 0 else (index < rows + by)
    return jnp.where(keep, rolled, 0.0)


def long_conv_kernel(u_ref, dz_ref, tab_ref, row_ref, z_ref, du_ref, mode_ref, skip_ref):
    chans, blocks, width = u_ref.shape
    modes = tab_ref.shape[2]

    def one_channel(c, carry):
        u_narrow = u_ref[c]
        dz_narrow = dz_ref[c]
        tabs = tab_ref[c]
        rows = row_ref[c]
        fall_end = (tabs[0], tabs[1])
        fall_start = (tabs[2], tabs[3])
        gain_fwd = (tabs[4], tabs[5])
        gain_bwd = (tabs[6], tabs[7])
        gain_lag = (tabs[8], tabs[9])
        rate_row = rows[6:7, :]
        step_row = rows[5:6, :]
        gain = rows[7:8, 0:1]
        lag_ids = lax.broadcasted_iota(jnp.int32, (width, modes), 0).astype(jnp.float32)
        rise = jnp.exp(lag_ids * rate_row)
        toeplitz = wide_nn(rise, gain_lag)
        col = lax.broadcasted_iota(jnp.int32, (width, width), 1)
        row = lax.broadcasted_iota(jnp.int32, (width, width), 0)
        upper = col >= row
        toeplitz = jnp.where(upper, toeplitz, 0.0)
        t_high, t_low = split_pair(toeplitz)
        z_in = mat_nn(u_narrow, t_high) + mat_nn(u_narrow, t_low)
        du_in = mat_nt(dz_narrow, t_high) + mat_nt(dz_narrow, t_low)
        ends = mat_nt(u_narrow, fall_end[0]) + mat_nt(u_narrow, fall_end[1])
        starts = mat_nt(dz_narrow, fall_start[0]) + mat_nt(dz_narrow, fall_start[1])
        fwd_state = ends
        bwd_state = starts
        level = 0
        span = 1
        while span < blocks:
            decay = rows[level : level + 1, :]
            fwd_state = fwd_state + decay * shifted(fwd_state, span, blocks)
            bwd_state = bwd_state + decay * shifted(bwd_state, -span, blocks)
            level += 1
            span *= 2
        state_before = shifted(fwd_state, 1, blocks)
        state_after = shifted(bwd_state, -1, blocks)
        z_carry = wide_nn(state_before, gain_fwd)
        du_carry = wide_nn(state_after, gain_bwd)
        u_wide = u_narrow.astype(jnp.float32)
        dz_wide = dz_narrow.astype(jnp.float32)
        z_ref[c] = (z_in + z_carry + gain * u_wide).astype(z_ref.dtype)
        du_ref[c] = (du_in + du_carry + gain * dz_wide).astype(du_ref.dtype)
        crossed = mat_tn(u_narrow, dz_narrow)
        crossed = jnp.where(upper, crossed, 0.0)
        c_high, c_low = split_pair(crossed)
        weighted = (
            mat_nt(c_high, fall_start[0]) + mat_nt(c_high, fall_start[1]) + mat_nt(c_low, fall_start[0])
        )
        mode_in = jnp.sum(weighted * rise, axis=0, keepdims=True)
        mode_carry = jnp.sum(state_before * starts, axis=0, keepdims=True) * step_row
        mode_ref[c] = mode_in + mode_carry
        skip_ref[c] = jnp.broadcast_to(jnp.sum(u_wide * dz_wide), skip_ref.shape[1:])
        return carry

    lax.fori_loop(0, chans, one_channel, 0)


def long_conv_tables(rate_rows, weight_rows, gain_rows, width, blocks):
    offsets = jnp.arange(width, dtype=jnp.float32)
    rate = rate_rows[:, :, None]
    weight = weight_rows[:, :, None]
    fall_end = jnp.exp(-rate * (width - 1.0 - offsets))
    fall_start = jnp.exp(-rate * offsets)
    gain_fwd = weight * jnp.exp(-rate * (offsets + 1.0))
    gain_bwd = weight * jnp.exp(-rate * (width - offsets))
    gain_lag = weight * jnp.exp(-rate * offsets)
    pairs = []
    for table in (fall_end, fall_start, gain_fwd, gain_bwd, gain_lag):
        high = lax.reduce_precision(table, exponent_bits=8, mantissa_bits=7)
        pairs.extend((high.astype(jnp.bfloat16), (table - high).astype(jnp.bfloat16)))
    tabs = jnp.stack(pairs, axis=1)
    levels = []
    span = 1
    while span < blocks:
        levels.append(jnp.exp(-rate_rows * (width * span)))
        span *= 2
    chan_count, modes = rate_rows.shape
    while len(levels) < 5:
        levels.append(jnp.zeros_like(rate_rows))
    levels.append(jnp.exp(-rate_rows))
    levels.append(rate_rows)
    levels.append(jnp.broadcast_to(gain_rows[:, None], (chan_count, modes)))
    return tabs, jnp.stack(levels, axis=1)


def long_conv(u_blocks, dz_blocks, rate_rows, weight_rows, gain_rows, chans_per_step=8):
    chan_count, blocks, width = u_blocks.shape
    modes = rate_rows.shape[1]
    tabs, rows = long_conv_tables(rate_rows, weight_rows, gain_rows, width, blocks)
    step = min(chans_per_step, chan_count)
    data_spec = pl.BlockSpec((step, blocks, width), lambda i: (i, 0, 0))
    return pl.pallas_call(
        long_conv_kernel,
        grid=(chan_count // step,),
        in_specs=[
            data_spec,
            data_spec,
            pl.BlockSpec((step,) + tabs.shape[1:], lambda i: (i, 0, 0, 0)),
            pl.BlockSpec((step,) + rows.shape[1:], lambda i: (i, 0, 0)),
        ],
        out_specs=[
            data_spec,
            data_spec,
            pl.BlockSpec((step, 1, modes), lambda i: (i, 0, 0)),
            pl.BlockSpec((step, 1, 128), lambda i: (i, 0, 0)),
        ],
        out_shape=[
            jax.ShapeDtypeStruct(u_blocks.shape, jnp.bfloat16),
            jax.ShapeDtypeStruct(u_blocks.shape, jnp.bfloat16),
            jax.ShapeDtypeStruct((chan_count, 1, modes), jnp.float32),
            jax.ShapeDtypeStruct((chan_count, 1, 128), jnp.float32),
        ],
        cost_estimate=pl.CostEstimate(
            flops=chan_count * 34 * width * width * blocks, transcendentals=chan_count * width * modes,
            bytes_accessed=chan_count * blocks * width * 8 + tabs.size * 2,
        ),
    )(u_blocks, dz_blocks, tabs, rows)


def grouped(function, arrays, group_size):
    stacked = tuple(
        (
            item.reshape((item.shape[0] // group_size, group_size) + item.shape[1:])
            for item in arrays
        )
    )
    results = lax.map(function, stacked)
    return tuple(
        (item.reshape((item.shape[0] * item.shape[1],) + item.shape[2:]) for item in results)
    )


def on_device(projected, cotangent, short_filter, residues, decay_rate, skip_gain):
    proj_rows = projected[0]
    token_count = proj_rows.shape[2]
    chans_tp = proj_rows.shape[1]
    rim_width = short_filter.shape[1] - 1
    grad_out = lax.all_to_all(cotangent[0], "tp", split_axis=0, concat_axis=1, tiled=True).astype(
        jnp.float32
    )
    prev_rim = from_behind(proj_rows[:, :, token_count - rim_width :], "ctx", 1)
    featured = lax.optimization_barrier(
        causal_short(proj_rows, prev_rim, short_filter).astype(jnp.bfloat16)
    )
    query_feat = featured[0].astype(jnp.float32)
    key_feat = featured[1].astype(jnp.float32)
    value_feat = featured[2].astype(jnp.float32)
    product = (key_feat * value_feat).astype(jnp.bfloat16)
    adjoint = (grad_out * query_feat).astype(jnp.bfloat16)
    ctx_count = lax.axis_size("ctx")
    token_total = token_count * ctx_count * lax.axis_size("dp")
    weight_all = residues * jnp.sqrt(2.0 * decay_rate)
    product_all, adjoint_all = (
        lax.all_to_all(product, "ctx", split_axis=0, concat_axis=1, tiled=True),
        lax.all_to_all(adjoint, "ctx", split_axis=0, concat_axis=1, tiled=True),
    )
    chan_count = chans_tp // ctx_count
    chan_start = lax.axis_index("ctx") * chan_count
    rate_rows = lax.dynamic_slice_in_dim(decay_rate, chan_start, chan_count, 0)
    weight_rows = lax.dynamic_slice_in_dim(weight_all, chan_start, chan_count, 0)
    gain_rows = lax.dynamic_slice_in_dim(skip_gain, chan_start, chan_count, 0)
    length = product_all.shape[1]
    block_len = math.gcd(256, length)
    block_count = length // block_len
    conv_blocks, back_blocks, mode_part, skip_part = long_conv(
        product_all.reshape(chan_count, block_count, block_len),
        adjoint_all.reshape(chan_count, block_count, block_len),
        rate_rows,
        weight_rows,
        gain_rows,
    )
    conv_rows = conv_blocks.reshape(chan_count, length)
    back_rows = back_blocks.reshape(chan_count, length)
    mode_part = mode_part[:, 0, :]
    skip_part = skip_part[:, 0, 0]
    signal, back_signal = (
        lax.all_to_all(conv_rows, "ctx", split_axis=1, concat_axis=0, tiled=True),
        lax.all_to_all(back_rows, "ctx", split_axis=1, concat_axis=0, tiled=True),
    )
    grad_scale = 1.0 / math.sqrt(token_total)
    local_grads = jnp.concatenate(
        [mode_part * jnp.sqrt(2.0 * rate_rows) * grad_scale, skip_part[:, None] * grad_scale], axis=1
    )
    local_grads = lax.psum(local_grads, "dp")
    spread = jnp.broadcast_to(local_grads[None], (ctx_count,) + local_grads.shape)
    gathered = lax.all_to_all(spread, "ctx", split_axis=0, concat_axis=0, tiled=True)
    gathered = gathered.reshape(chans_tp, local_grads.shape[1])
    residue_grad = gathered[:, : mode_part.shape[1]]
    skip_grad = gathered[:, mode_part.shape[1]]
    conv_wide = signal.astype(jnp.float32)
    back_wide = back_signal.astype(jnp.float32)
    hyena_out = (query_feat * conv_wide).astype(jnp.bfloat16)
    feature_grad = jnp.stack(
        [grad_out * conv_wide, back_wide * value_feat, back_wide * key_feat]
    ).astype(jnp.bfloat16)
    next_rim = from_behind(feature_grad[:, :, :rim_width], "ctx", -1)
    input_grad = anticausal_short(feature_grad, next_rim, short_filter).astype(jnp.bfloat16)
    return (hyena_out[None], input_grad[None], residue_grad, skip_grad)


def solution(mesh):
    placed = (
        P("dp", None, "tp", "ctx"),
        P("dp", None, ("ctx", "tp")),
        P(None, None, "tp"),
        P("tp", None),
        P("tp", None),
        P("tp"),
    )
    return jax.shard_map(
        on_device,
        mesh=mesh,
        in_specs=placed,
        out_specs=(P("dp", "tp", "ctx"), P("dp", None, "tp", "ctx"), P("tp", None), P("tp")),
        check_vma=False,
    )
```

```python
from functools import partial
import math

import jax
import jax.numpy as jnp
from jax import lax
from jax.sharding import PartitionSpec as P
from jax.experimental import pallas as pl
from jax.experimental.pallas import tpu as pltpu

exact_mode = lax.Precision.HIGHEST
data_mode = lax.Precision.HIGH


def from_behind(shard, axis, by):
    count = lax.axis_size(axis)
    pairs = [(i, i + by) for i in range(count) if 0 <= i + by < count]
    return lax.ppermute(shard, axis, pairs)


def causal_short(proj_rows, prev_rim, tap_weights):
    rim_width = prev_rim.shape[2]
    token_count = proj_rows.shape[2]
    extended = jnp.concatenate([prev_rim, proj_rows], axis=2).astype(jnp.float32)
    result = tap_weights[:, 0, :, None] * extended[:, :, rim_width : rim_width + token_count]
    for lag_index in range(1, rim_width + 1):
        start_at = rim_width - lag_index
        result = (
            result
            + tap_weights[:, lag_index, :, None] * extended[:, :, start_at : start_at + token_count]
        )
    return result


def anticausal_short(grad_rows, next_rim, tap_weights):
    rim_width = next_rim.shape[2]
    token_count = grad_rows.shape[2]
    extended = jnp.concatenate([grad_rows, next_rim], axis=2).astype(jnp.float32)
    result = tap_weights[:, 0, :, None] * extended[:, :, :token_count]
    for lag_index in range(1, rim_width + 1):
        result = (
            result
            + tap_weights[:, lag_index, :, None]
            * extended[:, :, lag_index : lag_index + token_count]
        )
    return result


def make_tables(rate_rows, block_len):
    offsets = jnp.arange(block_len, dtype=jnp.float32)
    fall_now = jnp.exp(-rate_rows[:, :, None] * offsets)
    rise_now = jnp.exp(rate_rows[:, :, None] * offsets)
    fall_next = jnp.exp(-rate_rows[:, :, None] * (offsets + 1.0))
    fall_tail = jnp.exp(-rate_rows[:, :, None] * (block_len - 1.0 - offsets))
    lower_mask = offsets[:, None] >= offsets[None, :]
    return (fall_now, rise_now, fall_next, fall_tail, lower_mask)


def chain_link(earlier, later):
    return (earlier[0] * later[0], later[0] * earlier[1] + later[1])


def modal_pass(signal, rate_rows, weights, incoming, tables):
    fall_now, rise_now, fall_next, fall_tail, lower_mask = tables
    block_len = fall_now.shape[2]
    chan_count, length = signal.shape
    block_count = length // block_len
    pieces = signal.reshape(chan_count, block_count, block_len)
    kernel = jnp.einsum(
        "cnt,cns->cts", weights[:, :, None] * fall_now, rise_now, precision=exact_mode
    )
    kernel = jnp.where(lower_mask[None], kernel, 0.0)
    inside = jnp.einsum("cts,cbs->cbt", kernel, pieces, precision=data_mode)
    block_ends = jnp.einsum("cns,cbs->cnb", fall_tail, pieces, precision=data_mode)
    span_decay = jnp.exp(-rate_rows * block_len)
    block_mults = jnp.broadcast_to(span_decay[:, :, None], block_ends.shape)
    _, running = lax.associative_scan(chain_link, (block_mults, block_ends), axis=2)
    block_steps = jnp.arange(block_count, dtype=jnp.float32)
    before = jnp.concatenate([jnp.zeros_like(running[:, :, :1]), running[:, :, :-1]], axis=2)
    before = (
        before + jnp.exp(-rate_rows[:, :, None] * block_len * block_steps) * incoming[:, :, None]
    )
    carry_in = jnp.einsum(
        "cnt,cnb->cbt", weights[:, :, None] * fall_next, before, precision=exact_mode
    )
    return ((inside + carry_in).reshape(chan_count, length), before)


def mode_products(signal, adjoint, before, tables):
    fall_now, rise_now, fall_next, fall_tail, lower_mask = tables
    block_len = fall_now.shape[2]
    chan_count, length = signal.shape
    block_count = length // block_len
    pieces = signal.reshape(chan_count, block_count, block_len)
    dual_pieces = adjoint.reshape(chan_count, block_count, block_len)
    crossed = jnp.einsum("cbt,cbs->cts", dual_pieces, pieces, precision=data_mode)
    crossed = jnp.where(lower_mask[None], crossed, 0.0)
    weighted = jnp.einsum("cts,cnt->cns", crossed, fall_now, precision=exact_mode)
    inside = jnp.sum(weighted * rise_now, axis=2)
    carried = jnp.einsum("cbt,cnt->cnb", dual_pieces, fall_next, precision=data_mode)
    return inside + jnp.sum(carried * before, axis=2)


def channel_group(group_items, block_len):
    (
        forward_narrow,
        backward_narrow,
        rate_rows,
        weights,
        gain_rows,
        enter_forward,
        enter_backward,
    ) = group_items
    forward_rows = forward_narrow.astype(jnp.float32)
    backward_rows = backward_narrow.astype(jnp.float32)
    tables = make_tables(rate_rows, block_len)
    carried, before = modal_pass(forward_rows, rate_rows, weights, enter_forward, tables)
    returned, _ = modal_pass(jnp.flip(backward_rows, 1), rate_rows, weights, enter_backward, tables)
    signal = (carried + gain_rows[:, None] * forward_rows).astype(jnp.bfloat16)
    back_signal = (jnp.flip(returned, 1) + gain_rows[:, None] * backward_rows).astype(jnp.bfloat16)
    mode_raw = mode_products(forward_rows, backward_rows, before, tables)
    skip_raw = jnp.sum(backward_rows * forward_rows, axis=1)
    return (signal, back_signal, mode_raw, skip_raw)


def split_pair(values):
    high = values.astype(jnp.bfloat16)
    low = (values - high.astype(jnp.float32)).astype(jnp.bfloat16)
    return high, low


def mat_nn(a, b):
    return jnp.dot(a, b, preferred_element_type=jnp.float32)


def mat_nt(a, b):
    return lax.dot_general(a, b, (((1,), (1,)), ((), ())), preferred_element_type=jnp.float32)


def mat_tn(a, b):
    return lax.dot_general(a, b, (((0,), (0,)), ((), ())), preferred_element_type=jnp.float32)


def wide_nn(a, b_pair):
    a_high, a_low = split_pair(a)
    return mat_nn(a_high, b_pair[0]) + mat_nn(a_high, b_pair[1]) + mat_nn(a_low, b_pair[0])


def shifted(values, by, lanes_rows):
    rows = values.shape[0]
    rolled = pltpu.roll(values, by % rows, 0)
    index = lax.broadcasted_iota(jnp.int32, values.shape, 0)
    keep = (index >= by) if by > 0 else (index < rows + by)
    return jnp.where(keep, rolled, 0.0)


def long_conv_kernel(u_ref, dz_ref, tab_ref, row_ref, z_ref, du_ref, mode_ref, skip_ref):
    chans, blocks, width = u_ref.shape
    modes = tab_ref.shape[2]

    def one_channel(c, carry):
        u_narrow = u_ref[c]
        dz_narrow = dz_ref[c]
        tabs = tab_ref[c]
        rows = row_ref[c]
        fall_end = (tabs[0], tabs[1])
        fall_start = (tabs[2], tabs[3])
        gain_fwd = (tabs[4], tabs[5])
        gain_bwd = (tabs[6], tabs[7])
        gain_lag = (tabs[8], tabs[9])
        rate_row = rows[6:7, :]
        step_row = rows[5:6, :]
        gain = rows[7:8, 0:1]
        lag_ids = lax.broadcasted_iota(jnp.int32, (width, modes), 0).astype(jnp.float32)
        rise = jnp.exp(lag_ids * rate_row)
        toeplitz = wide_nn(rise, gain_lag)
        col = lax.broadcasted_iota(jnp.int32, (width, width), 1)
        row = lax.broadcasted_iota(jnp.int32, (width, width), 0)
        upper = col >= row
        toeplitz = jnp.where(upper, toeplitz, 0.0)
        t_high, t_low = split_pair(toeplitz)
        z_in = mat_nn(u_narrow, t_high) + mat_nn(u_narrow, t_low)
        du_in = mat_nt(dz_narrow, t_high) + mat_nt(dz_narrow, t_low)
        ends = mat_nt(u_narrow, fall_end[0]) + mat_nt(u_narrow, fall_end[1])
        starts = mat_nt(dz_narrow, fall_start[0]) + mat_nt(dz_narrow, fall_start[1])
        fwd_state = ends
        bwd_state = starts
        level = 0
        span = 1
        while span < blocks:
            decay = rows[level : level + 1, :]
            fwd_state = fwd_state + decay * shifted(fwd_state, span, blocks)
            bwd_state = bwd_state + decay * shifted(bwd_state, -span, blocks)
            level += 1
            span *= 2
        state_before = shifted(fwd_state, 1, blocks)
        state_after = shifted(bwd_state, -1, blocks)
        z_carry = wide_nn(state_before, gain_fwd)
        du_carry = wide_nn(state_after, gain_bwd)
        u_wide = u_narrow.astype(jnp.float32)
        dz_wide = dz_narrow.astype(jnp.float32)
        z_ref[c] = (z_in + z_carry + gain * u_wide).astype(z_ref.dtype)
        du_ref[c] = (du_in + du_carry + gain * dz_wide).astype(du_ref.dtype)
        crossed = mat_tn(u_narrow, dz_narrow)
        crossed = jnp.where(upper, crossed, 0.0)
        c_high, c_low = split_pair(crossed)
        weighted = (
            mat_nt(c_high, fall_start[0]) + mat_nt(c_high, fall_start[1]) + mat_nt(c_low, fall_start[0])
        )
        mode_in = jnp.sum(weighted * rise, axis=0, keepdims=True)
        mode_carry = jnp.sum(state_before * starts, axis=0, keepdims=True) * step_row
        mode_ref[c] = mode_in + mode_carry
        skip_ref[c] = jnp.broadcast_to(jnp.sum(u_wide * dz_wide), skip_ref.shape[1:])
        return carry

    lax.fori_loop(0, chans, one_channel, 0)


def long_conv_tables(rate_rows, weight_rows, gain_rows, width, blocks):
    offsets = jnp.arange(width, dtype=jnp.float32)
    rate = rate_rows[:, :, None]
    weight = weight_rows[:, :, None]
    fall_end = jnp.exp(-rate * (width - 1.0 - offsets))
    fall_start = jnp.exp(-rate * offsets)
    gain_fwd = weight * jnp.exp(-rate * (offsets + 1.0))
    gain_bwd = weight * jnp.exp(-rate * (width - offsets))
    gain_lag = weight * jnp.exp(-rate * offsets)
    pairs = []
    for table in (fall_end, fall_start, gain_fwd, gain_bwd, gain_lag):
        high = lax.reduce_precision(table, exponent_bits=8, mantissa_bits=7)
        pairs.extend((high.astype(jnp.bfloat16), (table - high).astype(jnp.bfloat16)))
    tabs = jnp.stack(pairs, axis=1)
    levels = []
    span = 1
    while span < blocks:
        levels.append(jnp.exp(-rate_rows * (width * span)))
        span *= 2
    chan_count, modes = rate_rows.shape
    while len(levels) < 5:
        levels.append(jnp.zeros_like(rate_rows))
    levels.append(jnp.exp(-rate_rows))
    levels.append(rate_rows)
    levels.append(jnp.broadcast_to(gain_rows[:, None], (chan_count, modes)))
    return tabs, jnp.stack(levels, axis=1)


def long_conv(u_blocks, dz_blocks, rate_rows, weight_rows, gain_rows, chans_per_step=8):
    chan_count, blocks, width = u_blocks.shape
    modes = rate_rows.shape[1]
    tabs, rows = long_conv_tables(rate_rows, weight_rows, gain_rows, width, blocks)
    step = min(chans_per_step, chan_count)
    data_spec = pl.BlockSpec((step, blocks, width), lambda i: (i, 0, 0))
    return pl.pallas_call(
        long_conv_kernel,
        grid=(chan_count // step,),
        in_specs=[
            data_spec,
            data_spec,
            pl.BlockSpec((step,) + tabs.shape[1:], lambda i: (i, 0, 0, 0)),
            pl.BlockSpec((step,) + rows.shape[1:], lambda i: (i, 0, 0)),
        ],
        out_specs=[
            data_spec,
            data_spec,
            pl.BlockSpec((step, 1, modes), lambda i: (i, 0, 0)),
            pl.BlockSpec((step, 1, 128), lambda i: (i, 0, 0)),
        ],
        out_shape=[
            jax.ShapeDtypeStruct(u_blocks.shape, jnp.bfloat16),
            jax.ShapeDtypeStruct(u_blocks.shape, jnp.bfloat16),
            jax.ShapeDtypeStruct((chan_count, 1, modes), jnp.float32),
            jax.ShapeDtypeStruct((chan_count, 1, 128), jnp.float32),
        ],
        cost_estimate=pl.CostEstimate(
            flops=chan_count * 34 * width * width * blocks, transcendentals=chan_count * width * modes,
            bytes_accessed=chan_count * blocks * width * 8 + tabs.size * 2,
        ),
    )(u_blocks, dz_blocks, tabs, rows)


def grouped(function, arrays, group_size):
    stacked = tuple(
        (
            item.reshape((item.shape[0] // group_size, group_size) + item.shape[1:])
            for item in arrays
        )
    )
    results = lax.map(function, stacked)
    return tuple(
        (item.reshape((item.shape[0] * item.shape[1],) + item.shape[2:]) for item in results)
    )


def on_device(projected, cotangent, short_filter, residues, decay_rate, skip_gain):
    proj_rows = projected[0]
    token_count = proj_rows.shape[2]
    chans_tp = proj_rows.shape[1]
    rim_width = short_filter.shape[1] - 1
    grad_out = lax.all_to_all(cotangent[0], "tp", split_axis=0, concat_axis=1, tiled=True).astype(
        jnp.float32
    )
    prev_rim = from_behind(proj_rows[:, :, token_count - rim_width :], "ctx", 1)
    featured = lax.optimization_barrier(
        causal_short(proj_rows, prev_rim, short_filter).astype(jnp.bfloat16)
    )
    query_feat = featured[0].astype(jnp.float32)
    key_feat = featured[1].astype(jnp.float32)
    value_feat = featured[2].astype(jnp.float32)
    product = (key_feat * value_feat).astype(jnp.bfloat16)
    adjoint = (grad_out * query_feat).astype(jnp.bfloat16)
    ctx_count = lax.axis_size("ctx")
    token_total = token_count * ctx_count * lax.axis_size("dp")
    weight_all = residues * jnp.sqrt(2.0 * decay_rate)
    both_all = lax.all_to_all(
        jnp.stack([product, adjoint]), "ctx", split_axis=1, concat_axis=2, tiled=True
    )
    product_all, adjoint_all = both_all[0], both_all[1]
    chan_count = chans_tp // ctx_count
    chan_start = lax.axis_index("ctx") * chan_count
    rate_rows = lax.dynamic_slice_in_dim(decay_rate, chan_start, chan_count, 0)
    weight_rows = lax.dynamic_slice_in_dim(weight_all, chan_start, chan_count, 0)
    gain_rows = lax.dynamic_slice_in_dim(skip_gain, chan_start, chan_count, 0)
    length = product_all.shape[1]
    block_len = math.gcd(256, length)
    block_count = length // block_len
    conv_blocks, back_blocks, mode_part, skip_part = long_conv(
        product_all.reshape(chan_count, block_count, block_len),
        adjoint_all.reshape(chan_count, block_count, block_len),
        rate_rows,
        weight_rows,
        gain_rows,
    )
    conv_rows = conv_blocks.reshape(chan_count, length)
    back_rows = back_blocks.reshape(chan_count, length)
    mode_part = mode_part[:, 0, :]
    skip_part = skip_part[:, 0, 0]
    both_back = lax.all_to_all(
        jnp.stack([conv_rows, back_rows]), "ctx", split_axis=2, concat_axis=1, tiled=True
    )
    signal, back_signal = both_back[0], both_back[1]
    grad_scale = 1.0 / math.sqrt(token_total)
    local_grads = jnp.concatenate(
        [mode_part * jnp.sqrt(2.0 * rate_rows) * grad_scale, skip_part[:, None] * grad_scale], axis=1
    )
    dp_count = lax.axis_size("dp")
    grad_cols = local_grads.shape[1]
    pieces = local_grads.reshape(dp_count, chan_count // dp_count, grad_cols)
    pieces = lax.all_to_all(pieces, "dp", split_axis=0, concat_axis=0, tiled=True)
    summed = jnp.sum(pieces, axis=0)
    spread = jnp.broadcast_to(summed[None], (ctx_count,) + summed.shape)
    gathered = lax.all_to_all(spread, "ctx", split_axis=0, concat_axis=0, tiled=True)
    spread = jnp.broadcast_to(gathered[None], (dp_count,) + gathered.shape)
    gathered = lax.all_to_all(spread, "dp", split_axis=0, concat_axis=0, tiled=True)
    gathered = gathered.reshape(dp_count, ctx_count, chan_count // dp_count, grad_cols)
    gathered = jnp.swapaxes(gathered, 0, 1).reshape(chans_tp, grad_cols)
    residue_grad = gathered[:, : mode_part.shape[1]]
    skip_grad = gathered[:, mode_part.shape[1]]
    conv_wide = signal.astype(jnp.float32)
    back_wide = back_signal.astype(jnp.float32)
    hyena_out = (query_feat * conv_wide).astype(jnp.bfloat16)
    feature_grad = jnp.stack(
        [grad_out * conv_wide, back_wide * value_feat, back_wide * key_feat]
    ).astype(jnp.bfloat16)
    next_rim = from_behind(feature_grad[:, :, :rim_width], "ctx", -1)
    input_grad = anticausal_short(feature_grad, next_rim, short_filter).astype(jnp.bfloat16)
    return (hyena_out[None], input_grad[None], residue_grad, skip_grad)


def solution(mesh):
    placed = (
        P("dp", None, "tp", "ctx"),
        P("dp", None, ("ctx", "tp")),
        P(None, None, "tp"),
        P("tp", None),
        P("tp", None),
        P("tp"),
    )
    return jax.shard_map(
        on_device,
        mesh=mesh,
        in_specs=placed,
        out_specs=(P("dp", "tp", "ctx"), P("dp", None, "tp", "ctx"), P("tp", None), P("tp")),
        check_vma=False,
    )
```

```python
from functools import partial
import math

import jax
import jax.numpy as jnp
from jax import lax
from jax.sharding import PartitionSpec as P
from jax.experimental import pallas as pl
from jax.experimental.pallas import tpu as pltpu

exact_mode = lax.Precision.HIGHEST
data_mode = lax.Precision.HIGH


def from_behind(shard, axis, by):
    count = lax.axis_size(axis)
    pairs = [(i, i + by) for i in range(count) if 0 <= i + by < count]
    return lax.ppermute(shard, axis, pairs)


def causal_short(proj_rows, prev_rim, tap_weights):
    rim_width = prev_rim.shape[2]
    token_count = proj_rows.shape[2]
    extended = jnp.concatenate([prev_rim, proj_rows], axis=2).astype(jnp.float32)
    result = tap_weights[:, 0, :, None] * extended[:, :, rim_width : rim_width + token_count]
    for lag_index in range(1, rim_width + 1):
        start_at = rim_width - lag_index
        result = (
            result
            + tap_weights[:, lag_index, :, None] * extended[:, :, start_at : start_at + token_count]
        )
    return result


def anticausal_short(grad_rows, next_rim, tap_weights):
    rim_width = next_rim.shape[2]
    token_count = grad_rows.shape[2]
    extended = jnp.concatenate([grad_rows, next_rim], axis=2).astype(jnp.float32)
    result = tap_weights[:, 0, :, None] * extended[:, :, :token_count]
    for lag_index in range(1, rim_width + 1):
        result = (
            result
            + tap_weights[:, lag_index, :, None]
            * extended[:, :, lag_index : lag_index + token_count]
        )
    return result


def make_tables(rate_rows, block_len):
    offsets = jnp.arange(block_len, dtype=jnp.float32)
    fall_now = jnp.exp(-rate_rows[:, :, None] * offsets)
    rise_now = jnp.exp(rate_rows[:, :, None] * offsets)
    fall_next = jnp.exp(-rate_rows[:, :, None] * (offsets + 1.0))
    fall_tail = jnp.exp(-rate_rows[:, :, None] * (block_len - 1.0 - offsets))
    lower_mask = offsets[:, None] >= offsets[None, :]
    return (fall_now, rise_now, fall_next, fall_tail, lower_mask)


def chain_link(earlier, later):
    return (earlier[0] * later[0], later[0] * earlier[1] + later[1])


def modal_pass(signal, rate_rows, weights, incoming, tables):
    fall_now, rise_now, fall_next, fall_tail, lower_mask = tables
    block_len = fall_now.shape[2]
    chan_count, length = signal.shape
    block_count = length // block_len
    pieces = signal.reshape(chan_count, block_count, block_len)
    kernel = jnp.einsum(
        "cnt,cns->cts", weights[:, :, None] * fall_now, rise_now, precision=exact_mode
    )
    kernel = jnp.where(lower_mask[None], kernel, 0.0)
    inside = jnp.einsum("cts,cbs->cbt", kernel, pieces, precision=data_mode)
    block_ends = jnp.einsum("cns,cbs->cnb", fall_tail, pieces, precision=data_mode)
    span_decay = jnp.exp(-rate_rows * block_len)
    block_mults = jnp.broadcast_to(span_decay[:, :, None], block_ends.shape)
    _, running = lax.associative_scan(chain_link, (block_mults, block_ends), axis=2)
    block_steps = jnp.arange(block_count, dtype=jnp.float32)
    before = jnp.concatenate([jnp.zeros_like(running[:, :, :1]), running[:, :, :-1]], axis=2)
    before = (
        before + jnp.exp(-rate_rows[:, :, None] * block_len * block_steps) * incoming[:, :, None]
    )
    carry_in = jnp.einsum(
        "cnt,cnb->cbt", weights[:, :, None] * fall_next, before, precision=exact_mode
    )
    return ((inside + carry_in).reshape(chan_count, length), before)


def mode_products(signal, adjoint, before, tables):
    fall_now, rise_now, fall_next, fall_tail, lower_mask = tables
    block_len = fall_now.shape[2]
    chan_count, length = signal.shape
    block_count = length // block_len
    pieces = signal.reshape(chan_count, block_count, block_len)
    dual_pieces = adjoint.reshape(chan_count, block_count, block_len)
    crossed = jnp.einsum("cbt,cbs->cts", dual_pieces, pieces, precision=data_mode)
    crossed = jnp.where(lower_mask[None], crossed, 0.0)
    weighted = jnp.einsum("cts,cnt->cns", crossed, fall_now, precision=exact_mode)
    inside = jnp.sum(weighted * rise_now, axis=2)
    carried = jnp.einsum("cbt,cnt->cnb", dual_pieces, fall_next, precision=data_mode)
    return inside + jnp.sum(carried * before, axis=2)


def channel_group(group_items, block_len):
    (
        forward_narrow,
        backward_narrow,
        rate_rows,
        weights,
        gain_rows,
        enter_forward,
        enter_backward,
    ) = group_items
    forward_rows = forward_narrow.astype(jnp.float32)
    backward_rows = backward_narrow.astype(jnp.float32)
    tables = make_tables(rate_rows, block_len)
    carried, before = modal_pass(forward_rows, rate_rows, weights, enter_forward, tables)
    returned, _ = modal_pass(jnp.flip(backward_rows, 1), rate_rows, weights, enter_backward, tables)
    signal = (carried + gain_rows[:, None] * forward_rows).astype(jnp.bfloat16)
    back_signal = (jnp.flip(returned, 1) + gain_rows[:, None] * backward_rows).astype(jnp.bfloat16)
    mode_raw = mode_products(forward_rows, backward_rows, before, tables)
    skip_raw = jnp.sum(backward_rows * forward_rows, axis=1)
    return (signal, back_signal, mode_raw, skip_raw)


def split_pair(values):
    high = values.astype(jnp.bfloat16)
    low = (values - high.astype(jnp.float32)).astype(jnp.bfloat16)
    return high, low


def mat_nn(a, b):
    return jnp.dot(a, b, preferred_element_type=jnp.float32)


def mat_nt(a, b):
    return lax.dot_general(a, b, (((1,), (1,)), ((), ())), preferred_element_type=jnp.float32)


def mat_tn(a, b):
    return lax.dot_general(a, b, (((0,), (0,)), ((), ())), preferred_element_type=jnp.float32)


def wide_nn(a, b_pair):
    a_high, a_low = split_pair(a)
    return mat_nn(a_high, b_pair[0]) + mat_nn(a_high, b_pair[1]) + mat_nn(a_low, b_pair[0])


def shifted(values, by, lanes_rows):
    rows = values.shape[0]
    rolled = pltpu.roll(values, by % rows, 0)
    index = lax.broadcasted_iota(jnp.int32, values.shape, 0)
    keep = (index >= by) if by > 0 else (index < rows + by)
    return jnp.where(keep, rolled, 0.0)


def long_conv_kernel(u_ref, dz_ref, krow_ref, tab_ref, row_ref, z_ref, du_ref, mode_ref, skip_ref):
    chans, blocks, width = u_ref.shape
    modes = tab_ref.shape[2]
    col = lax.broadcasted_iota(jnp.int32, (width, width), 1)
    row = lax.broadcasted_iota(jnp.int32, (width, width), 0)
    upper = col >= row
    lower = col <= row
    lag_ids = lax.broadcasted_iota(jnp.int32, (width, modes), 0).astype(jnp.float32)

    def one_channel(c, carry):
        u_narrow = u_ref[c]
        dz_narrow = dz_ref[c]
        tabs = tab_ref[c]
        rows = row_ref[c]
        krow = krow_ref[c]
        fall_end = (tabs[0], tabs[1])
        fall_start = (tabs[2], tabs[3])
        gain_fwd = (tabs[4], tabs[5])
        gain_bwd = (tabs[6], tabs[7])
        rate_row = rows[6:7, :]
        step_row = rows[5:6, :]
        gain = rows[7:8, 0:1]
        ahead = pltpu.roll(jnp.broadcast_to(krow[0:1, :], (width, width)), 0, 1, stride=1, stride_axis=0)
        ahead = jnp.where(upper, ahead, 0.0)
        behind = pltpu.roll(jnp.broadcast_to(krow[1:2, :], (width, width)), 1, 1, stride=1, stride_axis=0)
        behind = jnp.where(lower, behind, 0.0)
        a_high, a_low = split_pair(ahead)
        b_high, b_low = split_pair(behind)
        z_in = mat_nn(
            jnp.concatenate([u_narrow, u_narrow], axis=1), jnp.concatenate([a_high, a_low], axis=0)
        )
        du_in = mat_nn(
            jnp.concatenate([dz_narrow, dz_narrow], axis=1), jnp.concatenate([b_high, b_low], axis=0)
        )
        ends = mat_nt(u_narrow, fall_end[0]) + mat_nt(u_narrow, fall_end[1])
        starts = mat_nt(dz_narrow, fall_start[0]) + mat_nt(dz_narrow, fall_start[1])
        fwd_state = ends
        bwd_state = starts
        level = 0
        span = 1
        while span < blocks:
            decay = rows[level : level + 1, :]
            fwd_state = fwd_state + decay * shifted(fwd_state, span, blocks)
            bwd_state = bwd_state + decay * shifted(bwd_state, -span, blocks)
            level += 1
            span *= 2
        state_before = shifted(fwd_state, 1, blocks)
        state_after = shifted(bwd_state, -1, blocks)
        z_carry = wide_nn(state_before, gain_fwd)
        du_carry = wide_nn(state_after, gain_bwd)
        u_wide = u_narrow.astype(jnp.float32)
        dz_wide = dz_narrow.astype(jnp.float32)
        z_ref[c] = (z_in + z_carry + gain * u_wide).astype(z_ref.dtype)
        du_ref[c] = (du_in + du_carry + gain * dz_wide).astype(du_ref.dtype)
        rise = jnp.exp(lag_ids * rate_row)
        crossed = mat_tn(u_narrow, dz_narrow)
        crossed = jnp.where(upper, crossed, 0.0)
        c_high, c_low = split_pair(crossed)
        weighted = (
            mat_nt(c_high, fall_start[0]) + mat_nt(c_high, fall_start[1]) + mat_nt(c_low, fall_start[0])
        )
        mode_in = jnp.sum(weighted * rise, axis=0, keepdims=True)
        mode_carry = jnp.sum(state_before * starts, axis=0, keepdims=True) * step_row
        mode_ref[c] = mode_in + mode_carry
        skip_ref[c] = jnp.broadcast_to(jnp.sum(u_wide * dz_wide), skip_ref.shape[1:])
        return carry

    lax.fori_loop(0, chans, one_channel, 0, unroll=8)


def long_conv_tables(rate_rows, weight_rows, gain_rows, width, blocks):
    offsets = jnp.arange(width, dtype=jnp.float32)
    rate = rate_rows[:, :, None]
    weight = weight_rows[:, :, None]
    fall_end = jnp.exp(-rate * (width - 1.0 - offsets))
    fall_start = jnp.exp(-rate * offsets)
    gain_fwd = weight * jnp.exp(-rate * (offsets + 1.0))
    gain_bwd = weight * jnp.exp(-rate * (width - offsets))
    pairs = []
    for table in (fall_end, fall_start, gain_fwd, gain_bwd):
        high = lax.reduce_precision(table, exponent_bits=8, mantissa_bits=7)
        pairs.extend((high.astype(jnp.bfloat16), (table - high).astype(jnp.bfloat16)))
    tabs = jnp.stack(pairs, axis=1)
    levels = []
    span = 1
    while span < blocks:
        levels.append(jnp.exp(-rate_rows * (width * span)))
        span *= 2
    chan_count, modes = rate_rows.shape
    while len(levels) < 5:
        levels.append(jnp.zeros_like(rate_rows))
    levels.append(jnp.exp(-rate_rows))
    levels.append(rate_rows)
    levels.append(jnp.broadcast_to(gain_rows[:, None], (chan_count, modes)))
    lag_kernel = jnp.sum(weight * fall_start, axis=1)
    krow = jnp.stack([lag_kernel, jnp.flip(lag_kernel, axis=1)], axis=1)
    return tabs, jnp.stack(levels, axis=1), krow


def long_conv(u_blocks, dz_blocks, rate_rows, weight_rows, gain_rows, chans_per_step=8):
    chan_count, blocks, width = u_blocks.shape
    modes = rate_rows.shape[1]
    tabs, rows, krow = long_conv_tables(rate_rows, weight_rows, gain_rows, width, blocks)
    step = min(chans_per_step, chan_count)
    data_spec = pl.BlockSpec((step, blocks, width), lambda i: (i, 0, 0))
    return pl.pallas_call(
        long_conv_kernel,
        grid=(chan_count // step,),
        in_specs=[
            data_spec,
            data_spec,
            pl.BlockSpec((step,) + krow.shape[1:], lambda i: (i, 0, 0)),
            pl.BlockSpec((step,) + tabs.shape[1:], lambda i: (i, 0, 0, 0)),
            pl.BlockSpec((step,) + rows.shape[1:], lambda i: (i, 0, 0)),
        ],
        out_specs=[
            data_spec,
            data_spec,
            pl.BlockSpec((step, 1, modes), lambda i: (i, 0, 0)),
            pl.BlockSpec((step, 1, 128), lambda i: (i, 0, 0)),
        ],
        out_shape=[
            jax.ShapeDtypeStruct(u_blocks.shape, jnp.bfloat16),
            jax.ShapeDtypeStruct(u_blocks.shape, jnp.bfloat16),
            jax.ShapeDtypeStruct((chan_count, 1, modes), jnp.float32),
            jax.ShapeDtypeStruct((chan_count, 1, 128), jnp.float32),
        ],
        cost_estimate=pl.CostEstimate(
            flops=chan_count * 34 * width * width * blocks, transcendentals=chan_count * width * modes,
            bytes_accessed=chan_count * blocks * width * 8 + tabs.size * 2,
        ),
    )(u_blocks, dz_blocks, krow, tabs, rows)


def grouped(function, arrays, group_size):
    stacked = tuple(
        (
            item.reshape((item.shape[0] // group_size, group_size) + item.shape[1:])
            for item in arrays
        )
    )
    results = lax.map(function, stacked)
    return tuple(
        (item.reshape((item.shape[0] * item.shape[1],) + item.shape[2:]) for item in results)
    )


def on_device(projected, cotangent, short_filter, residues, decay_rate, skip_gain):
    proj_rows = projected[0]
    token_count = proj_rows.shape[2]
    chans_tp = proj_rows.shape[1]
    rim_width = short_filter.shape[1] - 1
    grad_out = lax.all_to_all(cotangent[0], "tp", split_axis=0, concat_axis=1, tiled=True).astype(
        jnp.float32
    )
    prev_rim = from_behind(proj_rows[:, :, token_count - rim_width :], "ctx", 1)
    featured = lax.optimization_barrier(
        causal_short(proj_rows, prev_rim, short_filter).astype(jnp.bfloat16)
    )
    query_feat = featured[0].astype(jnp.float32)
    key_feat = featured[1].astype(jnp.float32)
    value_feat = featured[2].astype(jnp.float32)
    product = (key_feat * value_feat).astype(jnp.bfloat16)
    adjoint = (grad_out * query_feat).astype(jnp.bfloat16)
    ctx_count = lax.axis_size("ctx")
    token_total = token_count * ctx_count * lax.axis_size("dp")
    weight_all = residues * jnp.sqrt(2.0 * decay_rate)
    product_all, adjoint_all = (
        lax.all_to_all(product, "ctx", split_axis=0, concat_axis=1, tiled=True),
        lax.all_to_all(adjoint, "ctx", split_axis=0, concat_axis=1, tiled=True),
    )
    chan_count = chans_tp // ctx_count
    chan_start = lax.axis_index("ctx") * chan_count
    rate_rows = lax.dynamic_slice_in_dim(decay_rate, chan_start, chan_count, 0)
    weight_rows = lax.dynamic_slice_in_dim(weight_all, chan_start, chan_count, 0)
    gain_rows = lax.dynamic_slice_in_dim(skip_gain, chan_start, chan_count, 0)
    length = product_all.shape[1]
    block_len = math.gcd(256, length)
    block_count = length // block_len
    conv_blocks, back_blocks, mode_part, skip_part = long_conv(
        product_all.reshape(chan_count, block_count, block_len),
        adjoint_all.reshape(chan_count, block_count, block_len),
        rate_rows,
        weight_rows,
        gain_rows,
    )
    conv_rows = conv_blocks.reshape(chan_count, length)
    back_rows = back_blocks.reshape(chan_count, length)
    mode_part = mode_part[:, 0, :]
    skip_part = skip_part[:, 0, 0]
    signal, back_signal = (
        lax.all_to_all(conv_rows, "ctx", split_axis=1, concat_axis=0, tiled=True),
        lax.all_to_all(back_rows, "ctx", split_axis=1, concat_axis=0, tiled=True),
    )
    grad_scale = 1.0 / math.sqrt(token_total)
    local_grads = jnp.concatenate(
        [mode_part * jnp.sqrt(2.0 * rate_rows) * grad_scale, skip_part[:, None] * grad_scale], axis=1
    )
    local_grads = lax.psum(local_grads, "dp")
    spread = jnp.broadcast_to(local_grads[None], (ctx_count,) + local_grads.shape)
    gathered = lax.all_to_all(spread, "ctx", split_axis=0, concat_axis=0, tiled=True)
    gathered = gathered.reshape(chans_tp, local_grads.shape[1])
    residue_grad = gathered[:, : mode_part.shape[1]]
    skip_grad = gathered[:, mode_part.shape[1]]
    conv_wide = signal.astype(jnp.float32)
    back_wide = back_signal.astype(jnp.float32)
    hyena_out = (query_feat * conv_wide).astype(jnp.bfloat16)
    feature_grad = jnp.stack(
        [grad_out * conv_wide, back_wide * value_feat, back_wide * key_feat]
    ).astype(jnp.bfloat16)
    next_rim = from_behind(feature_grad[:, :, :rim_width], "ctx", -1)
    input_grad = anticausal_short(feature_grad, next_rim, short_filter).astype(jnp.bfloat16)
    return (hyena_out[None], input_grad[None], residue_grad, skip_grad)


def solution(mesh):
    placed = (
        P("dp", None, "tp", "ctx"),
        P("dp", None, ("ctx", "tp")),
        P(None, None, "tp"),
        P("tp", None),
        P("tp", None),
        P("tp"),
    )
    return jax.shard_map(
        on_device,
        mesh=mesh,
        in_specs=placed,
        out_specs=(P("dp", "tp", "ctx"), P("dp", None, "tp", "ctx"), P("tp", None), P("tp")),
        check_vma=False,
    )
```

```python
from functools import partial
import math

import jax
import jax.numpy as jnp
from jax import lax
from jax.sharding import PartitionSpec as P
from jax.experimental import pallas as pl
from jax.experimental.pallas import tpu as pltpu

exact_mode = lax.Precision.HIGHEST
data_mode = lax.Precision.HIGH


def from_behind(shard, axis, by):
    count = lax.axis_size(axis)
    pairs = [(i, i + by) for i in range(count) if 0 <= i + by < count]
    return lax.ppermute(shard, axis, pairs)


def causal_short(proj_rows, prev_rim, tap_weights):
    rim_width = prev_rim.shape[2]
    token_count = proj_rows.shape[2]
    extended = jnp.concatenate([prev_rim, proj_rows], axis=2).astype(jnp.float32)
    result = tap_weights[:, 0, :, None] * extended[:, :, rim_width : rim_width + token_count]
    for lag_index in range(1, rim_width + 1):
        start_at = rim_width - lag_index
        result = (
            result
            + tap_weights[:, lag_index, :, None] * extended[:, :, start_at : start_at + token_count]
        )
    return result


def anticausal_short(grad_rows, next_rim, tap_weights):
    rim_width = next_rim.shape[2]
    token_count = grad_rows.shape[2]
    extended = jnp.concatenate([grad_rows, next_rim], axis=2).astype(jnp.float32)
    result = tap_weights[:, 0, :, None] * extended[:, :, :token_count]
    for lag_index in range(1, rim_width + 1):
        result = (
            result
            + tap_weights[:, lag_index, :, None]
            * extended[:, :, lag_index : lag_index + token_count]
        )
    return result


def make_tables(rate_rows, block_len):
    offsets = jnp.arange(block_len, dtype=jnp.float32)
    fall_now = jnp.exp(-rate_rows[:, :, None] * offsets)
    rise_now = jnp.exp(rate_rows[:, :, None] * offsets)
    fall_next = jnp.exp(-rate_rows[:, :, None] * (offsets + 1.0))
    fall_tail = jnp.exp(-rate_rows[:, :, None] * (block_len - 1.0 - offsets))
    lower_mask = offsets[:, None] >= offsets[None, :]
    return (fall_now, rise_now, fall_next, fall_tail, lower_mask)


def chain_link(earlier, later):
    return (earlier[0] * later[0], later[0] * earlier[1] + later[1])


def modal_pass(signal, rate_rows, weights, incoming, tables):
    fall_now, rise_now, fall_next, fall_tail, lower_mask = tables
    block_len = fall_now.shape[2]
    chan_count, length = signal.shape
    block_count = length // block_len
    pieces = signal.reshape(chan_count, block_count, block_len)
    kernel = jnp.einsum(
        "cnt,cns->cts", weights[:, :, None] * fall_now, rise_now, precision=exact_mode
    )
    kernel = jnp.where(lower_mask[None], kernel, 0.0)
    inside = jnp.einsum("cts,cbs->cbt", kernel, pieces, precision=data_mode)
    block_ends = jnp.einsum("cns,cbs->cnb", fall_tail, pieces, precision=data_mode)
    span_decay = jnp.exp(-rate_rows * block_len)
    block_mults = jnp.broadcast_to(span_decay[:, :, None], block_ends.shape)
    _, running = lax.associative_scan(chain_link, (block_mults, block_ends), axis=2)
    block_steps = jnp.arange(block_count, dtype=jnp.float32)
    before = jnp.concatenate([jnp.zeros_like(running[:, :, :1]), running[:, :, :-1]], axis=2)
    before = (
        before + jnp.exp(-rate_rows[:, :, None] * block_len * block_steps) * incoming[:, :, None]
    )
    carry_in = jnp.einsum(
        "cnt,cnb->cbt", weights[:, :, None] * fall_next, before, precision=exact_mode
    )
    return ((inside + carry_in).reshape(chan_count, length), before)


def mode_products(signal, adjoint, before, tables):
    fall_now, rise_now, fall_next, fall_tail, lower_mask = tables
    block_len = fall_now.shape[2]
    chan_count, length = signal.shape
    block_count = length // block_len
    pieces = signal.reshape(chan_count, block_count, block_len)
    dual_pieces = adjoint.reshape(chan_count, block_count, block_len)
    crossed = jnp.einsum("cbt,cbs->cts", dual_pieces, pieces, precision=data_mode)
    crossed = jnp.where(lower_mask[None], crossed, 0.0)
    weighted = jnp.einsum("cts,cnt->cns", crossed, fall_now, precision=exact_mode)
    inside = jnp.sum(weighted * rise_now, axis=2)
    carried = jnp.einsum("cbt,cnt->cnb", dual_pieces, fall_next, precision=data_mode)
    return inside + jnp.sum(carried * before, axis=2)


def channel_group(group_items, block_len):
    (
        forward_narrow,
        backward_narrow,
        rate_rows,
        weights,
        gain_rows,
        enter_forward,
        enter_backward,
    ) = group_items
    forward_rows = forward_narrow.astype(jnp.float32)
    backward_rows = backward_narrow.astype(jnp.float32)
    tables = make_tables(rate_rows, block_len)
    carried, before = modal_pass(forward_rows, rate_rows, weights, enter_forward, tables)
    returned, _ = modal_pass(jnp.flip(backward_rows, 1), rate_rows, weights, enter_backward, tables)
    signal = (carried + gain_rows[:, None] * forward_rows).astype(jnp.bfloat16)
    back_signal = (jnp.flip(returned, 1) + gain_rows[:, None] * backward_rows).astype(jnp.bfloat16)
    mode_raw = mode_products(forward_rows, backward_rows, before, tables)
    skip_raw = jnp.sum(backward_rows * forward_rows, axis=1)
    return (signal, back_signal, mode_raw, skip_raw)


def split_pair(values):
    high = values.astype(jnp.bfloat16)
    low = (values - high.astype(jnp.float32)).astype(jnp.bfloat16)
    return high, low


def mat_nn(a, b):
    return jnp.dot(a, b, preferred_element_type=jnp.float32)


def mat_nt(a, b):
    return lax.dot_general(a, b, (((1,), (1,)), ((), ())), preferred_element_type=jnp.float32)


def mat_tn(a, b):
    return lax.dot_general(a, b, (((0,), (0,)), ((), ())), preferred_element_type=jnp.float32)


def wide_nn(a, b_pair):
    a_high, a_low = split_pair(a)
    return mat_nn(a_high, b_pair[0]) + mat_nn(a_high, b_pair[1]) + mat_nn(a_low, b_pair[0])


def shifted(values, by, lanes_rows):
    rows = values.shape[0]
    rolled = pltpu.roll(values, by % rows, 0)
    index = lax.broadcasted_iota(jnp.int32, values.shape, 0)
    keep = (index >= by) if by > 0 else (index < rows + by)
    return jnp.where(keep, rolled, 0.0)


def long_conv_kernel(u_ref, dz_ref, krow_ref, tab_ref, row_ref, z_ref, du_ref, mode_ref, skip_ref):
    chans, blocks, width = u_ref.shape
    modes = tab_ref.shape[2]
    col = lax.broadcasted_iota(jnp.int32, (width, width), 1)
    row = lax.broadcasted_iota(jnp.int32, (width, width), 0)
    upper = col >= row
    lower = col <= row
    lag_ids = lax.broadcasted_iota(jnp.int32, (width, modes), 0).astype(jnp.float32)

    def one_channel(c, carry):
        u_narrow = u_ref[c]
        dz_narrow = dz_ref[c]
        tabs = tab_ref[c]
        rows = row_ref[c]
        krow = krow_ref[c]
        fall_end = (tabs[0], tabs[1])
        fall_start = (tabs[2], tabs[3])
        gain_fwd = (tabs[4], tabs[5])
        gain_bwd = (tabs[6], tabs[7])
        rate_row = rows[6:7, :]
        step_row = rows[5:6, :]
        gain = rows[7:8, 0:1]
        ahead = pltpu.roll(jnp.broadcast_to(krow[0:1, :], (width, width)), 0, 1, stride=1, stride_axis=0)
        ahead = jnp.where(upper, ahead, 0.0)
        behind = pltpu.roll(jnp.broadcast_to(krow[1:2, :], (width, width)), 1, 1, stride=1, stride_axis=0)
        behind = jnp.where(lower, behind, 0.0)
        a_high, a_low = split_pair(ahead)
        b_high, b_low = split_pair(behind)
        z_in = mat_nn(
            jnp.concatenate([u_narrow, u_narrow], axis=1), jnp.concatenate([a_high, a_low], axis=0)
        )
        du_in = mat_nn(
            jnp.concatenate([dz_narrow, dz_narrow], axis=1), jnp.concatenate([b_high, b_low], axis=0)
        )
        ends = mat_nt(u_narrow, fall_end[0]) + mat_nt(u_narrow, fall_end[1])
        starts = mat_nt(dz_narrow, fall_start[0]) + mat_nt(dz_narrow, fall_start[1])
        fwd_state = ends
        bwd_state = starts
        level = 0
        span = 1
        while span < blocks:
            decay = rows[level : level + 1, :]
            fwd_state = fwd_state + decay * shifted(fwd_state, span, blocks)
            bwd_state = bwd_state + decay * shifted(bwd_state, -span, blocks)
            level += 1
            span *= 2
        state_before = shifted(fwd_state, 1, blocks)
        state_after = shifted(bwd_state, -1, blocks)
        z_carry = wide_nn(state_before, gain_fwd)
        du_carry = wide_nn(state_after, gain_bwd)
        u_wide = u_narrow.astype(jnp.float32)
        dz_wide = dz_narrow.astype(jnp.float32)
        z_ref[c] = (z_in + z_carry + gain * u_wide).astype(z_ref.dtype)
        du_ref[c] = (du_in + du_carry + gain * dz_wide).astype(du_ref.dtype)
        rise = jnp.exp(lag_ids * rate_row)
        crossed = mat_tn(u_narrow, dz_narrow)
        crossed = jnp.where(upper, crossed, 0.0)
        c_high, c_low = split_pair(crossed)
        weighted = (
            mat_nt(c_high, fall_start[0]) + mat_nt(c_high, fall_start[1]) + mat_nt(c_low, fall_start[0])
        )
        mode_in = jnp.sum(weighted * rise, axis=0, keepdims=True)
        mode_carry = jnp.sum(state_before * starts, axis=0, keepdims=True) * step_row
        mode_ref[c] = mode_in + mode_carry
        skip_ref[c] = jnp.broadcast_to(jnp.sum(u_wide * dz_wide), skip_ref.shape[1:])
        return carry

    lax.fori_loop(0, chans, one_channel, 0, unroll=8)


def long_conv_tables(rate_rows, weight_rows, gain_rows, width, blocks):
    offsets = jnp.arange(width, dtype=jnp.float32)
    rate = rate_rows[:, :, None]
    weight = weight_rows[:, :, None]
    fall_end = jnp.exp(-rate * (width - 1.0 - offsets))
    fall_start = jnp.exp(-rate * offsets)
    gain_fwd = weight * jnp.exp(-rate * (offsets + 1.0))
    gain_bwd = weight * jnp.exp(-rate * (width - offsets))
    pairs = []
    for table in (fall_end, fall_start, gain_fwd, gain_bwd):
        high = lax.reduce_precision(table, exponent_bits=8, mantissa_bits=7)
        pairs.extend((high.astype(jnp.bfloat16), (table - high).astype(jnp.bfloat16)))
    tabs = jnp.stack(pairs, axis=1)
    levels = []
    span = 1
    while span < blocks:
        levels.append(jnp.exp(-rate_rows * (width * span)))
        span *= 2
    chan_count, modes = rate_rows.shape
    while len(levels) < 5:
        levels.append(jnp.zeros_like(rate_rows))
    levels.append(jnp.exp(-rate_rows))
    levels.append(rate_rows)
    levels.append(jnp.broadcast_to(gain_rows[:, None], (chan_count, modes)))
    lag_kernel = jnp.sum(weight * fall_start, axis=1)
    krow = jnp.stack([lag_kernel, jnp.flip(lag_kernel, axis=1)], axis=1)
    return tabs, jnp.stack(levels, axis=1), krow


def long_conv(u_blocks, dz_blocks, rate_rows, weight_rows, gain_rows, chans_per_step=8):
    chan_count, blocks, width = u_blocks.shape
    modes = rate_rows.shape[1]
    tabs, rows, krow = long_conv_tables(rate_rows, weight_rows, gain_rows, width, blocks)
    step = min(chans_per_step, chan_count)
    data_spec = pl.BlockSpec((step, blocks, width), lambda i: (i, 0, 0))
    return pl.pallas_call(
        long_conv_kernel,
        grid=(chan_count // step,),
        in_specs=[
            data_spec,
            data_spec,
            pl.BlockSpec((step,) + krow.shape[1:], lambda i: (i, 0, 0)),
            pl.BlockSpec((step,) + tabs.shape[1:], lambda i: (i, 0, 0, 0)),
            pl.BlockSpec((step,) + rows.shape[1:], lambda i: (i, 0, 0)),
        ],
        out_specs=[
            data_spec,
            data_spec,
            pl.BlockSpec((step, 1, modes), lambda i: (i, 0, 0)),
            pl.BlockSpec((step, 1, 128), lambda i: (i, 0, 0)),
        ],
        out_shape=[
            jax.ShapeDtypeStruct(u_blocks.shape, jnp.bfloat16),
            jax.ShapeDtypeStruct(u_blocks.shape, jnp.bfloat16),
            jax.ShapeDtypeStruct((chan_count, 1, modes), jnp.float32),
            jax.ShapeDtypeStruct((chan_count, 1, 128), jnp.float32),
        ],
        cost_estimate=pl.CostEstimate(
            flops=chan_count * 34 * width * width * blocks, transcendentals=chan_count * width * modes,
            bytes_accessed=chan_count * blocks * width * 8 + tabs.size * 2,
        ),
    )(u_blocks, dz_blocks, krow, tabs, rows)


def grouped(function, arrays, group_size):
    stacked = tuple(
        (
            item.reshape((item.shape[0] // group_size, group_size) + item.shape[1:])
            for item in arrays
        )
    )
    results = lax.map(function, stacked)
    return tuple(
        (item.reshape((item.shape[0] * item.shape[1],) + item.shape[2:]) for item in results)
    )


def on_device(projected, cotangent, short_filter, residues, decay_rate, skip_gain):
    proj_rows = projected[0]
    token_count = proj_rows.shape[2]
    chans_tp = proj_rows.shape[1]
    rim_width = short_filter.shape[1] - 1
    grad_out = lax.all_to_all(cotangent[0], "tp", split_axis=0, concat_axis=1, tiled=True).astype(
        jnp.float32
    )
    prev_rim = from_behind(proj_rows[:, :, token_count - rim_width :], "ctx", 1)
    featured = lax.optimization_barrier(
        causal_short(proj_rows, prev_rim, short_filter).astype(jnp.bfloat16)
    )
    query_feat = featured[0].astype(jnp.float32)
    key_feat = featured[1].astype(jnp.float32)
    value_feat = featured[2].astype(jnp.float32)
    product = (key_feat * value_feat).astype(jnp.bfloat16)
    adjoint = (grad_out * query_feat).astype(jnp.bfloat16)
    ctx_count = lax.axis_size("ctx")
    token_total = token_count * ctx_count * lax.axis_size("dp")
    weight_all = residues * jnp.sqrt(2.0 * decay_rate)
    product_all, adjoint_all = (
        lax.all_to_all(product, "ctx", split_axis=0, concat_axis=1, tiled=True),
        lax.all_to_all(adjoint, "ctx", split_axis=0, concat_axis=1, tiled=True),
    )
    chan_count = chans_tp // ctx_count
    chan_start = lax.axis_index("ctx") * chan_count
    rate_rows = lax.dynamic_slice_in_dim(decay_rate, chan_start, chan_count, 0)
    weight_rows = lax.dynamic_slice_in_dim(weight_all, chan_start, chan_count, 0)
    gain_rows = lax.dynamic_slice_in_dim(skip_gain, chan_start, chan_count, 0)
    length = product_all.shape[1]
    block_len = math.gcd(256, length)
    block_count = length // block_len
    conv_blocks, back_blocks, mode_part, skip_part = long_conv(
        product_all.reshape(chan_count, block_count, block_len),
        adjoint_all.reshape(chan_count, block_count, block_len),
        rate_rows,
        weight_rows,
        gain_rows,
    )
    conv_rows = conv_blocks.reshape(chan_count, length)
    back_rows = back_blocks.reshape(chan_count, length)
    mode_part = mode_part[:, 0, :]
    skip_part = skip_part[:, 0, 0]
    signal, back_signal = (
        lax.all_to_all(conv_rows, "ctx", split_axis=1, concat_axis=0, tiled=True),
        lax.all_to_all(back_rows, "ctx", split_axis=1, concat_axis=0, tiled=True),
    )
    grad_scale = 1.0 / math.sqrt(token_total)
    local_grads = jnp.concatenate(
        [mode_part * jnp.sqrt(2.0 * rate_rows) * grad_scale, skip_part[:, None] * grad_scale], axis=1
    )
    dp_count = lax.axis_size("dp")
    if dp_count & (dp_count - 1) == 0:
        hop = 1
        while hop < dp_count:
            partners = [(i, i ^ hop) for i in range(dp_count)]
            local_grads = local_grads + lax.ppermute(local_grads, "dp", partners)
            hop *= 2
    else:
        local_grads = lax.psum(local_grads, "dp")
    spread = jnp.broadcast_to(local_grads[None], (ctx_count,) + local_grads.shape)
    gathered = lax.all_to_all(spread, "ctx", split_axis=0, concat_axis=0, tiled=True)
    gathered = gathered.reshape(chans_tp, local_grads.shape[1])
    residue_grad = gathered[:, : mode_part.shape[1]]
    skip_grad = gathered[:, mode_part.shape[1]]
    conv_wide = signal.astype(jnp.float32)
    back_wide = back_signal.astype(jnp.float32)
    hyena_out = (query_feat * conv_wide).astype(jnp.bfloat16)
    feature_grad = jnp.stack(
        [grad_out * conv_wide, back_wide * value_feat, back_wide * key_feat]
    ).astype(jnp.bfloat16)
    next_rim = from_behind(feature_grad[:, :, :rim_width], "ctx", -1)
    input_grad = anticausal_short(feature_grad, next_rim, short_filter).astype(jnp.bfloat16)
    return (hyena_out[None], input_grad[None], residue_grad, skip_grad)


def solution(mesh):
    placed = (
        P("dp", None, "tp", "ctx"),
        P("dp", None, ("ctx", "tp")),
        P(None, None, "tp"),
        P("tp", None),
        P("tp", None),
        P("tp"),
    )
    return jax.shard_map(
        on_device,
        mesh=mesh,
        in_specs=placed,
        out_specs=(P("dp", "tp", "ctx"), P("dp", None, "tp", "ctx"), P("tp", None), P("tp")),
        check_vma=False,
    )
```

```python
from functools import partial
import math

import jax
import jax.numpy as jnp
from jax import lax
from jax.sharding import PartitionSpec as P
from jax.experimental import pallas as pl
from jax.experimental.pallas import tpu as pltpu

exact_mode = lax.Precision.HIGHEST
data_mode = lax.Precision.HIGH


def from_behind(shard, axis, by):
    count = lax.axis_size(axis)
    pairs = [(i, i + by) for i in range(count) if 0 <= i + by < count]
    return lax.ppermute(shard, axis, pairs)


def causal_short(proj_rows, prev_rim, tap_weights):
    rim_width = prev_rim.shape[2]
    token_count = proj_rows.shape[2]
    extended = jnp.concatenate([prev_rim, proj_rows], axis=2).astype(jnp.float32)
    result = tap_weights[:, 0, :, None] * extended[:, :, rim_width : rim_width + token_count]
    for lag_index in range(1, rim_width + 1):
        start_at = rim_width - lag_index
        result = (
            result
            + tap_weights[:, lag_index, :, None] * extended[:, :, start_at : start_at + token_count]
        )
    return result


def anticausal_short(grad_rows, next_rim, tap_weights):
    rim_width = next_rim.shape[2]
    token_count = grad_rows.shape[2]
    extended = jnp.concatenate([grad_rows, next_rim], axis=2).astype(jnp.float32)
    result = tap_weights[:, 0, :, None] * extended[:, :, :token_count]
    for lag_index in range(1, rim_width + 1):
        result = (
            result
            + tap_weights[:, lag_index, :, None]
            * extended[:, :, lag_index : lag_index + token_count]
        )
    return result


def make_tables(rate_rows, block_len):
    offsets = jnp.arange(block_len, dtype=jnp.float32)
    fall_now = jnp.exp(-rate_rows[:, :, None] * offsets)
    rise_now = jnp.exp(rate_rows[:, :, None] * offsets)
    fall_next = jnp.exp(-rate_rows[:, :, None] * (offsets + 1.0))
    fall_tail = jnp.exp(-rate_rows[:, :, None] * (block_len - 1.0 - offsets))
    lower_mask = offsets[:, None] >= offsets[None, :]
    return (fall_now, rise_now, fall_next, fall_tail, lower_mask)


def chain_link(earlier, later):
    return (earlier[0] * later[0], later[0] * earlier[1] + later[1])


def modal_pass(signal, rate_rows, weights, incoming, tables):
    fall_now, rise_now, fall_next, fall_tail, lower_mask = tables
    block_len = fall_now.shape[2]
    chan_count, length = signal.shape
    block_count = length // block_len
    pieces = signal.reshape(chan_count, block_count, block_len)
    kernel = jnp.einsum(
        "cnt,cns->cts", weights[:, :, None] * fall_now, rise_now, precision=exact_mode
    )
    kernel = jnp.where(lower_mask[None], kernel, 0.0)
    inside = jnp.einsum("cts,cbs->cbt", kernel, pieces, precision=data_mode)
    block_ends = jnp.einsum("cns,cbs->cnb", fall_tail, pieces, precision=data_mode)
    span_decay = jnp.exp(-rate_rows * block_len)
    block_mults = jnp.broadcast_to(span_decay[:, :, None], block_ends.shape)
    _, running = lax.associative_scan(chain_link, (block_mults, block_ends), axis=2)
    block_steps = jnp.arange(block_count, dtype=jnp.float32)
    before = jnp.concatenate([jnp.zeros_like(running[:, :, :1]), running[:, :, :-1]], axis=2)
    before = (
        before + jnp.exp(-rate_rows[:, :, None] * block_len * block_steps) * incoming[:, :, None]
    )
    carry_in = jnp.einsum(
        "cnt,cnb->cbt", weights[:, :, None] * fall_next, before, precision=exact_mode
    )
    return ((inside + carry_in).reshape(chan_count, length), before)


def mode_products(signal, adjoint, before, tables):
    fall_now, rise_now, fall_next, fall_tail, lower_mask = tables
    block_len = fall_now.shape[2]
    chan_count, length = signal.shape
    block_count = length // block_len
    pieces = signal.reshape(chan_count, block_count, block_len)
    dual_pieces = adjoint.reshape(chan_count, block_count, block_len)
    crossed = jnp.einsum("cbt,cbs->cts", dual_pieces, pieces, precision=data_mode)
    crossed = jnp.where(lower_mask[None], crossed, 0.0)
    weighted = jnp.einsum("cts,cnt->cns", crossed, fall_now, precision=exact_mode)
    inside = jnp.sum(weighted * rise_now, axis=2)
    carried = jnp.einsum("cbt,cnt->cnb", dual_pieces, fall_next, precision=data_mode)
    return inside + jnp.sum(carried * before, axis=2)


def channel_group(group_items, block_len):
    (
        forward_narrow,
        backward_narrow,
        rate_rows,
        weights,
        gain_rows,
        enter_forward,
        enter_backward,
    ) = group_items
    forward_rows = forward_narrow.astype(jnp.float32)
    backward_rows = backward_narrow.astype(jnp.float32)
    tables = make_tables(rate_rows, block_len)
    carried, before = modal_pass(forward_rows, rate_rows, weights, enter_forward, tables)
    returned, _ = modal_pass(jnp.flip(backward_rows, 1), rate_rows, weights, enter_backward, tables)
    signal = (carried + gain_rows[:, None] * forward_rows).astype(jnp.bfloat16)
    back_signal = (jnp.flip(returned, 1) + gain_rows[:, None] * backward_rows).astype(jnp.bfloat16)
    mode_raw = mode_products(forward_rows, backward_rows, before, tables)
    skip_raw = jnp.sum(backward_rows * forward_rows, axis=1)
    return (signal, back_signal, mode_raw, skip_raw)


def split_pair(values):
    high = values.astype(jnp.bfloat16)
    low = (values - high.astype(jnp.float32)).astype(jnp.bfloat16)
    return high, low


def mat_nn(a, b):
    return jnp.dot(a, b, preferred_element_type=jnp.float32)


def mat_nt(a, b):
    return lax.dot_general(a, b, (((1,), (1,)), ((), ())), preferred_element_type=jnp.float32)


def mat_tn(a, b):
    return lax.dot_general(a, b, (((0,), (0,)), ((), ())), preferred_element_type=jnp.float32)


def wide_nn(a, b_pair):
    a_high, a_low = split_pair(a)
    return mat_nn(a_high, b_pair[0]) + mat_nn(a_high, b_pair[1]) + mat_nn(a_low, b_pair[0])


def shifted(values, by, lanes_rows):
    rows = values.shape[0]
    rolled = pltpu.roll(values, by % rows, 0)
    index = lax.broadcasted_iota(jnp.int32, values.shape, 0)
    keep = (index >= by) if by > 0 else (index < rows + by)
    return jnp.where(keep, rolled, 0.0)


def long_conv_kernel(u_ref, dz_ref, krow_ref, tab_ref, row_ref, z_ref, du_ref, mode_ref, skip_ref):
    chans, blocks, width = u_ref.shape
    modes = tab_ref.shape[2]
    col = lax.broadcasted_iota(jnp.int32, (width, width), 1)
    row = lax.broadcasted_iota(jnp.int32, (width, width), 0)
    upper = col >= row
    lower = col <= row
    lag_ids = lax.broadcasted_iota(jnp.int32, (width, modes), 0).astype(jnp.float32)

    def one_channel(c, carry):
        u_narrow = u_ref[c]
        dz_narrow = dz_ref[c]
        tabs = tab_ref[c]
        rows = row_ref[c]
        krow = krow_ref[c]
        fall_end = (tabs[0], tabs[1])
        fall_start = (tabs[2], tabs[3])
        gain_fwd = (tabs[4], tabs[5])
        gain_bwd = (tabs[6], tabs[7])
        rate_row = rows[6:7, :]
        step_row = rows[5:6, :]
        gain = rows[7:8, 0:1]
        ahead = pltpu.roll(jnp.broadcast_to(krow[0:1, :], (width, width)), 0, 1, stride=1, stride_axis=0)
        ahead = jnp.where(upper, ahead, 0.0)
        behind = pltpu.roll(jnp.broadcast_to(krow[1:2, :], (width, width)), 1, 1, stride=1, stride_axis=0)
        behind = jnp.where(lower, behind, 0.0)
        a_high, a_low = split_pair(ahead)
        b_high, b_low = split_pair(behind)
        z_in = mat_nn(
            jnp.concatenate([u_narrow, u_narrow], axis=1), jnp.concatenate([a_high, a_low], axis=0)
        )
        du_in = mat_nn(
            jnp.concatenate([dz_narrow, dz_narrow], axis=1), jnp.concatenate([b_high, b_low], axis=0)
        )
        ends = mat_nt(u_narrow, fall_end[0]) + mat_nt(u_narrow, fall_end[1])
        starts = mat_nt(dz_narrow, fall_start[0]) + mat_nt(dz_narrow, fall_start[1])
        fwd_state = ends
        bwd_state = starts
        level = 0
        span = 1
        while span < blocks:
            decay = rows[level : level + 1, :]
            fwd_state = fwd_state + decay * shifted(fwd_state, span, blocks)
            bwd_state = bwd_state + decay * shifted(bwd_state, -span, blocks)
            level += 1
            span *= 2
        state_before = shifted(fwd_state, 1, blocks)
        state_after = shifted(bwd_state, -1, blocks)
        z_carry = wide_nn(state_before, gain_fwd)
        du_carry = wide_nn(state_after, gain_bwd)
        u_wide = u_narrow.astype(jnp.float32)
        dz_wide = dz_narrow.astype(jnp.float32)
        z_ref[c] = (z_in + z_carry + gain * u_wide).astype(z_ref.dtype)
        du_ref[c] = (du_in + du_carry + gain * dz_wide).astype(du_ref.dtype)
        rise = jnp.exp(lag_ids * rate_row)
        crossed = mat_tn(u_narrow, dz_narrow)
        crossed = jnp.where(upper, crossed, 0.0)
        c_high, c_low = split_pair(crossed)
        weighted = (
            mat_nt(c_high, fall_start[0]) + mat_nt(c_high, fall_start[1]) + mat_nt(c_low, fall_start[0])
        )
        mode_in = jnp.sum(weighted * rise, axis=0, keepdims=True)
        mode_carry = jnp.sum(state_before * starts, axis=0, keepdims=True) * step_row
        mode_ref[c] = mode_in + mode_carry
        skip_ref[c] = jnp.broadcast_to(jnp.sum(u_wide * dz_wide), skip_ref.shape[1:])
        return carry

    lax.fori_loop(0, chans, one_channel, 0, unroll=8)


def long_conv_tables(rate_rows, weight_rows, gain_rows, width, blocks):
    offsets = jnp.arange(width, dtype=jnp.float32)
    rate = rate_rows[:, :, None]
    weight = weight_rows[:, :, None]
    fall_end = jnp.exp(-rate * (width - 1.0 - offsets))
    fall_start = jnp.exp(-rate * offsets)
    gain_fwd = weight * jnp.exp(-rate * (offsets + 1.0))
    gain_bwd = weight * jnp.exp(-rate * (width - offsets))
    pairs = []
    for table in (fall_end, fall_start, gain_fwd, gain_bwd):
        high = lax.reduce_precision(table, exponent_bits=8, mantissa_bits=7)
        pairs.extend((high.astype(jnp.bfloat16), (table - high).astype(jnp.bfloat16)))
    tabs = jnp.stack(pairs, axis=1)
    levels = []
    span = 1
    while span < blocks:
        levels.append(jnp.exp(-rate_rows * (width * span)))
        span *= 2
    chan_count, modes = rate_rows.shape
    while len(levels) < 5:
        levels.append(jnp.zeros_like(rate_rows))
    levels.append(jnp.exp(-rate_rows))
    levels.append(rate_rows)
    levels.append(jnp.broadcast_to(gain_rows[:, None], (chan_count, modes)))
    lag_kernel = jnp.sum(weight * fall_start, axis=1)
    krow = jnp.stack([lag_kernel, jnp.flip(lag_kernel, axis=1)], axis=1)
    return tabs, jnp.stack(levels, axis=1), krow


def long_conv(u_blocks, dz_blocks, rate_rows, weight_rows, gain_rows, chans_per_step=8):
    chan_count, blocks, width = u_blocks.shape
    modes = rate_rows.shape[1]
    tabs, rows, krow = long_conv_tables(rate_rows, weight_rows, gain_rows, width, blocks)
    step = min(chans_per_step, chan_count)
    data_spec = pl.BlockSpec((step, blocks, width), lambda i: (i, 0, 0))
    return pl.pallas_call(
        long_conv_kernel,
        grid=(chan_count // step,),
        in_specs=[
            data_spec,
            data_spec,
            pl.BlockSpec((step,) + krow.shape[1:], lambda i: (i, 0, 0)),
            pl.BlockSpec((step,) + tabs.shape[1:], lambda i: (i, 0, 0, 0)),
            pl.BlockSpec((step,) + rows.shape[1:], lambda i: (i, 0, 0)),
        ],
        out_specs=[
            data_spec,
            data_spec,
            pl.BlockSpec((step, 1, modes), lambda i: (i, 0, 0)),
            pl.BlockSpec((step, 1, 128), lambda i: (i, 0, 0)),
        ],
        out_shape=[
            jax.ShapeDtypeStruct(u_blocks.shape, jnp.bfloat16),
            jax.ShapeDtypeStruct(u_blocks.shape, jnp.bfloat16),
            jax.ShapeDtypeStruct((chan_count, 1, modes), jnp.float32),
            jax.ShapeDtypeStruct((chan_count, 1, 128), jnp.float32),
        ],
        cost_estimate=pl.CostEstimate(
            flops=chan_count * 800 * width * width * blocks, transcendentals=chan_count * width * modes,
            bytes_accessed=chan_count * blocks * width * 8 + tabs.size * 2,
        ),
    )(u_blocks, dz_blocks, krow, tabs, rows)


def grouped(function, arrays, group_size):
    stacked = tuple(
        (
            item.reshape((item.shape[0] // group_size, group_size) + item.shape[1:])
            for item in arrays
        )
    )
    results = lax.map(function, stacked)
    return tuple(
        (item.reshape((item.shape[0] * item.shape[1],) + item.shape[2:]) for item in results)
    )


def on_device(projected, cotangent, short_filter, residues, decay_rate, skip_gain, halves=2):
    proj_rows = projected[0]
    token_count = proj_rows.shape[2]
    chans_tp = proj_rows.shape[1]
    rim_width = short_filter.shape[1] - 1
    grad_out = lax.all_to_all(cotangent[0], "tp", split_axis=0, concat_axis=1, tiled=True).astype(
        jnp.float32
    )
    prev_rim = from_behind(proj_rows[:, :, token_count - rim_width :], "ctx", 1)
    featured = lax.optimization_barrier(
        causal_short(proj_rows, prev_rim, short_filter).astype(jnp.bfloat16)
    )
    query_feat = featured[0].astype(jnp.float32)
    key_feat = featured[1].astype(jnp.float32)
    value_feat = featured[2].astype(jnp.float32)
    product = (key_feat * value_feat).astype(jnp.bfloat16)
    adjoint = (grad_out * query_feat).astype(jnp.bfloat16)
    ctx_count = lax.axis_size("ctx")
    token_total = token_count * ctx_count * lax.axis_size("dp")
    weight_all = residues * jnp.sqrt(2.0 * decay_rate)
    part = chans_tp // halves
    chan_count = part // ctx_count
    grad_scale = 1.0 / math.sqrt(token_total)
    outs, grads_out, grad_parts = [], [], []
    for half in range(halves):
        chans = slice(half * part, (half + 1) * part)
        product_all = lax.all_to_all(product[chans], "ctx", split_axis=0, concat_axis=1, tiled=True)
        adjoint_all = lax.all_to_all(adjoint[chans], "ctx", split_axis=0, concat_axis=1, tiled=True)
        chan_start = half * part + lax.axis_index("ctx") * chan_count
        rate_rows = lax.dynamic_slice_in_dim(decay_rate, chan_start, chan_count, 0)
        weight_rows = lax.dynamic_slice_in_dim(weight_all, chan_start, chan_count, 0)
        gain_rows = lax.dynamic_slice_in_dim(skip_gain, chan_start, chan_count, 0)
        length = product_all.shape[1]
        block_len = math.gcd(256, length)
        block_count = length // block_len
        conv_blocks, back_blocks, mode_part, skip_part = long_conv(
            product_all.reshape(chan_count, block_count, block_len),
            adjoint_all.reshape(chan_count, block_count, block_len),
            rate_rows,
            weight_rows,
            gain_rows,
        )
        mode_part = mode_part[:, 0, :]
        skip_part = skip_part[:, 0, 0]
        grad_parts.append(
            jnp.concatenate(
                [mode_part * jnp.sqrt(2.0 * rate_rows) * grad_scale, skip_part[:, None] * grad_scale],
                axis=1,
            )
        )
        signal = lax.all_to_all(
            conv_blocks.reshape(chan_count, length), "ctx", split_axis=1, concat_axis=0, tiled=True
        )
        back_signal = lax.all_to_all(
            back_blocks.reshape(chan_count, length), "ctx", split_axis=1, concat_axis=0, tiled=True
        )
        conv_wide = signal.astype(jnp.float32)
        back_wide = back_signal.astype(jnp.float32)
        outs.append((query_feat[chans] * conv_wide).astype(jnp.bfloat16))
        feature_grad = jnp.stack(
            [grad_out[chans] * conv_wide, back_wide * value_feat[chans], back_wide * key_feat[chans]]
        ).astype(jnp.bfloat16)
        next_rim = from_behind(feature_grad[:, :, :rim_width], "ctx", -1)
        grads_out.append(
            anticausal_short(feature_grad, next_rim, short_filter[:, :, chans]).astype(jnp.bfloat16)
        )
    hyena_out = jnp.concatenate(outs, axis=0)
    input_grad = jnp.concatenate(grads_out, axis=1)
    local_grads = jnp.concatenate(grad_parts, axis=0)
    grad_cols = local_grads.shape[1]
    dp_count = lax.axis_size("dp")
    if dp_count & (dp_count - 1) == 0:
        hop = 1
        while hop < dp_count:
            partners = [(i, i ^ hop) for i in range(dp_count)]
            local_grads = local_grads + lax.ppermute(local_grads, "dp", partners)
            hop *= 2
    else:
        local_grads = lax.psum(local_grads, "dp")
    spread = jnp.broadcast_to(local_grads[None], (ctx_count,) + local_grads.shape)
    gathered = lax.all_to_all(spread, "ctx", split_axis=0, concat_axis=0, tiled=True)
    gathered = gathered.reshape(ctx_count, halves, chan_count, grad_cols)
    gathered = jnp.swapaxes(gathered, 0, 1).reshape(chans_tp, grad_cols)
    residue_grad = gathered[:, : grad_cols - 1]
    skip_grad = gathered[:, grad_cols - 1]
    return (hyena_out[None], input_grad[None], residue_grad, skip_grad)


def solution(mesh):
    placed = (
        P("dp", None, "tp", "ctx"),
        P("dp", None, ("ctx", "tp")),
        P(None, None, "tp"),
        P("tp", None),
        P("tp", None),
        P("tp"),
    )
    return jax.shard_map(
        on_device,
        mesh=mesh,
        in_specs=placed,
        out_specs=(P("dp", "tp", "ctx"), P("dp", None, "tp", "ctx"), P("tp", None), P("tp")),
        check_vma=False,
    )
```

```python
from functools import partial
import math

import jax
import jax.numpy as jnp
from jax import lax
from jax.sharding import PartitionSpec as P
from jax.experimental import pallas as pl
from jax.experimental.pallas import tpu as pltpu

exact_mode = lax.Precision.HIGHEST
data_mode = lax.Precision.HIGH


def from_behind(shard, axis, by):
    count = lax.axis_size(axis)
    pairs = [(i, i + by) for i in range(count) if 0 <= i + by < count]
    return lax.ppermute(shard, axis, pairs)


def causal_short(proj_rows, prev_rim, tap_weights):
    rim_width = prev_rim.shape[2]
    token_count = proj_rows.shape[2]
    extended = jnp.concatenate([prev_rim, proj_rows], axis=2).astype(jnp.float32)
    result = tap_weights[:, 0, :, None] * extended[:, :, rim_width : rim_width + token_count]
    for lag_index in range(1, rim_width + 1):
        start_at = rim_width - lag_index
        result = (
            result
            + tap_weights[:, lag_index, :, None] * extended[:, :, start_at : start_at + token_count]
        )
    return result


def anticausal_short(grad_rows, next_rim, tap_weights):
    rim_width = next_rim.shape[2]
    token_count = grad_rows.shape[2]
    extended = jnp.concatenate([grad_rows, next_rim], axis=2).astype(jnp.float32)
    result = tap_weights[:, 0, :, None] * extended[:, :, :token_count]
    for lag_index in range(1, rim_width + 1):
        result = (
            result
            + tap_weights[:, lag_index, :, None]
            * extended[:, :, lag_index : lag_index + token_count]
        )
    return result


def make_tables(rate_rows, block_len):
    offsets = jnp.arange(block_len, dtype=jnp.float32)
    fall_now = jnp.exp(-rate_rows[:, :, None] * offsets)
    rise_now = jnp.exp(rate_rows[:, :, None] * offsets)
    fall_next = jnp.exp(-rate_rows[:, :, None] * (offsets + 1.0))
    fall_tail = jnp.exp(-rate_rows[:, :, None] * (block_len - 1.0 - offsets))
    lower_mask = offsets[:, None] >= offsets[None, :]
    return (fall_now, rise_now, fall_next, fall_tail, lower_mask)


def chain_link(earlier, later):
    return (earlier[0] * later[0], later[0] * earlier[1] + later[1])


def modal_pass(signal, rate_rows, weights, incoming, tables):
    fall_now, rise_now, fall_next, fall_tail, lower_mask = tables
    block_len = fall_now.shape[2]
    chan_count, length = signal.shape
    block_count = length // block_len
    pieces = signal.reshape(chan_count, block_count, block_len)
    kernel = jnp.einsum(
        "cnt,cns->cts", weights[:, :, None] * fall_now, rise_now, precision=exact_mode
    )
    kernel = jnp.where(lower_mask[None], kernel, 0.0)
    inside = jnp.einsum("cts,cbs->cbt", kernel, pieces, precision=data_mode)
    block_ends = jnp.einsum("cns,cbs->cnb", fall_tail, pieces, precision=data_mode)
    span_decay = jnp.exp(-rate_rows * block_len)
    block_mults = jnp.broadcast_to(span_decay[:, :, None], block_ends.shape)
    _, running = lax.associative_scan(chain_link, (block_mults, block_ends), axis=2)
    block_steps = jnp.arange(block_count, dtype=jnp.float32)
    before = jnp.concatenate([jnp.zeros_like(running[:, :, :1]), running[:, :, :-1]], axis=2)
    before = (
        before + jnp.exp(-rate_rows[:, :, None] * block_len * block_steps) * incoming[:, :, None]
    )
    carry_in = jnp.einsum(
        "cnt,cnb->cbt", weights[:, :, None] * fall_next, before, precision=exact_mode
    )
    return ((inside + carry_in).reshape(chan_count, length), before)


def mode_products(signal, adjoint, before, tables):
    fall_now, rise_now, fall_next, fall_tail, lower_mask = tables
    block_len = fall_now.shape[2]
    chan_count, length = signal.shape
    block_count = length // block_len
    pieces = signal.reshape(chan_count, block_count, block_len)
    dual_pieces = adjoint.reshape(chan_count, block_count, block_len)
    crossed = jnp.einsum("cbt,cbs->cts", dual_pieces, pieces, precision=data_mode)
    crossed = jnp.where(lower_mask[None], crossed, 0.0)
    weighted = jnp.einsum("cts,cnt->cns", crossed, fall_now, precision=exact_mode)
    inside = jnp.sum(weighted * rise_now, axis=2)
    carried = jnp.einsum("cbt,cnt->cnb", dual_pieces, fall_next, precision=data_mode)
    return inside + jnp.sum(carried * before, axis=2)


def channel_group(group_items, block_len):
    (
        forward_narrow,
        backward_narrow,
        rate_rows,
        weights,
        gain_rows,
        enter_forward,
        enter_backward,
    ) = group_items
    forward_rows = forward_narrow.astype(jnp.float32)
    backward_rows = backward_narrow.astype(jnp.float32)
    tables = make_tables(rate_rows, block_len)
    carried, before = modal_pass(forward_rows, rate_rows, weights, enter_forward, tables)
    returned, _ = modal_pass(jnp.flip(backward_rows, 1), rate_rows, weights, enter_backward, tables)
    signal = (carried + gain_rows[:, None] * forward_rows).astype(jnp.bfloat16)
    back_signal = (jnp.flip(returned, 1) + gain_rows[:, None] * backward_rows).astype(jnp.bfloat16)
    mode_raw = mode_products(forward_rows, backward_rows, before, tables)
    skip_raw = jnp.sum(backward_rows * forward_rows, axis=1)
    return (signal, back_signal, mode_raw, skip_raw)


def split_pair(values):
    high = values.astype(jnp.bfloat16)
    low = (values - high.astype(jnp.float32)).astype(jnp.bfloat16)
    return high, low


def mat_nn(a, b):
    return jnp.dot(a, b, preferred_element_type=jnp.float32)


def mat_nt(a, b):
    return lax.dot_general(a, b, (((1,), (1,)), ((), ())), preferred_element_type=jnp.float32)


def mat_tn(a, b):
    return lax.dot_general(a, b, (((0,), (0,)), ((), ())), preferred_element_type=jnp.float32)


def wide_nn(a, b_pair):
    a_high, a_low = split_pair(a)
    return mat_nn(a_high, b_pair[0]) + mat_nn(a_high, b_pair[1]) + mat_nn(a_low, b_pair[0])


def shifted(values, by, lanes_rows):
    rows = values.shape[0]
    rolled = pltpu.roll(values, by % rows, 0)
    index = lax.broadcasted_iota(jnp.int32, values.shape, 0)
    keep = (index >= by) if by > 0 else (index < rows + by)
    return jnp.where(keep, rolled, 0.0)


def long_conv_kernel(u_ref, dz_ref, krow_ref, tab_ref, row_ref, z_ref, du_ref, mode_ref, skip_ref):
    chans, blocks, width = u_ref.shape
    modes = tab_ref.shape[2]
    col = lax.broadcasted_iota(jnp.int32, (width, width), 1)
    row = lax.broadcasted_iota(jnp.int32, (width, width), 0)
    upper = col >= row
    lower = col <= row
    lag_ids = lax.broadcasted_iota(jnp.int32, (width, modes), 0).astype(jnp.float32)

    def one_channel(c, carry):
        u_narrow = u_ref[c]
        dz_narrow = dz_ref[c]
        tabs = tab_ref[c]
        rows = row_ref[c]
        krow = krow_ref[c]
        fall_end = (tabs[0], tabs[1])
        fall_start = (tabs[2], tabs[3])
        gain_fwd = (tabs[4], tabs[5])
        gain_bwd = (tabs[6], tabs[7])
        rate_row = rows[6:7, :]
        step_row = rows[5:6, :]
        gain = rows[7:8, 0:1]
        ahead = pltpu.roll(jnp.broadcast_to(krow[0:1, :], (width, width)), 0, 1, stride=1, stride_axis=0)
        ahead = jnp.where(upper, ahead, 0.0)
        behind = pltpu.roll(jnp.broadcast_to(krow[1:2, :], (width, width)), 1, 1, stride=1, stride_axis=0)
        behind = jnp.where(lower, behind, 0.0)
        a_high, a_low = split_pair(ahead)
        b_high, b_low = split_pair(behind)
        z_in = mat_nn(
            jnp.concatenate([u_narrow, u_narrow], axis=1), jnp.concatenate([a_high, a_low], axis=0)
        )
        du_in = mat_nn(
            jnp.concatenate([dz_narrow, dz_narrow], axis=1), jnp.concatenate([b_high, b_low], axis=0)
        )
        ends = mat_nt(u_narrow, fall_end[0]) + mat_nt(u_narrow, fall_end[1])
        starts = mat_nt(dz_narrow, fall_start[0]) + mat_nt(dz_narrow, fall_start[1])
        fwd_state = ends
        bwd_state = starts
        level = 0
        span = 1
        while span < blocks:
            decay = rows[level : level + 1, :]
            fwd_state = fwd_state + decay * shifted(fwd_state, span, blocks)
            bwd_state = bwd_state + decay * shifted(bwd_state, -span, blocks)
            level += 1
            span *= 2
        state_before = shifted(fwd_state, 1, blocks)
        state_after = shifted(bwd_state, -1, blocks)
        z_carry = wide_nn(state_before, gain_fwd)
        du_carry = wide_nn(state_after, gain_bwd)
        u_wide = u_narrow.astype(jnp.float32)
        dz_wide = dz_narrow.astype(jnp.float32)
        z_ref[c] = (z_in + z_carry + gain * u_wide).astype(z_ref.dtype)
        du_ref[c] = (du_in + du_carry + gain * dz_wide).astype(du_ref.dtype)
        rise = jnp.exp(lag_ids * rate_row)
        crossed = mat_tn(u_narrow, dz_narrow)
        crossed = jnp.where(upper, crossed, 0.0)
        c_high, c_low = split_pair(crossed)
        weighted = (
            mat_nt(c_high, fall_start[0]) + mat_nt(c_high, fall_start[1]) + mat_nt(c_low, fall_start[0])
        )
        mode_in = jnp.sum(weighted * rise, axis=0, keepdims=True)
        mode_carry = jnp.sum(state_before * starts, axis=0, keepdims=True) * step_row
        mode_ref[c] = mode_in + mode_carry
        skip_ref[c] = jnp.broadcast_to(jnp.sum(u_wide * dz_wide), skip_ref.shape[1:])
        return carry

    lax.fori_loop(0, chans, one_channel, 0, unroll=8)


def long_conv_tables(rate_rows, weight_rows, gain_rows, width, blocks):
    offsets = jnp.arange(width, dtype=jnp.float32)
    rate = rate_rows[:, :, None]
    weight = weight_rows[:, :, None]
    fall_end = jnp.exp(-rate * (width - 1.0 - offsets))
    fall_start = jnp.exp(-rate * offsets)
    gain_fwd = weight * jnp.exp(-rate * (offsets + 1.0))
    gain_bwd = weight * jnp.exp(-rate * (width - offsets))
    pairs = []
    for table in (fall_end, fall_start, gain_fwd, gain_bwd):
        high = lax.reduce_precision(table, exponent_bits=8, mantissa_bits=7)
        pairs.extend((high.astype(jnp.bfloat16), (table - high).astype(jnp.bfloat16)))
    tabs = jnp.stack(pairs, axis=1)
    levels = []
    span = 1
    while span < blocks:
        levels.append(jnp.exp(-rate_rows * (width * span)))
        span *= 2
    chan_count, modes = rate_rows.shape
    while len(levels) < 5:
        levels.append(jnp.zeros_like(rate_rows))
    levels.append(jnp.exp(-rate_rows))
    levels.append(rate_rows)
    levels.append(jnp.broadcast_to(gain_rows[:, None], (chan_count, modes)))
    lag_kernel = jnp.sum(weight * fall_start, axis=1)
    krow = jnp.stack([lag_kernel, jnp.flip(lag_kernel, axis=1)], axis=1)
    return tabs, jnp.stack(levels, axis=1), krow


def long_conv(u_blocks, dz_blocks, rate_rows, weight_rows, gain_rows, chans_per_step=8):
    chan_count, blocks, width = u_blocks.shape
    modes = rate_rows.shape[1]
    tabs, rows, krow = long_conv_tables(rate_rows, weight_rows, gain_rows, width, blocks)
    step = min(chans_per_step, chan_count)
    data_spec = pl.BlockSpec((step, blocks, width), lambda i: (i, 0, 0))
    return pl.pallas_call(
        long_conv_kernel,
        grid=(chan_count // step,),
        in_specs=[
            data_spec,
            data_spec,
            pl.BlockSpec((step,) + krow.shape[1:], lambda i: (i, 0, 0)),
            pl.BlockSpec((step,) + tabs.shape[1:], lambda i: (i, 0, 0, 0)),
            pl.BlockSpec((step,) + rows.shape[1:], lambda i: (i, 0, 0)),
        ],
        out_specs=[
            data_spec,
            data_spec,
            pl.BlockSpec((step, 1, modes), lambda i: (i, 0, 0)),
            pl.BlockSpec((step, 1, 128), lambda i: (i, 0, 0)),
        ],
        out_shape=[
            jax.ShapeDtypeStruct(u_blocks.shape, jnp.bfloat16),
            jax.ShapeDtypeStruct(u_blocks.shape, jnp.bfloat16),
            jax.ShapeDtypeStruct((chan_count, 1, modes), jnp.float32),
            jax.ShapeDtypeStruct((chan_count, 1, 128), jnp.float32),
        ],
        cost_estimate=pl.CostEstimate(
            flops=chan_count * 34 * width * width * blocks, transcendentals=chan_count * width * modes,
            bytes_accessed=chan_count * blocks * width * 8 + tabs.size * 2,
        ),
    )(u_blocks, dz_blocks, krow, tabs, rows)


def grouped(function, arrays, group_size):
    stacked = tuple(
        (
            item.reshape((item.shape[0] // group_size, group_size) + item.shape[1:])
            for item in arrays
        )
    )
    results = lax.map(function, stacked)
    return tuple(
        (item.reshape((item.shape[0] * item.shape[1],) + item.shape[2:]) for item in results)
    )


def on_device(projected, cotangent, short_filter, residues, decay_rate, skip_gain):
    proj_rows = projected[0]
    token_count = proj_rows.shape[2]
    chans_tp = proj_rows.shape[1]
    rim_width = short_filter.shape[1] - 1
    tp_count = lax.axis_size("tp")
    if tp_count == 2:
        tp_index = lax.axis_index("tp")
        grad_rows = cotangent[0]
        mine = lax.dynamic_slice_in_dim(grad_rows, tp_index * chans_tp, chans_tp, 0)
        other = lax.dynamic_slice_in_dim(grad_rows, (1 - tp_index) * chans_tp, chans_tp, 0)
        theirs = lax.ppermute(other, "tp", [(0, 1), (1, 0)])
        first = jnp.where(tp_index == 0, mine, theirs)
        second = jnp.where(tp_index == 0, theirs, mine)
        grad_out = jnp.concatenate([first, second], axis=1).astype(jnp.float32)
    else:
        grad_out = lax.all_to_all(
            cotangent[0], "tp", split_axis=0, concat_axis=1, tiled=True
        ).astype(jnp.float32)
    prev_rim = from_behind(proj_rows[:, :, token_count - rim_width :], "ctx", 1)
    featured = lax.optimization_barrier(
        causal_short(proj_rows, prev_rim, short_filter).astype(jnp.bfloat16)
    )
    query_feat = featured[0].astype(jnp.float32)
    key_feat = featured[1].astype(jnp.float32)
    value_feat = featured[2].astype(jnp.float32)
    product = (key_feat * value_feat).astype(jnp.bfloat16)
    adjoint = (grad_out * query_feat).astype(jnp.bfloat16)
    ctx_count = lax.axis_size("ctx")
    token_total = token_count * ctx_count * lax.axis_size("dp")
    weight_all = residues * jnp.sqrt(2.0 * decay_rate)
    product_all, adjoint_all = (
        lax.all_to_all(product, "ctx", split_axis=0, concat_axis=1, tiled=True),
        lax.all_to_all(adjoint, "ctx", split_axis=0, concat_axis=1, tiled=True),
    )
    chan_count = chans_tp // ctx_count
    chan_start = lax.axis_index("ctx") * chan_count
    rate_rows = lax.dynamic_slice_in_dim(decay_rate, chan_start, chan_count, 0)
    weight_rows = lax.dynamic_slice_in_dim(weight_all, chan_start, chan_count, 0)
    gain_rows = lax.dynamic_slice_in_dim(skip_gain, chan_start, chan_count, 0)
    length = product_all.shape[1]
    block_len = math.gcd(256, length)
    block_count = length // block_len
    conv_blocks, back_blocks, mode_part, skip_part = long_conv(
        product_all.reshape(chan_count, block_count, block_len),
        adjoint_all.reshape(chan_count, block_count, block_len),
        rate_rows,
        weight_rows,
        gain_rows,
    )
    conv_rows = conv_blocks.reshape(chan_count, length)
    back_rows = back_blocks.reshape(chan_count, length)
    mode_part = mode_part[:, 0, :]
    skip_part = skip_part[:, 0, 0]
    signal, back_signal = (
        lax.all_to_all(conv_rows, "ctx", split_axis=1, concat_axis=0, tiled=True),
        lax.all_to_all(back_rows, "ctx", split_axis=1, concat_axis=0, tiled=True),
    )
    grad_scale = 1.0 / math.sqrt(token_total)
    local_grads = jnp.concatenate(
        [mode_part * jnp.sqrt(2.0 * rate_rows) * grad_scale, skip_part[:, None] * grad_scale], axis=1
    )
    dp_count = lax.axis_size("dp")
    if dp_count & (dp_count - 1) == 0:
        hop = 1
        while hop < dp_count:
            partners = [(i, i ^ hop) for i in range(dp_count)]
            local_grads = local_grads + lax.ppermute(local_grads, "dp", partners)
            hop *= 2
    else:
        local_grads = lax.psum(local_grads, "dp")
    if ctx_count & (ctx_count - 1) == 0:
        ctx_index = lax.axis_index("ctx")
        gathered = local_grads
        hop = 1
        while hop < ctx_count:
            partners = [(i, i ^ hop) for i in range(ctx_count)]
            theirs = lax.ppermute(gathered, "ctx", partners)
            low_side = (ctx_index & hop) == 0
            gathered = jnp.where(
                low_side,
                jnp.concatenate([gathered, theirs], axis=0),
                jnp.concatenate([theirs, gathered], axis=0),
            )
            hop *= 2
    else:
        spread = jnp.broadcast_to(local_grads[None], (ctx_count,) + local_grads.shape)
        gathered = lax.all_to_all(spread, "ctx", split_axis=0, concat_axis=0, tiled=True)
    gathered = gathered.reshape(chans_tp, local_grads.shape[1])
    residue_grad = gathered[:, : mode_part.shape[1]]
    skip_grad = gathered[:, mode_part.shape[1]]
    conv_wide = signal.astype(jnp.float32)
    back_wide = back_signal.astype(jnp.float32)
    hyena_out = (query_feat * conv_wide).astype(jnp.bfloat16)
    feature_grad = jnp.stack(
        [grad_out * conv_wide, back_wide * value_feat, back_wide * key_feat]
    ).astype(jnp.bfloat16)
    next_rim = from_behind(feature_grad[:, :, :rim_width], "ctx", -1)
    input_grad = anticausal_short(feature_grad, next_rim, short_filter).astype(jnp.bfloat16)
    return (hyena_out[None], input_grad[None], residue_grad, skip_grad)


def solution(mesh):
    placed = (
        P("dp", None, "tp", "ctx"),
        P("dp", None, ("ctx", "tp")),
        P(None, None, "tp"),
        P("tp", None),
        P("tp", None),
        P("tp"),
    )
    return jax.shard_map(
        on_device,
        mesh=mesh,
        in_specs=placed,
        out_specs=(P("dp", "tp", "ctx"), P("dp", None, "tp", "ctx"), P("tp", None), P("tp")),
        check_vma=False,
    )
```

```python
from functools import partial
import math

import jax
import jax.numpy as jnp
from jax import lax
from jax.sharding import PartitionSpec as P
from jax.experimental import pallas as pl
from jax.experimental.pallas import tpu as pltpu

exact_mode = lax.Precision.HIGHEST
data_mode = lax.Precision.HIGH


def from_behind(shard, axis, by):
    count = lax.axis_size(axis)
    pairs = [(i, i + by) for i in range(count) if 0 <= i + by < count]
    return lax.ppermute(shard, axis, pairs)


def causal_short(proj_rows, prev_rim, tap_weights):
    rim_width = prev_rim.shape[2]
    token_count = proj_rows.shape[2]
    extended = jnp.concatenate([prev_rim, proj_rows], axis=2).astype(jnp.float32)
    result = tap_weights[:, 0, :, None] * extended[:, :, rim_width : rim_width + token_count]
    for lag_index in range(1, rim_width + 1):
        start_at = rim_width - lag_index
        result = (
            result
            + tap_weights[:, lag_index, :, None] * extended[:, :, start_at : start_at + token_count]
        )
    return result


def anticausal_short(grad_rows, next_rim, tap_weights):
    rim_width = next_rim.shape[2]
    token_count = grad_rows.shape[2]
    extended = jnp.concatenate([grad_rows, next_rim], axis=2).astype(jnp.float32)
    result = tap_weights[:, 0, :, None] * extended[:, :, :token_count]
    for lag_index in range(1, rim_width + 1):
        result = (
            result
            + tap_weights[:, lag_index, :, None]
            * extended[:, :, lag_index : lag_index + token_count]
        )
    return result


def make_tables(rate_rows, block_len):
    offsets = jnp.arange(block_len, dtype=jnp.float32)
    fall_now = jnp.exp(-rate_rows[:, :, None] * offsets)
    rise_now = jnp.exp(rate_rows[:, :, None] * offsets)
    fall_next = jnp.exp(-rate_rows[:, :, None] * (offsets + 1.0))
    fall_tail = jnp.exp(-rate_rows[:, :, None] * (block_len - 1.0 - offsets))
    lower_mask = offsets[:, None] >= offsets[None, :]
    return (fall_now, rise_now, fall_next, fall_tail, lower_mask)


def chain_link(earlier, later):
    return (earlier[0] * later[0], later[0] * earlier[1] + later[1])


def modal_pass(signal, rate_rows, weights, incoming, tables):
    fall_now, rise_now, fall_next, fall_tail, lower_mask = tables
    block_len = fall_now.shape[2]
    chan_count, length = signal.shape
    block_count = length // block_len
    pieces = signal.reshape(chan_count, block_count, block_len)
    kernel = jnp.einsum(
        "cnt,cns->cts", weights[:, :, None] * fall_now, rise_now, precision=exact_mode
    )
    kernel = jnp.where(lower_mask[None], kernel, 0.0)
    inside = jnp.einsum("cts,cbs->cbt", kernel, pieces, precision=data_mode)
    block_ends = jnp.einsum("cns,cbs->cnb", fall_tail, pieces, precision=data_mode)
    span_decay = jnp.exp(-rate_rows * block_len)
    block_mults = jnp.broadcast_to(span_decay[:, :, None], block_ends.shape)
    _, running = lax.associative_scan(chain_link, (block_mults, block_ends), axis=2)
    block_steps = jnp.arange(block_count, dtype=jnp.float32)
    before = jnp.concatenate([jnp.zeros_like(running[:, :, :1]), running[:, :, :-1]], axis=2)
    before = (
        before + jnp.exp(-rate_rows[:, :, None] * block_len * block_steps) * incoming[:, :, None]
    )
    carry_in = jnp.einsum(
        "cnt,cnb->cbt", weights[:, :, None] * fall_next, before, precision=exact_mode
    )
    return ((inside + carry_in).reshape(chan_count, length), before)


def mode_products(signal, adjoint, before, tables):
    fall_now, rise_now, fall_next, fall_tail, lower_mask = tables
    block_len = fall_now.shape[2]
    chan_count, length = signal.shape
    block_count = length // block_len
    pieces = signal.reshape(chan_count, block_count, block_len)
    dual_pieces = adjoint.reshape(chan_count, block_count, block_len)
    crossed = jnp.einsum("cbt,cbs->cts", dual_pieces, pieces, precision=data_mode)
    crossed = jnp.where(lower_mask[None], crossed, 0.0)
    weighted = jnp.einsum("cts,cnt->cns", crossed, fall_now, precision=exact_mode)
    inside = jnp.sum(weighted * rise_now, axis=2)
    carried = jnp.einsum("cbt,cnt->cnb", dual_pieces, fall_next, precision=data_mode)
    return inside + jnp.sum(carried * before, axis=2)


def channel_group(group_items, block_len):
    (
        forward_narrow,
        backward_narrow,
        rate_rows,
        weights,
        gain_rows,
        enter_forward,
        enter_backward,
    ) = group_items
    forward_rows = forward_narrow.astype(jnp.float32)
    backward_rows = backward_narrow.astype(jnp.float32)
    tables = make_tables(rate_rows, block_len)
    carried, before = modal_pass(forward_rows, rate_rows, weights, enter_forward, tables)
    returned, _ = modal_pass(jnp.flip(backward_rows, 1), rate_rows, weights, enter_backward, tables)
    signal = (carried + gain_rows[:, None] * forward_rows).astype(jnp.bfloat16)
    back_signal = (jnp.flip(returned, 1) + gain_rows[:, None] * backward_rows).astype(jnp.bfloat16)
    mode_raw = mode_products(forward_rows, backward_rows, before, tables)
    skip_raw = jnp.sum(backward_rows * forward_rows, axis=1)
    return (signal, back_signal, mode_raw, skip_raw)


def split_pair(values):
    high = values.astype(jnp.bfloat16)
    low = (values - high.astype(jnp.float32)).astype(jnp.bfloat16)
    return high, low


def mat_nn(a, b):
    return jnp.dot(a, b, preferred_element_type=jnp.float32)


def mat_nt(a, b):
    return lax.dot_general(a, b, (((1,), (1,)), ((), ())), preferred_element_type=jnp.float32)


def mat_tn(a, b):
    return lax.dot_general(a, b, (((0,), (0,)), ((), ())), preferred_element_type=jnp.float32)


def wide_nn(a, b_pair):
    a_high, a_low = split_pair(a)
    return mat_nn(a_high, b_pair[0]) + mat_nn(a_high, b_pair[1]) + mat_nn(a_low, b_pair[0])


def shifted(values, by, lanes_rows):
    rows = values.shape[0]
    rolled = pltpu.roll(values, by % rows, 0)
    index = lax.broadcasted_iota(jnp.int32, values.shape, 0)
    keep = (index >= by) if by > 0 else (index < rows + by)
    return jnp.where(keep, rolled, 0.0)


def long_conv_kernel(u_ref, dz_ref, krow_ref, tab_ref, row_ref, z_ref, du_ref, mode_ref, skip_ref):
    chans, blocks, width = u_ref.shape
    modes = tab_ref.shape[2]
    col = lax.broadcasted_iota(jnp.int32, (width, width), 1)
    row = lax.broadcasted_iota(jnp.int32, (width, width), 0)
    upper = col >= row
    lower = col <= row
    lag_ids = lax.broadcasted_iota(jnp.int32, (width, modes), 0).astype(jnp.float32)

    def one_channel(c, carry):
        u_narrow = u_ref[c]
        dz_narrow = dz_ref[c]
        tabs = tab_ref[c]
        rows = row_ref[c]
        krow = krow_ref[c]
        fall_end = (tabs[0], tabs[1])
        fall_start = (tabs[2], tabs[3])
        gain_fwd = (tabs[4], tabs[5])
        gain_bwd = (tabs[6], tabs[7])
        rate_row = rows[6:7, :]
        step_row = rows[5:6, :]
        gain = rows[7:8, 0:1]
        ahead = pltpu.roll(jnp.broadcast_to(krow[0:1, :], (width, width)), 0, 1, stride=1, stride_axis=0)
        ahead = jnp.where(upper, ahead, 0.0)
        behind = pltpu.roll(jnp.broadcast_to(krow[1:2, :], (width, width)), 1, 1, stride=1, stride_axis=0)
        behind = jnp.where(lower, behind, 0.0)
        a_high, a_low = split_pair(ahead)
        b_high, b_low = split_pair(behind)
        z_in = mat_nn(
            jnp.concatenate([u_narrow, u_narrow], axis=1), jnp.concatenate([a_high, a_low], axis=0)
        )
        du_in = mat_nn(
            jnp.concatenate([dz_narrow, dz_narrow], axis=1), jnp.concatenate([b_high, b_low], axis=0)
        )
        ends = mat_nt(u_narrow, fall_end[0]) + mat_nt(u_narrow, fall_end[1])
        starts = mat_nt(dz_narrow, fall_start[0]) + mat_nt(dz_narrow, fall_start[1])
        fwd_state = ends
        bwd_state = starts
        level = 0
        span = 1
        while span < blocks:
            decay = rows[level : level + 1, :]
            fwd_state = fwd_state + decay * shifted(fwd_state, span, blocks)
            bwd_state = bwd_state + decay * shifted(bwd_state, -span, blocks)
            level += 1
            span *= 2
        state_before = shifted(fwd_state, 1, blocks)
        state_after = shifted(bwd_state, -1, blocks)
        z_carry = wide_nn(state_before, gain_fwd)
        du_carry = wide_nn(state_after, gain_bwd)
        u_wide = u_narrow.astype(jnp.float32)
        dz_wide = dz_narrow.astype(jnp.float32)
        z_ref[c] = (z_in + z_carry + gain * u_wide).astype(z_ref.dtype)
        du_ref[c] = (du_in + du_carry + gain * dz_wide).astype(du_ref.dtype)
        rise = jnp.exp(lag_ids * rate_row)
        crossed = mat_tn(u_narrow, dz_narrow)
        crossed = jnp.where(upper, crossed, 0.0)
        c_high, c_low = split_pair(crossed)
        weighted = (
            mat_nt(c_high, fall_start[0]) + mat_nt(c_high, fall_start[1]) + mat_nt(c_low, fall_start[0])
        )
        mode_in = jnp.sum(weighted * rise, axis=0, keepdims=True)
        mode_carry = jnp.sum(state_before * starts, axis=0, keepdims=True) * step_row
        mode_ref[c] = mode_in + mode_carry
        skip_ref[c] = jnp.broadcast_to(jnp.sum(u_wide * dz_wide), skip_ref.shape[1:])
        return carry

    lax.fori_loop(0, chans, one_channel, 0, unroll=8)


def long_conv_tables(rate_rows, weight_rows, gain_rows, width, blocks):
    offsets = jnp.arange(width, dtype=jnp.float32)
    rate = rate_rows[:, :, None]
    weight = weight_rows[:, :, None]
    fall_end = jnp.exp(-rate * (width - 1.0 - offsets))
    fall_start = jnp.exp(-rate * offsets)
    gain_fwd = weight * jnp.exp(-rate * (offsets + 1.0))
    gain_bwd = weight * jnp.exp(-rate * (width - offsets))
    pairs = []
    for table in (fall_end, fall_start, gain_fwd, gain_bwd):
        high = lax.reduce_precision(table, exponent_bits=8, mantissa_bits=7)
        pairs.extend((high.astype(jnp.bfloat16), (table - high).astype(jnp.bfloat16)))
    tabs = jnp.stack(pairs, axis=1)
    levels = []
    span = 1
    while span < blocks:
        levels.append(jnp.exp(-rate_rows * (width * span)))
        span *= 2
    chan_count, modes = rate_rows.shape
    while len(levels) < 5:
        levels.append(jnp.zeros_like(rate_rows))
    levels.append(jnp.exp(-rate_rows))
    levels.append(rate_rows)
    levels.append(jnp.broadcast_to(gain_rows[:, None], (chan_count, modes)))
    lag_kernel = jnp.sum(weight * fall_start, axis=1)
    krow = jnp.stack([lag_kernel, jnp.flip(lag_kernel, axis=1)], axis=1)
    return tabs, jnp.stack(levels, axis=1), krow


def long_conv(u_blocks, dz_blocks, rate_rows, weight_rows, gain_rows, chans_per_step=8):
    chan_count, blocks, width = u_blocks.shape
    modes = rate_rows.shape[1]
    tabs, rows, krow = long_conv_tables(rate_rows, weight_rows, gain_rows, width, blocks)
    step = min(chans_per_step, chan_count)
    data_spec = pl.BlockSpec((step, blocks, width), lambda i: (i, 0, 0))
    return pl.pallas_call(
        long_conv_kernel,
        grid=(chan_count // step,),
        in_specs=[
            data_spec,
            data_spec,
            pl.BlockSpec((step,) + krow.shape[1:], lambda i: (i, 0, 0)),
            pl.BlockSpec((step,) + tabs.shape[1:], lambda i: (i, 0, 0, 0)),
            pl.BlockSpec((step,) + rows.shape[1:], lambda i: (i, 0, 0)),
        ],
        out_specs=[
            data_spec,
            data_spec,
            pl.BlockSpec((step, 1, modes), lambda i: (i, 0, 0)),
            pl.BlockSpec((step, 1, 128), lambda i: (i, 0, 0)),
        ],
        out_shape=[
            jax.ShapeDtypeStruct(u_blocks.shape, jnp.bfloat16),
            jax.ShapeDtypeStruct(u_blocks.shape, jnp.bfloat16),
            jax.ShapeDtypeStruct((chan_count, 1, modes), jnp.float32),
            jax.ShapeDtypeStruct((chan_count, 1, 128), jnp.float32),
        ],
        cost_estimate=pl.CostEstimate(
            flops=chan_count * 34 * width * width * blocks, transcendentals=chan_count * width * modes,
            bytes_accessed=chan_count * blocks * width * 8 + tabs.size * 2,
        ),
    )(u_blocks, dz_blocks, krow, tabs, rows)


def grouped(function, arrays, group_size):
    stacked = tuple(
        (
            item.reshape((item.shape[0] // group_size, group_size) + item.shape[1:])
            for item in arrays
        )
    )
    results = lax.map(function, stacked)
    return tuple(
        (item.reshape((item.shape[0] * item.shape[1],) + item.shape[2:]) for item in results)
    )


def on_device(projected, cotangent, short_filter, residues, decay_rate, skip_gain):
    proj_rows = projected[0]
    token_count = proj_rows.shape[2]
    chans_tp = proj_rows.shape[1]
    rim_width = short_filter.shape[1] - 1
    tp_count = lax.axis_size("tp")
    if tp_count == 2:
        tp_index = lax.axis_index("tp")
        grad_rows = cotangent[0]
        mine = lax.dynamic_slice_in_dim(grad_rows, tp_index * chans_tp, chans_tp, 0)
        other = lax.dynamic_slice_in_dim(grad_rows, (1 - tp_index) * chans_tp, chans_tp, 0)
        theirs = lax.ppermute(other, "tp", [(0, 1), (1, 0)])
        first = jnp.where(tp_index == 0, mine, theirs)
        second = jnp.where(tp_index == 0, theirs, mine)
        grad_out = jnp.concatenate([first, second], axis=1).astype(jnp.float32)
    else:
        grad_out = lax.all_to_all(
            cotangent[0], "tp", split_axis=0, concat_axis=1, tiled=True
        ).astype(jnp.float32)
    prev_rim = from_behind(proj_rows[:, :, token_count - rim_width :], "ctx", 1)
    featured = lax.optimization_barrier(
        causal_short(proj_rows, prev_rim, short_filter).astype(jnp.bfloat16)
    )
    query_feat = featured[0].astype(jnp.float32)
    key_feat = featured[1].astype(jnp.float32)
    value_feat = featured[2].astype(jnp.float32)
    product = (key_feat * value_feat).astype(jnp.bfloat16)
    adjoint = (grad_out * query_feat).astype(jnp.bfloat16)
    ctx_count = lax.axis_size("ctx")
    token_total = token_count * ctx_count * lax.axis_size("dp")
    weight_all = residues * jnp.sqrt(2.0 * decay_rate)
    product_all, adjoint_all = (
        lax.all_to_all(product, "ctx", split_axis=0, concat_axis=1, tiled=True),
        lax.all_to_all(adjoint, "ctx", split_axis=0, concat_axis=1, tiled=True),
    )
    chan_count = chans_tp // ctx_count
    chan_start = lax.axis_index("ctx") * chan_count
    rate_rows = lax.dynamic_slice_in_dim(decay_rate, chan_start, chan_count, 0)
    weight_rows = lax.dynamic_slice_in_dim(weight_all, chan_start, chan_count, 0)
    gain_rows = lax.dynamic_slice_in_dim(skip_gain, chan_start, chan_count, 0)
    length = product_all.shape[1]
    block_len = math.gcd(256, length)
    block_count = length // block_len
    conv_blocks, back_blocks, mode_part, skip_part = long_conv(
        product_all.reshape(chan_count, block_count, block_len),
        adjoint_all.reshape(chan_count, block_count, block_len),
        rate_rows,
        weight_rows,
        gain_rows,
    )
    conv_rows = conv_blocks.reshape(chan_count, length)
    back_rows = back_blocks.reshape(chan_count, length)
    mode_part = mode_part[:, 0, :]
    skip_part = skip_part[:, 0, 0]
    signal = lax.all_to_all(conv_rows, "ctx", split_axis=1, concat_axis=0, tiled=True)
    grad_scale = 1.0 / math.sqrt(token_total)
    local_grads = jnp.concatenate(
        [mode_part * jnp.sqrt(2.0 * rate_rows) * grad_scale, skip_part[:, None] * grad_scale], axis=1
    )
    dp_count = lax.axis_size("dp")
    if dp_count & (dp_count - 1) == 0:
        hop = 1
        while hop < dp_count:
            partners = [(i, i ^ hop) for i in range(dp_count)]
            local_grads = local_grads + lax.ppermute(local_grads, "dp", partners)
            hop *= 2
    else:
        local_grads = lax.psum(local_grads, "dp")
    if ctx_count & (ctx_count - 1) == 0:
        ctx_index = lax.axis_index("ctx")
        gathered = local_grads
        hop = 1
        while hop < ctx_count:
            partners = [(i, i ^ hop) for i in range(ctx_count)]
            theirs = lax.ppermute(gathered, "ctx", partners)
            low_side = (ctx_index & hop) == 0
            gathered = jnp.where(
                low_side,
                jnp.concatenate([gathered, theirs], axis=0),
                jnp.concatenate([theirs, gathered], axis=0),
            )
            hop *= 2
    else:
        spread = jnp.broadcast_to(local_grads[None], (ctx_count,) + local_grads.shape)
        gathered = lax.all_to_all(spread, "ctx", split_axis=0, concat_axis=0, tiled=True)
    back_rows, gathered = lax.optimization_barrier((back_rows, gathered))
    back_signal = lax.all_to_all(back_rows, "ctx", split_axis=1, concat_axis=0, tiled=True)
    gathered = gathered.reshape(chans_tp, local_grads.shape[1])
    residue_grad = gathered[:, : mode_part.shape[1]]
    skip_grad = gathered[:, mode_part.shape[1]]
    conv_wide = signal.astype(jnp.float32)
    hyena_out = (query_feat * conv_wide).astype(jnp.bfloat16)
    query_grad = (grad_out * conv_wide).astype(jnp.bfloat16)[None]
    query_rim = from_behind(query_grad[:, :, :rim_width], "ctx", -1)
    query_input = anticausal_short(query_grad, query_rim, short_filter[0:1]).astype(jnp.bfloat16)
    back_wide = back_signal.astype(jnp.float32)
    feature_grad = jnp.stack([back_wide * value_feat, back_wide * key_feat]).astype(jnp.bfloat16)
    next_rim = from_behind(feature_grad[:, :, :rim_width], "ctx", -1)
    input_grad = anticausal_short(feature_grad, next_rim, short_filter[1:]).astype(jnp.bfloat16)
    input_grad = jnp.concatenate([query_input, input_grad], axis=0)
    return (hyena_out[None], input_grad[None], residue_grad, skip_grad)


def solution(mesh):
    placed = (
        P("dp", None, "tp", "ctx"),
        P("dp", None, ("ctx", "tp")),
        P(None, None, "tp"),
        P("tp", None),
        P("tp", None),
        P("tp"),
    )
    return jax.shard_map(
        on_device,
        mesh=mesh,
        in_specs=placed,
        out_specs=(P("dp", "tp", "ctx"), P("dp", None, "tp", "ctx"), P("tp", None), P("tp")),
        check_vma=False,
    )
```

```python
from functools import partial
import math

import jax
import jax.numpy as jnp
from jax import lax
from jax.sharding import PartitionSpec as P
from jax.experimental import pallas as pl
from jax.experimental.pallas import tpu as pltpu

exact_mode = lax.Precision.HIGHEST
data_mode = lax.Precision.HIGH


def from_behind(shard, axis, by):
    count = lax.axis_size(axis)
    pairs = [(i, i + by) for i in range(count) if 0 <= i + by < count]
    return lax.ppermute(shard, axis, pairs)


def causal_short(proj_rows, prev_rim, tap_weights):
    rim_width = prev_rim.shape[2]
    token_count = proj_rows.shape[2]
    extended = jnp.concatenate([prev_rim, proj_rows], axis=2).astype(jnp.float32)
    result = tap_weights[:, 0, :, None] * extended[:, :, rim_width : rim_width + token_count]
    for lag_index in range(1, rim_width + 1):
        start_at = rim_width - lag_index
        result = (
            result
            + tap_weights[:, lag_index, :, None] * extended[:, :, start_at : start_at + token_count]
        )
    return result


def anticausal_short(grad_rows, next_rim, tap_weights):
    rim_width = next_rim.shape[2]
    token_count = grad_rows.shape[2]
    extended = jnp.concatenate([grad_rows, next_rim], axis=2).astype(jnp.float32)
    result = tap_weights[:, 0, :, None] * extended[:, :, :token_count]
    for lag_index in range(1, rim_width + 1):
        result = (
            result
            + tap_weights[:, lag_index, :, None]
            * extended[:, :, lag_index : lag_index + token_count]
        )
    return result


def make_tables(rate_rows, block_len):
    offsets = jnp.arange(block_len, dtype=jnp.float32)
    fall_now = jnp.exp(-rate_rows[:, :, None] * offsets)
    rise_now = jnp.exp(rate_rows[:, :, None] * offsets)
    fall_next = jnp.exp(-rate_rows[:, :, None] * (offsets + 1.0))
    fall_tail = jnp.exp(-rate_rows[:, :, None] * (block_len - 1.0 - offsets))
    lower_mask = offsets[:, None] >= offsets[None, :]
    return (fall_now, rise_now, fall_next, fall_tail, lower_mask)


def chain_link(earlier, later):
    return (earlier[0] * later[0], later[0] * earlier[1] + later[1])


def modal_pass(signal, rate_rows, weights, incoming, tables):
    fall_now, rise_now, fall_next, fall_tail, lower_mask = tables
    block_len = fall_now.shape[2]
    chan_count, length = signal.shape
    block_count = length // block_len
    pieces = signal.reshape(chan_count, block_count, block_len)
    kernel = jnp.einsum(
        "cnt,cns->cts", weights[:, :, None] * fall_now, rise_now, precision=exact_mode
    )
    kernel = jnp.where(lower_mask[None], kernel, 0.0)
    inside = jnp.einsum("cts,cbs->cbt", kernel, pieces, precision=data_mode)
    block_ends = jnp.einsum("cns,cbs->cnb", fall_tail, pieces, precision=data_mode)
    span_decay = jnp.exp(-rate_rows * block_len)
    block_mults = jnp.broadcast_to(span_decay[:, :, None], block_ends.shape)
    _, running = lax.associative_scan(chain_link, (block_mults, block_ends), axis=2)
    block_steps = jnp.arange(block_count, dtype=jnp.float32)
    before = jnp.concatenate([jnp.zeros_like(running[:, :, :1]), running[:, :, :-1]], axis=2)
    before = (
        before + jnp.exp(-rate_rows[:, :, None] * block_len * block_steps) * incoming[:, :, None]
    )
    carry_in = jnp.einsum(
        "cnt,cnb->cbt", weights[:, :, None] * fall_next, before, precision=exact_mode
    )
    return ((inside + carry_in).reshape(chan_count, length), before)


def mode_products(signal, adjoint, before, tables):
    fall_now, rise_now, fall_next, fall_tail, lower_mask = tables
    block_len = fall_now.shape[2]
    chan_count, length = signal.shape
    block_count = length // block_len
    pieces = signal.reshape(chan_count, block_count, block_len)
    dual_pieces = adjoint.reshape(chan_count, block_count, block_len)
    crossed = jnp.einsum("cbt,cbs->cts", dual_pieces, pieces, precision=data_mode)
    crossed = jnp.where(lower_mask[None], crossed, 0.0)
    weighted = jnp.einsum("cts,cnt->cns", crossed, fall_now, precision=exact_mode)
    inside = jnp.sum(weighted * rise_now, axis=2)
    carried = jnp.einsum("cbt,cnt->cnb", dual_pieces, fall_next, precision=data_mode)
    return inside + jnp.sum(carried * before, axis=2)


def channel_group(group_items, block_len):
    (
        forward_narrow,
        backward_narrow,
        rate_rows,
        weights,
        gain_rows,
        enter_forward,
        enter_backward,
    ) = group_items
    forward_rows = forward_narrow.astype(jnp.float32)
    backward_rows = backward_narrow.astype(jnp.float32)
    tables = make_tables(rate_rows, block_len)
    carried, before = modal_pass(forward_rows, rate_rows, weights, enter_forward, tables)
    returned, _ = modal_pass(jnp.flip(backward_rows, 1), rate_rows, weights, enter_backward, tables)
    signal = (carried + gain_rows[:, None] * forward_rows).astype(jnp.bfloat16)
    back_signal = (jnp.flip(returned, 1) + gain_rows[:, None] * backward_rows).astype(jnp.bfloat16)
    mode_raw = mode_products(forward_rows, backward_rows, before, tables)
    skip_raw = jnp.sum(backward_rows * forward_rows, axis=1)
    return (signal, back_signal, mode_raw, skip_raw)


def split_pair(values):
    high = values.astype(jnp.bfloat16)
    low = (values - high.astype(jnp.float32)).astype(jnp.bfloat16)
    return high, low


def mat_nn(a, b):
    return jnp.dot(a, b, preferred_element_type=jnp.float32)


def mat_nt(a, b):
    return lax.dot_general(a, b, (((1,), (1,)), ((), ())), preferred_element_type=jnp.float32)


def mat_tn(a, b):
    return lax.dot_general(a, b, (((0,), (0,)), ((), ())), preferred_element_type=jnp.float32)


def wide_nn(a, b_pair):
    a_high, a_low = split_pair(a)
    return mat_nn(a_high, b_pair[0]) + mat_nn(a_high, b_pair[1]) + mat_nn(a_low, b_pair[0])


def shifted(values, by, lanes_rows):
    rows = values.shape[0]
    rolled = pltpu.roll(values, by % rows, 0)
    index = lax.broadcasted_iota(jnp.int32, values.shape, 0)
    keep = (index >= by) if by > 0 else (index < rows + by)
    return jnp.where(keep, rolled, 0.0)


def long_conv_kernel(u_ref, dz_ref, krow_ref, tab_ref, row_ref, z_ref, du_ref, mode_ref, skip_ref):
    chans, blocks, width = u_ref.shape
    modes = tab_ref.shape[2]
    col = lax.broadcasted_iota(jnp.int32, (width, width), 1)
    row = lax.broadcasted_iota(jnp.int32, (width, width), 0)
    upper = col >= row
    lower = col <= row
    lag_ids = lax.broadcasted_iota(jnp.int32, (width, modes), 0).astype(jnp.float32)

    def one_channel(c, carry):
        u_narrow = u_ref[c]
        dz_narrow = dz_ref[c]
        tabs = tab_ref[c]
        rows = row_ref[c]
        krow = krow_ref[c]
        fall_end = (tabs[0], tabs[1])
        fall_start = (tabs[2], tabs[3])
        gain_fwd = (tabs[4], tabs[5])
        gain_bwd = (tabs[6], tabs[7])
        rate_row = rows[6:7, :]
        step_row = rows[5:6, :]
        gain = rows[7:8, 0:1]
        ahead = pltpu.roll(jnp.broadcast_to(krow[0:1, :], (width, width)), 0, 1, stride=1, stride_axis=0)
        ahead = jnp.where(upper, ahead, 0.0)
        behind = pltpu.roll(jnp.broadcast_to(krow[1:2, :], (width, width)), 1, 1, stride=1, stride_axis=0)
        behind = jnp.where(lower, behind, 0.0)
        a_high, a_low = split_pair(ahead)
        b_high, b_low = split_pair(behind)
        z_in = mat_nn(
            jnp.concatenate([u_narrow, u_narrow], axis=1), jnp.concatenate([a_high, a_low], axis=0)
        )
        du_in = mat_nn(
            jnp.concatenate([dz_narrow, dz_narrow], axis=1), jnp.concatenate([b_high, b_low], axis=0)
        )
        ends = mat_nt(u_narrow, fall_end[0]) + mat_nt(u_narrow, fall_end[1])
        starts = mat_nt(dz_narrow, fall_start[0]) + mat_nt(dz_narrow, fall_start[1])
        fwd_state = ends
        bwd_state = starts
        level = 0
        span = 1
        while span < blocks:
            decay = rows[level : level + 1, :]
            fwd_state = fwd_state + decay * shifted(fwd_state, span, blocks)
            bwd_state = bwd_state + decay * shifted(bwd_state, -span, blocks)
            level += 1
            span *= 2
        state_before = shifted(fwd_state, 1, blocks)
        state_after = shifted(bwd_state, -1, blocks)
        z_carry = wide_nn(state_before, gain_fwd)
        du_carry = wide_nn(state_after, gain_bwd)
        u_wide = u_narrow.astype(jnp.float32)
        dz_wide = dz_narrow.astype(jnp.float32)
        z_ref[c] = (z_in + z_carry + gain * u_wide).astype(z_ref.dtype)
        du_ref[c] = (du_in + du_carry + gain * dz_wide).astype(du_ref.dtype)
        rise = jnp.exp(lag_ids * rate_row)
        crossed = mat_tn(u_narrow, dz_narrow)
        crossed = jnp.where(upper, crossed, 0.0)
        c_high, c_low = split_pair(crossed)
        weighted = (
            mat_nt(c_high, fall_start[0]) + mat_nt(c_high, fall_start[1]) + mat_nt(c_low, fall_start[0])
        )
        mode_in = jnp.sum(weighted * rise, axis=0, keepdims=True)
        mode_carry = jnp.sum(state_before * starts, axis=0, keepdims=True) * step_row
        mode_ref[c] = mode_in + mode_carry
        skip_ref[c] = jnp.broadcast_to(jnp.sum(u_wide * dz_wide), skip_ref.shape[1:])
        return carry

    lax.fori_loop(0, chans, one_channel, 0, unroll=8)


def long_conv_tables(rate_rows, weight_rows, gain_rows, width, blocks):
    offsets = jnp.arange(width, dtype=jnp.float32)
    rate = rate_rows[:, :, None]
    weight = weight_rows[:, :, None]
    fall_end = jnp.exp(-rate * (width - 1.0 - offsets))
    fall_start = jnp.exp(-rate * offsets)
    gain_fwd = weight * jnp.exp(-rate * (offsets + 1.0))
    gain_bwd = weight * jnp.exp(-rate * (width - offsets))
    pairs = []
    for table in (fall_end, fall_start, gain_fwd, gain_bwd):
        high = lax.reduce_precision(table, exponent_bits=8, mantissa_bits=7)
        pairs.extend((high.astype(jnp.bfloat16), (table - high).astype(jnp.bfloat16)))
    tabs = jnp.stack(pairs, axis=1)
    levels = []
    span = 1
    while span < blocks:
        levels.append(jnp.exp(-rate_rows * (width * span)))
        span *= 2
    chan_count, modes = rate_rows.shape
    while len(levels) < 5:
        levels.append(jnp.zeros_like(rate_rows))
    levels.append(jnp.exp(-rate_rows))
    levels.append(rate_rows)
    levels.append(jnp.broadcast_to(gain_rows[:, None], (chan_count, modes)))
    lag_kernel = jnp.sum(weight * fall_start, axis=1)
    krow = jnp.stack([lag_kernel, jnp.flip(lag_kernel, axis=1)], axis=1)
    return tabs, jnp.stack(levels, axis=1), krow


def long_conv(u_blocks, dz_blocks, rate_rows, weight_rows, gain_rows, chans_per_step=8):
    chan_count, blocks, width = u_blocks.shape
    modes = rate_rows.shape[1]
    tabs, rows, krow = long_conv_tables(rate_rows, weight_rows, gain_rows, width, blocks)
    step = min(chans_per_step, chan_count)
    data_spec = pl.BlockSpec((step, blocks, width), lambda i: (i, 0, 0))
    return pl.pallas_call(
        long_conv_kernel,
        grid=(chan_count // step,),
        in_specs=[
            data_spec,
            data_spec,
            pl.BlockSpec((step,) + krow.shape[1:], lambda i: (i, 0, 0)),
            pl.BlockSpec((step,) + tabs.shape[1:], lambda i: (i, 0, 0, 0)),
            pl.BlockSpec((step,) + rows.shape[1:], lambda i: (i, 0, 0)),
        ],
        out_specs=[
            data_spec,
            data_spec,
            pl.BlockSpec((step, 1, modes), lambda i: (i, 0, 0)),
            pl.BlockSpec((step, 1, 128), lambda i: (i, 0, 0)),
        ],
        out_shape=[
            jax.ShapeDtypeStruct(u_blocks.shape, jnp.bfloat16),
            jax.ShapeDtypeStruct(u_blocks.shape, jnp.bfloat16),
            jax.ShapeDtypeStruct((chan_count, 1, modes), jnp.float32),
            jax.ShapeDtypeStruct((chan_count, 1, 128), jnp.float32),
        ],
        cost_estimate=pl.CostEstimate(
            flops=chan_count * 34 * width * width * blocks, transcendentals=chan_count * width * modes,
            bytes_accessed=chan_count * blocks * width * 8 + tabs.size * 2,
        ),
    )(u_blocks, dz_blocks, krow, tabs, rows)


def grouped(function, arrays, group_size):
    stacked = tuple(
        (
            item.reshape((item.shape[0] // group_size, group_size) + item.shape[1:])
            for item in arrays
        )
    )
    results = lax.map(function, stacked)
    return tuple(
        (item.reshape((item.shape[0] * item.shape[1],) + item.shape[2:]) for item in results)
    )


def on_device(projected, cotangent, short_filter, residues, decay_rate, skip_gain):
    proj_rows = projected[0]
    token_count = proj_rows.shape[2]
    chans_tp = proj_rows.shape[1]
    rim_width = short_filter.shape[1] - 1
    tp_count = lax.axis_size("tp")
    if tp_count == 2:
        tp_index = lax.axis_index("tp")
        grad_rows = cotangent[0]
        mine = lax.dynamic_slice_in_dim(grad_rows, tp_index * chans_tp, chans_tp, 0)
        other = lax.dynamic_slice_in_dim(grad_rows, (1 - tp_index) * chans_tp, chans_tp, 0)
        theirs = lax.ppermute(other, "tp", [(0, 1), (1, 0)])
        first = jnp.where(tp_index == 0, mine, theirs)
        second = jnp.where(tp_index == 0, theirs, mine)
        grad_out = jnp.concatenate([first, second], axis=1).astype(jnp.float32)
    else:
        grad_out = lax.all_to_all(
            cotangent[0], "tp", split_axis=0, concat_axis=1, tiled=True
        ).astype(jnp.float32)
    prev_rim = from_behind(proj_rows[:, :, token_count - rim_width :], "ctx", 1)
    featured = lax.optimization_barrier(
        causal_short(proj_rows, prev_rim, short_filter).astype(jnp.bfloat16)
    )
    query_feat = featured[0].astype(jnp.float32)
    key_feat = featured[1].astype(jnp.float32)
    value_feat = featured[2].astype(jnp.float32)
    product = (key_feat * value_feat).astype(jnp.bfloat16)
    adjoint = (grad_out * query_feat).astype(jnp.bfloat16)
    ctx_count = lax.axis_size("ctx")
    token_total = token_count * ctx_count * lax.axis_size("dp")
    weight_all = residues * jnp.sqrt(2.0 * decay_rate)
    product_all, adjoint_all = (
        lax.all_to_all(product, "ctx", split_axis=0, concat_axis=1, tiled=True),
        lax.all_to_all(adjoint, "ctx", split_axis=0, concat_axis=1, tiled=True),
    )
    chan_count = chans_tp // ctx_count
    chan_start = lax.axis_index("ctx") * chan_count
    rate_rows = lax.dynamic_slice_in_dim(decay_rate, chan_start, chan_count, 0)
    weight_rows = lax.dynamic_slice_in_dim(weight_all, chan_start, chan_count, 0)
    gain_rows = lax.dynamic_slice_in_dim(skip_gain, chan_start, chan_count, 0)
    length = product_all.shape[1]
    block_len = math.gcd(256, length)
    block_count = length // block_len
    conv_blocks, back_blocks, mode_part, skip_part = long_conv(
        product_all.reshape(chan_count, block_count, block_len),
        adjoint_all.reshape(chan_count, block_count, block_len),
        rate_rows,
        weight_rows,
        gain_rows,
    )
    conv_rows = conv_blocks.reshape(chan_count, length)
    back_rows = back_blocks.reshape(chan_count, length)
    mode_part = mode_part[:, 0, :]
    skip_part = skip_part[:, 0, 0]
    signal = lax.all_to_all(conv_rows, "ctx", split_axis=1, concat_axis=0, tiled=True)
    grad_scale = 1.0 / math.sqrt(token_total)
    local_grads = jnp.concatenate(
        [mode_part * jnp.sqrt(2.0 * rate_rows) * grad_scale, skip_part[:, None] * grad_scale], axis=1
    )
    dp_count = lax.axis_size("dp")
    if dp_count & (dp_count - 1) == 0:
        hop = 1
        while hop < dp_count:
            partners = [(i, i ^ hop) for i in range(dp_count)]
            local_grads = local_grads + lax.ppermute(local_grads, "dp", partners)
            hop *= 2
    else:
        local_grads = lax.psum(local_grads, "dp")
    back_rows, local_grads = lax.optimization_barrier((back_rows, local_grads))
    back_signal = lax.all_to_all(back_rows, "ctx", split_axis=1, concat_axis=0, tiled=True)
    if ctx_count & (ctx_count - 1) == 0:
        ctx_index = lax.axis_index("ctx")
        gathered = local_grads
        hop = 1
        while hop < ctx_count:
            partners = [(i, i ^ hop) for i in range(ctx_count)]
            theirs = lax.ppermute(gathered, "ctx", partners)
            low_side = (ctx_index & hop) == 0
            gathered = jnp.where(
                low_side,
                jnp.concatenate([gathered, theirs], axis=0),
                jnp.concatenate([theirs, gathered], axis=0),
            )
            hop *= 2
    else:
        spread = jnp.broadcast_to(local_grads[None], (ctx_count,) + local_grads.shape)
        gathered = lax.all_to_all(spread, "ctx", split_axis=0, concat_axis=0, tiled=True)
    gathered = gathered.reshape(chans_tp, local_grads.shape[1])
    residue_grad = gathered[:, : mode_part.shape[1]]
    skip_grad = gathered[:, mode_part.shape[1]]
    conv_wide = signal.astype(jnp.float32)
    back_wide = back_signal.astype(jnp.float32)
    hyena_out = (query_feat * conv_wide).astype(jnp.bfloat16)
    feature_grad = jnp.stack(
        [grad_out * conv_wide, back_wide * value_feat, back_wide * key_feat]
    ).astype(jnp.bfloat16)
    next_rim = from_behind(feature_grad[:, :, :rim_width], "ctx", -1)
    input_grad = anticausal_short(feature_grad, next_rim, short_filter).astype(jnp.bfloat16)
    return (hyena_out[None], input_grad[None], residue_grad, skip_grad)


def solution(mesh):
    placed = (
        P("dp", None, "tp", "ctx"),
        P("dp", None, ("ctx", "tp")),
        P(None, None, "tp"),
        P("tp", None),
        P("tp", None),
        P("tp"),
    )
    return jax.shard_map(
        on_device,
        mesh=mesh,
        in_specs=placed,
        out_specs=(P("dp", "tp", "ctx"), P("dp", None, "tp", "ctx"), P("tp", None), P("tp")),
        check_vma=False,
    )
```

```python
from functools import partial
import math

import jax
import jax.numpy as jnp
from jax import lax
from jax.sharding import PartitionSpec as P
from jax.experimental import pallas as pl
from jax.experimental.pallas import tpu as pltpu

exact_mode = lax.Precision.HIGHEST
data_mode = lax.Precision.HIGH


def from_behind(shard, axis, by):
    count = lax.axis_size(axis)
    pairs = [(i, i + by) for i in range(count) if 0 <= i + by < count]
    return lax.ppermute(shard, axis, pairs)


def causal_short(proj_rows, prev_rim, tap_weights):
    rim_width = prev_rim.shape[2]
    token_count = proj_rows.shape[2]
    extended = jnp.concatenate([prev_rim, proj_rows], axis=2).astype(jnp.float32)
    result = tap_weights[:, 0, :, None] * extended[:, :, rim_width : rim_width + token_count]
    for lag_index in range(1, rim_width + 1):
        start_at = rim_width - lag_index
        result = (
            result
            + tap_weights[:, lag_index, :, None] * extended[:, :, start_at : start_at + token_count]
        )
    return result


def anticausal_short(grad_rows, next_rim, tap_weights):
    rim_width = next_rim.shape[2]
    token_count = grad_rows.shape[2]
    extended = jnp.concatenate([grad_rows, next_rim], axis=2).astype(jnp.float32)
    result = tap_weights[:, 0, :, None] * extended[:, :, :token_count]
    for lag_index in range(1, rim_width + 1):
        result = (
            result
            + tap_weights[:, lag_index, :, None]
            * extended[:, :, lag_index : lag_index + token_count]
        )
    return result


def make_tables(rate_rows, block_len):
    offsets = jnp.arange(block_len, dtype=jnp.float32)
    fall_now = jnp.exp(-rate_rows[:, :, None] * offsets)
    rise_now = jnp.exp(rate_rows[:, :, None] * offsets)
    fall_next = jnp.exp(-rate_rows[:, :, None] * (offsets + 1.0))
    fall_tail = jnp.exp(-rate_rows[:, :, None] * (block_len - 1.0 - offsets))
    lower_mask = offsets[:, None] >= offsets[None, :]
    return (fall_now, rise_now, fall_next, fall_tail, lower_mask)


def chain_link(earlier, later):
    return (earlier[0] * later[0], later[0] * earlier[1] + later[1])


def modal_pass(signal, rate_rows, weights, incoming, tables):
    fall_now, rise_now, fall_next, fall_tail, lower_mask = tables
    block_len = fall_now.shape[2]
    chan_count, length = signal.shape
    block_count = length // block_len
    pieces = signal.reshape(chan_count, block_count, block_len)
    kernel = jnp.einsum(
        "cnt,cns->cts", weights[:, :, None] * fall_now, rise_now, precision=exact_mode
    )
    kernel = jnp.where(lower_mask[None], kernel, 0.0)
    inside = jnp.einsum("cts,cbs->cbt", kernel, pieces, precision=data_mode)
    block_ends = jnp.einsum("cns,cbs->cnb", fall_tail, pieces, precision=data_mode)
    span_decay = jnp.exp(-rate_rows * block_len)
    block_mults = jnp.broadcast_to(span_decay[:, :, None], block_ends.shape)
    _, running = lax.associative_scan(chain_link, (block_mults, block_ends), axis=2)
    block_steps = jnp.arange(block_count, dtype=jnp.float32)
    before = jnp.concatenate([jnp.zeros_like(running[:, :, :1]), running[:, :, :-1]], axis=2)
    before = (
        before + jnp.exp(-rate_rows[:, :, None] * block_len * block_steps) * incoming[:, :, None]
    )
    carry_in = jnp.einsum(
        "cnt,cnb->cbt", weights[:, :, None] * fall_next, before, precision=exact_mode
    )
    return ((inside + carry_in).reshape(chan_count, length), before)


def mode_products(signal, adjoint, before, tables):
    fall_now, rise_now, fall_next, fall_tail, lower_mask = tables
    block_len = fall_now.shape[2]
    chan_count, length = signal.shape
    block_count = length // block_len
    pieces = signal.reshape(chan_count, block_count, block_len)
    dual_pieces = adjoint.reshape(chan_count, block_count, block_len)
    crossed = jnp.einsum("cbt,cbs->cts", dual_pieces, pieces, precision=data_mode)
    crossed = jnp.where(lower_mask[None], crossed, 0.0)
    weighted = jnp.einsum("cts,cnt->cns", crossed, fall_now, precision=exact_mode)
    inside = jnp.sum(weighted * rise_now, axis=2)
    carried = jnp.einsum("cbt,cnt->cnb", dual_pieces, fall_next, precision=data_mode)
    return inside + jnp.sum(carried * before, axis=2)


def channel_group(group_items, block_len):
    (
        forward_narrow,
        backward_narrow,
        rate_rows,
        weights,
        gain_rows,
        enter_forward,
        enter_backward,
    ) = group_items
    forward_rows = forward_narrow.astype(jnp.float32)
    backward_rows = backward_narrow.astype(jnp.float32)
    tables = make_tables(rate_rows, block_len)
    carried, before = modal_pass(forward_rows, rate_rows, weights, enter_forward, tables)
    returned, _ = modal_pass(jnp.flip(backward_rows, 1), rate_rows, weights, enter_backward, tables)
    signal = (carried + gain_rows[:, None] * forward_rows).astype(jnp.bfloat16)
    back_signal = (jnp.flip(returned, 1) + gain_rows[:, None] * backward_rows).astype(jnp.bfloat16)
    mode_raw = mode_products(forward_rows, backward_rows, before, tables)
    skip_raw = jnp.sum(backward_rows * forward_rows, axis=1)
    return (signal, back_signal, mode_raw, skip_raw)


def split_pair(values):
    high = values.astype(jnp.bfloat16)
    low = (values - high.astype(jnp.float32)).astype(jnp.bfloat16)
    return high, low


def mat_nn(a, b):
    return jnp.dot(a, b, preferred_element_type=jnp.float32)


def mat_nt(a, b):
    return lax.dot_general(a, b, (((1,), (1,)), ((), ())), preferred_element_type=jnp.float32)


def mat_tn(a, b):
    return lax.dot_general(a, b, (((0,), (0,)), ((), ())), preferred_element_type=jnp.float32)


def wide_nn(a, b_pair):
    a_high, a_low = split_pair(a)
    return mat_nn(a_high, b_pair[0]) + mat_nn(a_high, b_pair[1]) + mat_nn(a_low, b_pair[0])


def shifted(values, by, lanes_rows):
    rows = values.shape[0]
    rolled = pltpu.roll(values, by % rows, 0)
    index = lax.broadcasted_iota(jnp.int32, values.shape, 0)
    keep = (index >= by) if by > 0 else (index < rows + by)
    return jnp.where(keep, rolled, 0.0)


def long_conv_kernel(backward, *refs):
    if backward:
        u_ref, dz_ref, krow_ref, tab_ref, row_ref, du_ref, mode_ref, skip_ref = refs
    else:
        u_ref, krow_ref, tab_ref, row_ref, z_ref = refs
    chans, blocks, width = u_ref.shape
    modes = tab_ref.shape[2]
    col = lax.broadcasted_iota(jnp.int32, (width, width), 1)
    row = lax.broadcasted_iota(jnp.int32, (width, width), 0)
    upper = col >= row
    lower = col <= row
    lag_ids = lax.broadcasted_iota(jnp.int32, (width, modes), 0).astype(jnp.float32)

    def one_channel(c, carry):
        u_narrow = u_ref[c]
        tabs = tab_ref[c]
        rows = row_ref[c]
        krow = krow_ref[c]
        fall_end = (tabs[0], tabs[1])
        fall_start = (tabs[2], tabs[3])
        gain_fwd = (tabs[4], tabs[5])
        gain_bwd = (tabs[6], tabs[7])
        rate_row = rows[6:7, :]
        step_row = rows[5:6, :]
        gain = rows[7:8, 0:1]
        u_wide = u_narrow.astype(jnp.float32)
        ends = mat_nt(u_narrow, fall_end[0]) + mat_nt(u_narrow, fall_end[1])
        fwd_state = ends
        level = 0
        span = 1
        while span < blocks:
            decay = rows[level : level + 1, :]
            fwd_state = fwd_state + decay * shifted(fwd_state, span, blocks)
            level += 1
            span *= 2
        state_before = shifted(fwd_state, 1, blocks)
        if not backward:
            ahead = pltpu.roll(
                jnp.broadcast_to(krow[0:1, :], (width, width)), 0, 1, stride=1, stride_axis=0
            )
            ahead = jnp.where(upper, ahead, 0.0)
            a_high, a_low = split_pair(ahead)
            z_in = mat_nn(
                jnp.concatenate([u_narrow, u_narrow], axis=1), jnp.concatenate([a_high, a_low], axis=0)
            )
            z_carry = wide_nn(state_before, gain_fwd)
            z_ref[c] = (z_in + z_carry + gain * u_wide).astype(z_ref.dtype)
            return carry
        dz_narrow = dz_ref[c]
        behind = pltpu.roll(
            jnp.broadcast_to(krow[1:2, :], (width, width)), 1, 1, stride=1, stride_axis=0
        )
        behind = jnp.where(lower, behind, 0.0)
        b_high, b_low = split_pair(behind)
        du_in = mat_nn(
            jnp.concatenate([dz_narrow, dz_narrow], axis=1), jnp.concatenate([b_high, b_low], axis=0)
        )
        starts = mat_nt(dz_narrow, fall_start[0]) + mat_nt(dz_narrow, fall_start[1])
        bwd_state = starts
        level = 0
        span = 1
        while span < blocks:
            decay = rows[level : level + 1, :]
            bwd_state = bwd_state + decay * shifted(bwd_state, -span, blocks)
            level += 1
            span *= 2
        state_after = shifted(bwd_state, -1, blocks)
        du_carry = wide_nn(state_after, gain_bwd)
        dz_wide = dz_narrow.astype(jnp.float32)
        du_ref[c] = (du_in + du_carry + gain * dz_wide).astype(du_ref.dtype)
        rise = jnp.exp(lag_ids * rate_row)
        crossed = mat_tn(u_narrow, dz_narrow)
        crossed = jnp.where(upper, crossed, 0.0)
        c_high, c_low = split_pair(crossed)
        weighted = (
            mat_nt(c_high, fall_start[0]) + mat_nt(c_high, fall_start[1]) + mat_nt(c_low, fall_start[0])
        )
        mode_in = jnp.sum(weighted * rise, axis=0, keepdims=True)
        mode_carry = jnp.sum(state_before * starts, axis=0, keepdims=True) * step_row
        mode_ref[c] = mode_in + mode_carry
        skip_ref[c] = jnp.broadcast_to(jnp.sum(u_wide * dz_wide), skip_ref.shape[1:])
        return carry

    lax.fori_loop(0, chans, one_channel, 0, unroll=chans)


def long_conv_tables(rate_rows, weight_rows, gain_rows, width, blocks):
    offsets = jnp.arange(width, dtype=jnp.float32)
    rate = rate_rows[:, :, None]
    weight = weight_rows[:, :, None]
    fall_end = jnp.exp(-rate * (width - 1.0 - offsets))
    fall_start = jnp.exp(-rate * offsets)
    gain_fwd = weight * jnp.exp(-rate * (offsets + 1.0))
    gain_bwd = weight * jnp.exp(-rate * (width - offsets))
    pairs = []
    for table in (fall_end, fall_start, gain_fwd, gain_bwd):
        high = lax.reduce_precision(table, exponent_bits=8, mantissa_bits=7)
        pairs.extend((high.astype(jnp.bfloat16), (table - high).astype(jnp.bfloat16)))
    tabs = jnp.stack(pairs, axis=1)
    levels = []
    span = 1
    while span < blocks:
        levels.append(jnp.exp(-rate_rows * (width * span)))
        span *= 2
    chan_count, modes = rate_rows.shape
    while len(levels) < 5:
        levels.append(jnp.zeros_like(rate_rows))
    levels.append(jnp.exp(-rate_rows))
    levels.append(rate_rows)
    levels.append(jnp.broadcast_to(gain_rows[:, None], (chan_count, modes)))
    lag_kernel = jnp.sum(weight * fall_start, axis=1)
    krow = jnp.stack([lag_kernel, jnp.flip(lag_kernel, axis=1)], axis=1)
    return tabs, jnp.stack(levels, axis=1), krow


def long_conv(u_blocks, dz_blocks, rate_rows, weight_rows, gain_rows, chans_per_step=8):
    chan_count, blocks, width = u_blocks.shape
    modes = rate_rows.shape[1]
    tabs, rows, krow = long_conv_tables(rate_rows, weight_rows, gain_rows, width, blocks)
    step = min(chans_per_step, chan_count)
    data_spec = pl.BlockSpec((step, blocks, width), lambda i: (i, 0, 0))
    side_specs = [
        pl.BlockSpec((step,) + krow.shape[1:], lambda i: (i, 0, 0)),
        pl.BlockSpec((step,) + tabs.shape[1:], lambda i: (i, 0, 0, 0)),
        pl.BlockSpec((step,) + rows.shape[1:], lambda i: (i, 0, 0)),
    ]
    forward = pl.pallas_call(
        partial(long_conv_kernel, False),
        grid=(chan_count // step,),
        in_specs=[data_spec] + side_specs,
        out_specs=data_spec,
        out_shape=jax.ShapeDtypeStruct(u_blocks.shape, jnp.bfloat16),
        cost_estimate=pl.CostEstimate(
            flops=chan_count * 300 * width * width * blocks, transcendentals=0,
            bytes_accessed=chan_count * blocks * width * 4 + tabs.size * 2,
        ),
    )(u_blocks, krow, tabs, rows)
    backward = pl.pallas_call(
        partial(long_conv_kernel, True),
        grid=(chan_count // step,),
        in_specs=[data_spec, data_spec] + side_specs,
        out_specs=[
            data_spec,
            pl.BlockSpec((step, 1, modes), lambda i: (i, 0, 0)),
            pl.BlockSpec((step, 1, 128), lambda i: (i, 0, 0)),
        ],
        out_shape=[
            jax.ShapeDtypeStruct(u_blocks.shape, jnp.bfloat16),
            jax.ShapeDtypeStruct((chan_count, 1, modes), jnp.float32),
            jax.ShapeDtypeStruct((chan_count, 1, 128), jnp.float32),
        ],
        cost_estimate=pl.CostEstimate(
            flops=chan_count * 500 * width * width * blocks, transcendentals=chan_count * width * modes,
            bytes_accessed=chan_count * blocks * width * 6 + tabs.size * 2,
        ),
    )(u_blocks, dz_blocks, krow, tabs, rows)
    return (forward,) + tuple(backward)


def grouped(function, arrays, group_size):
    stacked = tuple(
        (
            item.reshape((item.shape[0] // group_size, group_size) + item.shape[1:])
            for item in arrays
        )
    )
    results = lax.map(function, stacked)
    return tuple(
        (item.reshape((item.shape[0] * item.shape[1],) + item.shape[2:]) for item in results)
    )


def on_device(projected, cotangent, short_filter, residues, decay_rate, skip_gain):
    proj_rows = projected[0]
    token_count = proj_rows.shape[2]
    chans_tp = proj_rows.shape[1]
    rim_width = short_filter.shape[1] - 1
    tp_count = lax.axis_size("tp")
    if tp_count == 2:
        tp_index = lax.axis_index("tp")
        grad_rows = cotangent[0]
        mine = lax.dynamic_slice_in_dim(grad_rows, tp_index * chans_tp, chans_tp, 0)
        other = lax.dynamic_slice_in_dim(grad_rows, (1 - tp_index) * chans_tp, chans_tp, 0)
        theirs = lax.ppermute(other, "tp", [(0, 1), (1, 0)])
        first = jnp.where(tp_index == 0, mine, theirs)
        second = jnp.where(tp_index == 0, theirs, mine)
        grad_out = jnp.concatenate([first, second], axis=1).astype(jnp.float32)
    else:
        grad_out = lax.all_to_all(
            cotangent[0], "tp", split_axis=0, concat_axis=1, tiled=True
        ).astype(jnp.float32)
    prev_rim = from_behind(proj_rows[:, :, token_count - rim_width :], "ctx", 1)
    featured = lax.optimization_barrier(
        causal_short(proj_rows, prev_rim, short_filter).astype(jnp.bfloat16)
    )
    query_feat = featured[0].astype(jnp.float32)
    key_feat = featured[1].astype(jnp.float32)
    value_feat = featured[2].astype(jnp.float32)
    product = (key_feat * value_feat).astype(jnp.bfloat16)
    adjoint = (grad_out * query_feat).astype(jnp.bfloat16)
    ctx_count = lax.axis_size("ctx")
    token_total = token_count * ctx_count * lax.axis_size("dp")
    weight_all = residues * jnp.sqrt(2.0 * decay_rate)
    product_all, adjoint_all = (
        lax.all_to_all(product, "ctx", split_axis=0, concat_axis=1, tiled=True),
        lax.all_to_all(adjoint, "ctx", split_axis=0, concat_axis=1, tiled=True),
    )
    chan_count = chans_tp // ctx_count
    chan_start = lax.axis_index("ctx") * chan_count
    rate_rows = lax.dynamic_slice_in_dim(decay_rate, chan_start, chan_count, 0)
    weight_rows = lax.dynamic_slice_in_dim(weight_all, chan_start, chan_count, 0)
    gain_rows = lax.dynamic_slice_in_dim(skip_gain, chan_start, chan_count, 0)
    length = product_all.shape[1]
    block_len = math.gcd(256, length)
    block_count = length // block_len
    conv_blocks, back_blocks, mode_part, skip_part = long_conv(
        product_all.reshape(chan_count, block_count, block_len),
        adjoint_all.reshape(chan_count, block_count, block_len),
        rate_rows,
        weight_rows,
        gain_rows,
    )
    conv_rows = conv_blocks.reshape(chan_count, length)
    back_rows = back_blocks.reshape(chan_count, length)
    mode_part = mode_part[:, 0, :]
    skip_part = skip_part[:, 0, 0]
    signal, back_signal = (
        lax.all_to_all(conv_rows, "ctx", split_axis=1, concat_axis=0, tiled=True),
        lax.all_to_all(back_rows, "ctx", split_axis=1, concat_axis=0, tiled=True),
    )
    grad_scale = 1.0 / math.sqrt(token_total)
    local_grads = jnp.concatenate(
        [mode_part * jnp.sqrt(2.0 * rate_rows) * grad_scale, skip_part[:, None] * grad_scale], axis=1
    )
    dp_count = lax.axis_size("dp")
    if dp_count & (dp_count - 1) == 0:
        hop = 1
        while hop < dp_count:
            partners = [(i, i ^ hop) for i in range(dp_count)]
            local_grads = local_grads + lax.ppermute(local_grads, "dp", partners)
            hop *= 2
    else:
        local_grads = lax.psum(local_grads, "dp")
    if ctx_count & (ctx_count - 1) == 0:
        ctx_index = lax.axis_index("ctx")
        gathered = local_grads
        hop = 1
        while hop < ctx_count:
            partners = [(i, i ^ hop) for i in range(ctx_count)]
            theirs = lax.ppermute(gathered, "ctx", partners)
            low_side = (ctx_index & hop) == 0
            gathered = jnp.where(
                low_side,
                jnp.concatenate([gathered, theirs], axis=0),
                jnp.concatenate([theirs, gathered], axis=0),
            )
            hop *= 2
    else:
        spread = jnp.broadcast_to(local_grads[None], (ctx_count,) + local_grads.shape)
        gathered = lax.all_to_all(spread, "ctx", split_axis=0, concat_axis=0, tiled=True)
    gathered = gathered.reshape(chans_tp, local_grads.shape[1])
    residue_grad = gathered[:, : mode_part.shape[1]]
    skip_grad = gathered[:, mode_part.shape[1]]
    conv_wide = signal.astype(jnp.float32)
    back_wide = back_signal.astype(jnp.float32)
    hyena_out = (query_feat * conv_wide).astype(jnp.bfloat16)
    feature_grad = jnp.stack(
        [grad_out * conv_wide, back_wide * value_feat, back_wide * key_feat]
    ).astype(jnp.bfloat16)
    next_rim = from_behind(feature_grad[:, :, :rim_width], "ctx", -1)
    input_grad = anticausal_short(feature_grad, next_rim, short_filter).astype(jnp.bfloat16)
    return (hyena_out[None], input_grad[None], residue_grad, skip_grad)


def solution(mesh):
    placed = (
        P("dp", None, "tp", "ctx"),
        P("dp", None, ("ctx", "tp")),
        P(None, None, "tp"),
        P("tp", None),
        P("tp", None),
        P("tp"),
    )
    return jax.shard_map(
        on_device,
        mesh=mesh,
        in_specs=placed,
        out_specs=(P("dp", "tp", "ctx"), P("dp", None, "tp", "ctx"), P("tp", None), P("tp")),
        check_vma=False,
    )
```

```python
from functools import partial
import math

import jax
import jax.numpy as jnp
from jax import lax
from jax.sharding import PartitionSpec as P
from jax.experimental import pallas as pl
from jax.experimental.pallas import tpu as pltpu

exact_mode = lax.Precision.HIGHEST
data_mode = lax.Precision.HIGH


def from_behind(shard, axis, by):
    count = lax.axis_size(axis)
    pairs = [(i, i + by) for i in range(count) if 0 <= i + by < count]
    return lax.ppermute(shard, axis, pairs)


def causal_short(proj_rows, prev_rim, tap_weights):
    rim_width = prev_rim.shape[2]
    token_count = proj_rows.shape[2]
    extended = jnp.concatenate([prev_rim, proj_rows], axis=2).astype(jnp.float32)
    result = tap_weights[:, 0, :, None] * extended[:, :, rim_width : rim_width + token_count]
    for lag_index in range(1, rim_width + 1):
        start_at = rim_width - lag_index
        result = (
            result
            + tap_weights[:, lag_index, :, None] * extended[:, :, start_at : start_at + token_count]
        )
    return result


def anticausal_short(grad_rows, next_rim, tap_weights):
    rim_width = next_rim.shape[2]
    token_count = grad_rows.shape[2]
    extended = jnp.concatenate([grad_rows, next_rim], axis=2).astype(jnp.float32)
    result = tap_weights[:, 0, :, None] * extended[:, :, :token_count]
    for lag_index in range(1, rim_width + 1):
        result = (
            result
            + tap_weights[:, lag_index, :, None]
            * extended[:, :, lag_index : lag_index + token_count]
        )
    return result


def make_tables(rate_rows, block_len):
    offsets = jnp.arange(block_len, dtype=jnp.float32)
    fall_now = jnp.exp(-rate_rows[:, :, None] * offsets)
    rise_now = jnp.exp(rate_rows[:, :, None] * offsets)
    fall_next = jnp.exp(-rate_rows[:, :, None] * (offsets + 1.0))
    fall_tail = jnp.exp(-rate_rows[:, :, None] * (block_len - 1.0 - offsets))
    lower_mask = offsets[:, None] >= offsets[None, :]
    return (fall_now, rise_now, fall_next, fall_tail, lower_mask)


def chain_link(earlier, later):
    return (earlier[0] * later[0], later[0] * earlier[1] + later[1])


def modal_pass(signal, rate_rows, weights, incoming, tables):
    fall_now, rise_now, fall_next, fall_tail, lower_mask = tables
    block_len = fall_now.shape[2]
    chan_count, length = signal.shape
    block_count = length // block_len
    pieces = signal.reshape(chan_count, block_count, block_len)
    kernel = jnp.einsum(
        "cnt,cns->cts", weights[:, :, None] * fall_now, rise_now, precision=exact_mode
    )
    kernel = jnp.where(lower_mask[None], kernel, 0.0)
    inside = jnp.einsum("cts,cbs->cbt", kernel, pieces, precision=data_mode)
    block_ends = jnp.einsum("cns,cbs->cnb", fall_tail, pieces, precision=data_mode)
    span_decay = jnp.exp(-rate_rows * block_len)
    block_mults = jnp.broadcast_to(span_decay[:, :, None], block_ends.shape)
    _, running = lax.associative_scan(chain_link, (block_mults, block_ends), axis=2)
    block_steps = jnp.arange(block_count, dtype=jnp.float32)
    before = jnp.concatenate([jnp.zeros_like(running[:, :, :1]), running[:, :, :-1]], axis=2)
    before = (
        before + jnp.exp(-rate_rows[:, :, None] * block_len * block_steps) * incoming[:, :, None]
    )
    carry_in = jnp.einsum(
        "cnt,cnb->cbt", weights[:, :, None] * fall_next, before, precision=exact_mode
    )
    return ((inside + carry_in).reshape(chan_count, length), before)


def mode_products(signal, adjoint, before, tables):
    fall_now, rise_now, fall_next, fall_tail, lower_mask = tables
    block_len = fall_now.shape[2]
    chan_count, length = signal.shape
    block_count = length // block_len
    pieces = signal.reshape(chan_count, block_count, block_len)
    dual_pieces = adjoint.reshape(chan_count, block_count, block_len)
    crossed = jnp.einsum("cbt,cbs->cts", dual_pieces, pieces, precision=data_mode)
    crossed = jnp.where(lower_mask[None], crossed, 0.0)
    weighted = jnp.einsum("cts,cnt->cns", crossed, fall_now, precision=exact_mode)
    inside = jnp.sum(weighted * rise_now, axis=2)
    carried = jnp.einsum("cbt,cnt->cnb", dual_pieces, fall_next, precision=data_mode)
    return inside + jnp.sum(carried * before, axis=2)


def channel_group(group_items, block_len):
    (
        forward_narrow,
        backward_narrow,
        rate_rows,
        weights,
        gain_rows,
        enter_forward,
        enter_backward,
    ) = group_items
    forward_rows = forward_narrow.astype(jnp.float32)
    backward_rows = backward_narrow.astype(jnp.float32)
    tables = make_tables(rate_rows, block_len)
    carried, before = modal_pass(forward_rows, rate_rows, weights, enter_forward, tables)
    returned, _ = modal_pass(jnp.flip(backward_rows, 1), rate_rows, weights, enter_backward, tables)
    signal = (carried + gain_rows[:, None] * forward_rows).astype(jnp.bfloat16)
    back_signal = (jnp.flip(returned, 1) + gain_rows[:, None] * backward_rows).astype(jnp.bfloat16)
    mode_raw = mode_products(forward_rows, backward_rows, before, tables)
    skip_raw = jnp.sum(backward_rows * forward_rows, axis=1)
    return (signal, back_signal, mode_raw, skip_raw)


def split_pair(values):
    high = values.astype(jnp.bfloat16)
    low = (values - high.astype(jnp.float32)).astype(jnp.bfloat16)
    return high, low


def mat_nn(a, b):
    return jnp.dot(a, b, preferred_element_type=jnp.float32)


def mat_nt(a, b):
    return lax.dot_general(a, b, (((1,), (1,)), ((), ())), preferred_element_type=jnp.float32)


def mat_tn(a, b):
    return lax.dot_general(a, b, (((0,), (0,)), ((), ())), preferred_element_type=jnp.float32)


def wide_nn(a, b_pair):
    a_high, a_low = split_pair(a)
    return mat_nn(a_high, b_pair[0]) + mat_nn(a_high, b_pair[1]) + mat_nn(a_low, b_pair[0])


def shifted(values, by, lanes_rows):
    rows = values.shape[0]
    rolled = pltpu.roll(values, by % rows, 0)
    index = lax.broadcasted_iota(jnp.int32, values.shape, 0)
    keep = (index >= by) if by > 0 else (index < rows + by)
    return jnp.where(keep, rolled, 0.0)


def long_conv_kernel(backward, *refs):
    if backward:
        u_ref, dz_ref, krow_ref, tab_ref, row_ref, du_ref, mode_ref, skip_ref = refs
    else:
        u_ref, krow_ref, tab_ref, row_ref, z_ref = refs
    chans, blocks, width = u_ref.shape
    modes = tab_ref.shape[2]
    col = lax.broadcasted_iota(jnp.int32, (width, width), 1)
    row = lax.broadcasted_iota(jnp.int32, (width, width), 0)
    upper = col >= row
    lower = col <= row
    lag_ids = lax.broadcasted_iota(jnp.int32, (width, modes), 0).astype(jnp.float32)

    def one_channel(c, carry):
        u_narrow = u_ref[c]
        tabs = tab_ref[c]
        rows = row_ref[c]
        krow = krow_ref[c]
        fall_end = (tabs[0], tabs[1])
        fall_start = (tabs[2], tabs[3])
        gain_fwd = (tabs[4], tabs[5])
        gain_bwd = (tabs[6], tabs[7])
        rate_row = rows[6:7, :]
        step_row = rows[5:6, :]
        gain = rows[7:8, 0:1]
        u_wide = u_narrow.astype(jnp.float32)
        ends = mat_nt(u_narrow, fall_end[0]) + mat_nt(u_narrow, fall_end[1])
        fwd_state = ends
        level = 0
        span = 1
        while span < blocks:
            decay = rows[level : level + 1, :]
            fwd_state = fwd_state + decay * shifted(fwd_state, span, blocks)
            level += 1
            span *= 2
        state_before = shifted(fwd_state, 1, blocks)
        if not backward:
            ahead = pltpu.roll(
                jnp.broadcast_to(krow[0:1, :], (width, width)), 0, 1, stride=1, stride_axis=0
            )
            ahead = jnp.where(upper, ahead, 0.0)
            a_high, a_low = split_pair(ahead)
            z_in = mat_nn(
                jnp.concatenate([u_narrow, u_narrow], axis=1), jnp.concatenate([a_high, a_low], axis=0)
            )
            z_carry = wide_nn(state_before, gain_fwd)
            z_ref[c] = (z_in + z_carry + gain * u_wide).astype(z_ref.dtype)
            return carry
        dz_narrow = dz_ref[c]
        behind = pltpu.roll(
            jnp.broadcast_to(krow[1:2, :], (width, width)), 1, 1, stride=1, stride_axis=0
        )
        behind = jnp.where(lower, behind, 0.0)
        b_high, b_low = split_pair(behind)
        du_in = mat_nn(
            jnp.concatenate([dz_narrow, dz_narrow], axis=1), jnp.concatenate([b_high, b_low], axis=0)
        )
        starts = mat_nt(dz_narrow, fall_start[0]) + mat_nt(dz_narrow, fall_start[1])
        bwd_state = starts
        level = 0
        span = 1
        while span < blocks:
            decay = rows[level : level + 1, :]
            bwd_state = bwd_state + decay * shifted(bwd_state, -span, blocks)
            level += 1
            span *= 2
        state_after = shifted(bwd_state, -1, blocks)
        du_carry = wide_nn(state_after, gain_bwd)
        dz_wide = dz_narrow.astype(jnp.float32)
        du_ref[c] = (du_in + du_carry + gain * dz_wide).astype(du_ref.dtype)
        rise = jnp.exp(lag_ids * rate_row)
        crossed = mat_tn(u_narrow, dz_narrow)
        crossed = jnp.where(upper, crossed, 0.0)
        c_high, c_low = split_pair(crossed)
        weighted = (
            mat_nt(c_high, fall_start[0]) + mat_nt(c_high, fall_start[1]) + mat_nt(c_low, fall_start[0])
        )
        mode_in = jnp.sum(weighted * rise, axis=0, keepdims=True)
        mode_carry = jnp.sum(state_before * starts, axis=0, keepdims=True) * step_row
        mode_ref[c] = mode_in + mode_carry
        skip_ref[c] = jnp.broadcast_to(jnp.sum(u_wide * dz_wide), skip_ref.shape[1:])
        return carry

    lax.fori_loop(0, chans, one_channel, 0, unroll=chans)


def long_conv_tables(rate_rows, weight_rows, gain_rows, width, blocks):
    offsets = jnp.arange(width, dtype=jnp.float32)
    rate = rate_rows[:, :, None]
    weight = weight_rows[:, :, None]
    fall_end = jnp.exp(-rate * (width - 1.0 - offsets))
    fall_start = jnp.exp(-rate * offsets)
    gain_fwd = weight * jnp.exp(-rate * (offsets + 1.0))
    gain_bwd = weight * jnp.exp(-rate * (width - offsets))
    pairs = []
    for table in (fall_end, fall_start, gain_fwd, gain_bwd):
        high = lax.reduce_precision(table, exponent_bits=8, mantissa_bits=7)
        pairs.extend((high.astype(jnp.bfloat16), (table - high).astype(jnp.bfloat16)))
    tabs = jnp.stack(pairs, axis=1)
    levels = []
    span = 1
    while span < blocks:
        levels.append(jnp.exp(-rate_rows * (width * span)))
        span *= 2
    chan_count, modes = rate_rows.shape
    while len(levels) < 5:
        levels.append(jnp.zeros_like(rate_rows))
    levels.append(jnp.exp(-rate_rows))
    levels.append(rate_rows)
    levels.append(jnp.broadcast_to(gain_rows[:, None], (chan_count, modes)))
    lag_kernel = jnp.sum(weight * fall_start, axis=1)
    krow = jnp.stack([lag_kernel, jnp.flip(lag_kernel, axis=1)], axis=1)
    return tabs, jnp.stack(levels, axis=1), krow


def long_conv(u_blocks, dz_blocks, rate_rows, weight_rows, gain_rows, chans_per_step=16):
    chan_count, blocks, width = u_blocks.shape
    modes = rate_rows.shape[1]
    tabs, rows, krow = long_conv_tables(rate_rows, weight_rows, gain_rows, width, blocks)
    step = min(chans_per_step, chan_count)
    data_spec = pl.BlockSpec((step, blocks, width), lambda i: (i, 0, 0))
    side_specs = [
        pl.BlockSpec((step,) + krow.shape[1:], lambda i: (i, 0, 0)),
        pl.BlockSpec((step,) + tabs.shape[1:], lambda i: (i, 0, 0, 0)),
        pl.BlockSpec((step,) + rows.shape[1:], lambda i: (i, 0, 0)),
    ]
    forward = pl.pallas_call(
        partial(long_conv_kernel, False),
        grid=(chan_count // step,),
        in_specs=[data_spec] + side_specs,
        out_specs=data_spec,
        out_shape=jax.ShapeDtypeStruct(u_blocks.shape, jnp.bfloat16),
        cost_estimate=pl.CostEstimate(
            flops=chan_count * 300 * width * width * blocks, transcendentals=0,
            bytes_accessed=chan_count * blocks * width * 4 + tabs.size * 2,
        ),
    )(u_blocks, krow, tabs, rows)
    backward = pl.pallas_call(
        partial(long_conv_kernel, True),
        grid=(chan_count // step,),
        in_specs=[data_spec, data_spec] + side_specs,
        out_specs=[
            data_spec,
            pl.BlockSpec((step, 1, modes), lambda i: (i, 0, 0)),
            pl.BlockSpec((step, 1, 128), lambda i: (i, 0, 0)),
        ],
        out_shape=[
            jax.ShapeDtypeStruct(u_blocks.shape, jnp.bfloat16),
            jax.ShapeDtypeStruct((chan_count, 1, modes), jnp.float32),
            jax.ShapeDtypeStruct((chan_count, 1, 128), jnp.float32),
        ],
        cost_estimate=pl.CostEstimate(
            flops=chan_count * 500 * width * width * blocks, transcendentals=chan_count * width * modes,
            bytes_accessed=chan_count * blocks * width * 6 + tabs.size * 2,
        ),
    )(u_blocks, dz_blocks, krow, tabs, rows)
    return (forward,) + tuple(backward)


def grouped(function, arrays, group_size):
    stacked = tuple(
        (
            item.reshape((item.shape[0] // group_size, group_size) + item.shape[1:])
            for item in arrays
        )
    )
    results = lax.map(function, stacked)
    return tuple(
        (item.reshape((item.shape[0] * item.shape[1],) + item.shape[2:]) for item in results)
    )


def on_device(projected, cotangent, short_filter, residues, decay_rate, skip_gain):
    proj_rows = projected[0]
    token_count = proj_rows.shape[2]
    chans_tp = proj_rows.shape[1]
    rim_width = short_filter.shape[1] - 1
    tp_count = lax.axis_size("tp")
    if tp_count == 2:
        tp_index = lax.axis_index("tp")
        grad_rows = cotangent[0]
        mine = lax.dynamic_slice_in_dim(grad_rows, tp_index * chans_tp, chans_tp, 0)
        other = lax.dynamic_slice_in_dim(grad_rows, (1 - tp_index) * chans_tp, chans_tp, 0)
        theirs = lax.ppermute(other, "tp", [(0, 1), (1, 0)])
        first = jnp.where(tp_index == 0, mine, theirs)
        second = jnp.where(tp_index == 0, theirs, mine)
        grad_out = jnp.concatenate([first, second], axis=1).astype(jnp.float32)
    else:
        grad_out = lax.all_to_all(
            cotangent[0], "tp", split_axis=0, concat_axis=1, tiled=True
        ).astype(jnp.float32)
    prev_rim = from_behind(proj_rows[:, :, token_count - rim_width :], "ctx", 1)
    featured = lax.optimization_barrier(
        causal_short(proj_rows, prev_rim, short_filter).astype(jnp.bfloat16)
    )
    query_feat = featured[0].astype(jnp.float32)
    key_feat = featured[1].astype(jnp.float32)
    value_feat = featured[2].astype(jnp.float32)
    product = (key_feat * value_feat).astype(jnp.bfloat16)
    adjoint = (grad_out * query_feat).astype(jnp.bfloat16)
    ctx_count = lax.axis_size("ctx")
    token_total = token_count * ctx_count * lax.axis_size("dp")
    weight_all = residues * jnp.sqrt(2.0 * decay_rate)
    product_all, adjoint_all = (
        lax.all_to_all(product, "ctx", split_axis=0, concat_axis=1, tiled=True),
        lax.all_to_all(adjoint, "ctx", split_axis=0, concat_axis=1, tiled=True),
    )
    chan_count = chans_tp // ctx_count
    chan_start = lax.axis_index("ctx") * chan_count
    rate_rows = lax.dynamic_slice_in_dim(decay_rate, chan_start, chan_count, 0)
    weight_rows = lax.dynamic_slice_in_dim(weight_all, chan_start, chan_count, 0)
    gain_rows = lax.dynamic_slice_in_dim(skip_gain, chan_start, chan_count, 0)
    length = product_all.shape[1]
    block_len = math.gcd(256, length)
    block_count = length // block_len
    conv_blocks, back_blocks, mode_part, skip_part = long_conv(
        product_all.reshape(chan_count, block_count, block_len),
        adjoint_all.reshape(chan_count, block_count, block_len),
        rate_rows,
        weight_rows,
        gain_rows,
    )
    conv_rows = conv_blocks.reshape(chan_count, length)
    back_rows = back_blocks.reshape(chan_count, length)
    mode_part = mode_part[:, 0, :]
    skip_part = skip_part[:, 0, 0]
    signal, back_signal = (
        lax.all_to_all(conv_rows, "ctx", split_axis=1, concat_axis=0, tiled=True),
        lax.all_to_all(back_rows, "ctx", split_axis=1, concat_axis=0, tiled=True),
    )
    grad_scale = 1.0 / math.sqrt(token_total)
    local_grads = jnp.concatenate(
        [mode_part * jnp.sqrt(2.0 * rate_rows) * grad_scale, skip_part[:, None] * grad_scale], axis=1
    )
    dp_count = lax.axis_size("dp")
    if dp_count & (dp_count - 1) == 0:
        hop = 1
        while hop < dp_count:
            partners = [(i, i ^ hop) for i in range(dp_count)]
            local_grads = local_grads + lax.ppermute(local_grads, "dp", partners)
            hop *= 2
    else:
        local_grads = lax.psum(local_grads, "dp")
    if ctx_count & (ctx_count - 1) == 0:
        ctx_index = lax.axis_index("ctx")
        gathered = local_grads
        hop = 1
        while hop < ctx_count:
            partners = [(i, i ^ hop) for i in range(ctx_count)]
            theirs = lax.ppermute(gathered, "ctx", partners)
            low_side = (ctx_index & hop) == 0
            gathered = jnp.where(
                low_side,
                jnp.concatenate([gathered, theirs], axis=0),
                jnp.concatenate([theirs, gathered], axis=0),
            )
            hop *= 2
    else:
        spread = jnp.broadcast_to(local_grads[None], (ctx_count,) + local_grads.shape)
        gathered = lax.all_to_all(spread, "ctx", split_axis=0, concat_axis=0, tiled=True)
    gathered = gathered.reshape(chans_tp, local_grads.shape[1])
    residue_grad = gathered[:, : mode_part.shape[1]]
    skip_grad = gathered[:, mode_part.shape[1]]
    conv_wide = signal.astype(jnp.float32)
    back_wide = back_signal.astype(jnp.float32)
    hyena_out = (query_feat * conv_wide).astype(jnp.bfloat16)
    feature_grad = jnp.stack(
        [grad_out * conv_wide, back_wide * value_feat, back_wide * key_feat]
    ).astype(jnp.bfloat16)
    next_rim = from_behind(feature_grad[:, :, :rim_width], "ctx", -1)
    input_grad = anticausal_short(feature_grad, next_rim, short_filter).astype(jnp.bfloat16)
    return (hyena_out[None], input_grad[None], residue_grad, skip_grad)


def solution(mesh):
    placed = (
        P("dp", None, "tp", "ctx"),
        P("dp", None, ("ctx", "tp")),
        P(None, None, "tp"),
        P("tp", None),
        P("tp", None),
        P("tp"),
    )
    return jax.shard_map(
        on_device,
        mesh=mesh,
        in_specs=placed,
        out_specs=(P("dp", "tp", "ctx"), P("dp", None, "tp", "ctx"), P("tp", None), P("tp")),
        check_vma=False,
    )
```

```python
from functools import partial
import math

import jax
import jax.numpy as jnp
from jax import lax
from jax.sharding import PartitionSpec as P
from jax.experimental import pallas as pl
from jax.experimental.pallas import tpu as pltpu

exact_mode = lax.Precision.HIGHEST
data_mode = lax.Precision.HIGH


def from_behind(shard, axis, by):
    count = lax.axis_size(axis)
    pairs = [(i, i + by) for i in range(count) if 0 <= i + by < count]
    return lax.ppermute(shard, axis, pairs)


def causal_short(proj_rows, prev_rim, tap_weights):
    rim_width = prev_rim.shape[2]
    token_count = proj_rows.shape[2]
    extended = jnp.concatenate([prev_rim, proj_rows], axis=2).astype(jnp.float32)
    result = tap_weights[:, 0, :, None] * extended[:, :, rim_width : rim_width + token_count]
    for lag_index in range(1, rim_width + 1):
        start_at = rim_width - lag_index
        result = (
            result
            + tap_weights[:, lag_index, :, None] * extended[:, :, start_at : start_at + token_count]
        )
    return result


def anticausal_short(grad_rows, next_rim, tap_weights):
    rim_width = next_rim.shape[2]
    token_count = grad_rows.shape[2]
    extended = jnp.concatenate([grad_rows, next_rim], axis=2).astype(jnp.float32)
    result = tap_weights[:, 0, :, None] * extended[:, :, :token_count]
    for lag_index in range(1, rim_width + 1):
        result = (
            result
            + tap_weights[:, lag_index, :, None]
            * extended[:, :, lag_index : lag_index + token_count]
        )
    return result


def make_tables(rate_rows, block_len):
    offsets = jnp.arange(block_len, dtype=jnp.float32)
    fall_now = jnp.exp(-rate_rows[:, :, None] * offsets)
    rise_now = jnp.exp(rate_rows[:, :, None] * offsets)
    fall_next = jnp.exp(-rate_rows[:, :, None] * (offsets + 1.0))
    fall_tail = jnp.exp(-rate_rows[:, :, None] * (block_len - 1.0 - offsets))
    lower_mask = offsets[:, None] >= offsets[None, :]
    return (fall_now, rise_now, fall_next, fall_tail, lower_mask)


def chain_link(earlier, later):
    return (earlier[0] * later[0], later[0] * earlier[1] + later[1])


def modal_pass(signal, rate_rows, weights, incoming, tables):
    fall_now, rise_now, fall_next, fall_tail, lower_mask = tables
    block_len = fall_now.shape[2]
    chan_count, length = signal.shape
    block_count = length // block_len
    pieces = signal.reshape(chan_count, block_count, block_len)
    kernel = jnp.einsum(
        "cnt,cns->cts", weights[:, :, None] * fall_now, rise_now, precision=exact_mode
    )
    kernel = jnp.where(lower_mask[None], kernel, 0.0)
    inside = jnp.einsum("cts,cbs->cbt", kernel, pieces, precision=data_mode)
    block_ends = jnp.einsum("cns,cbs->cnb", fall_tail, pieces, precision=data_mode)
    span_decay = jnp.exp(-rate_rows * block_len)
    block_mults = jnp.broadcast_to(span_decay[:, :, None], block_ends.shape)
    _, running = lax.associative_scan(chain_link, (block_mults, block_ends), axis=2)
    block_steps = jnp.arange(block_count, dtype=jnp.float32)
    before = jnp.concatenate([jnp.zeros_like(running[:, :, :1]), running[:, :, :-1]], axis=2)
    before = (
        before + jnp.exp(-rate_rows[:, :, None] * block_len * block_steps) * incoming[:, :, None]
    )
    carry_in = jnp.einsum(
        "cnt,cnb->cbt", weights[:, :, None] * fall_next, before, precision=exact_mode
    )
    return ((inside + carry_in).reshape(chan_count, length), before)


def mode_products(signal, adjoint, before, tables):
    fall_now, rise_now, fall_next, fall_tail, lower_mask = tables
    block_len = fall_now.shape[2]
    chan_count, length = signal.shape
    block_count = length // block_len
    pieces = signal.reshape(chan_count, block_count, block_len)
    dual_pieces = adjoint.reshape(chan_count, block_count, block_len)
    crossed = jnp.einsum("cbt,cbs->cts", dual_pieces, pieces, precision=data_mode)
    crossed = jnp.where(lower_mask[None], crossed, 0.0)
    weighted = jnp.einsum("cts,cnt->cns", crossed, fall_now, precision=exact_mode)
    inside = jnp.sum(weighted * rise_now, axis=2)
    carried = jnp.einsum("cbt,cnt->cnb", dual_pieces, fall_next, precision=data_mode)
    return inside + jnp.sum(carried * before, axis=2)


def channel_group(group_items, block_len):
    (
        forward_narrow,
        backward_narrow,
        rate_rows,
        weights,
        gain_rows,
        enter_forward,
        enter_backward,
    ) = group_items
    forward_rows = forward_narrow.astype(jnp.float32)
    backward_rows = backward_narrow.astype(jnp.float32)
    tables = make_tables(rate_rows, block_len)
    carried, before = modal_pass(forward_rows, rate_rows, weights, enter_forward, tables)
    returned, _ = modal_pass(jnp.flip(backward_rows, 1), rate_rows, weights, enter_backward, tables)
    signal = (carried + gain_rows[:, None] * forward_rows).astype(jnp.bfloat16)
    back_signal = (jnp.flip(returned, 1) + gain_rows[:, None] * backward_rows).astype(jnp.bfloat16)
    mode_raw = mode_products(forward_rows, backward_rows, before, tables)
    skip_raw = jnp.sum(backward_rows * forward_rows, axis=1)
    return (signal, back_signal, mode_raw, skip_raw)


def split_pair(values):
    high = values.astype(jnp.bfloat16)
    low = (values - high.astype(jnp.float32)).astype(jnp.bfloat16)
    return high, low


def mat_nn(a, b):
    return jnp.dot(a, b, preferred_element_type=jnp.float32)


def mat_nt(a, b):
    return lax.dot_general(a, b, (((1,), (1,)), ((), ())), preferred_element_type=jnp.float32)


def mat_tn(a, b):
    return lax.dot_general(a, b, (((0,), (0,)), ((), ())), preferred_element_type=jnp.float32)


def wide_nn(a, b_pair):
    a_high, a_low = split_pair(a)
    return mat_nn(a_high, b_pair[0]) + mat_nn(a_high, b_pair[1]) + mat_nn(a_low, b_pair[0])


def shifted(values, by, lanes_rows):
    rows = values.shape[0]
    rolled = pltpu.roll(values, by % rows, 0)
    index = lax.broadcasted_iota(jnp.int32, values.shape, 0)
    keep = (index >= by) if by > 0 else (index < rows + by)
    return jnp.where(keep, rolled, 0.0)


def long_conv_kernel(backward, *refs):
    if backward:
        u_ref, dz_ref, krow_ref, tab_ref, row_ref, du_ref, mode_ref, skip_ref = refs
    else:
        u_ref, krow_ref, tab_ref, row_ref, z_ref = refs
    chans, blocks, width = u_ref.shape
    modes = tab_ref.shape[2]
    col = lax.broadcasted_iota(jnp.int32, (width, width), 1)
    row = lax.broadcasted_iota(jnp.int32, (width, width), 0)
    upper = col >= row
    lower = col <= row
    lag_ids = lax.broadcasted_iota(jnp.int32, (width, modes), 0).astype(jnp.float32)

    def one_channel(c, carry):
        u_narrow = u_ref[c]
        tabs = tab_ref[c]
        rows = row_ref[c]
        krow = krow_ref[c]
        fall_end = (tabs[0], tabs[1])
        fall_start = (tabs[2], tabs[3])
        gain_fwd = (tabs[4], tabs[5])
        gain_bwd = (tabs[6], tabs[7])
        rate_row = rows[6:7, :]
        step_row = rows[5:6, :]
        gain = rows[7:8, 0:1]
        u_wide = u_narrow.astype(jnp.float32)
        ends = mat_nt(u_narrow, fall_end[0]) + mat_nt(u_narrow, fall_end[1])
        fwd_state = ends
        level = 0
        span = 1
        while span < blocks:
            decay = rows[level : level + 1, :]
            fwd_state = fwd_state + decay * shifted(fwd_state, span, blocks)
            level += 1
            span *= 2
        state_before = shifted(fwd_state, 1, blocks)
        if not backward:
            ahead = pltpu.roll(
                jnp.broadcast_to(krow[0:1, :], (width, width)), 0, 1, stride=1, stride_axis=0
            )
            ahead = jnp.where(upper, ahead, 0.0)
            a_high, a_low = split_pair(ahead)
            z_in = mat_nn(
                jnp.concatenate([u_narrow, u_narrow], axis=1), jnp.concatenate([a_high, a_low], axis=0)
            )
            z_carry = wide_nn(state_before, gain_fwd)
            z_ref[c] = (z_in + z_carry + gain * u_wide).astype(z_ref.dtype)
            return carry
        dz_narrow = dz_ref[c]
        behind = pltpu.roll(
            jnp.broadcast_to(krow[1:2, :], (width, width)), 1, 1, stride=1, stride_axis=0
        )
        behind = jnp.where(lower, behind, 0.0)
        b_high, b_low = split_pair(behind)
        du_in = mat_nn(
            jnp.concatenate([dz_narrow, dz_narrow], axis=1), jnp.concatenate([b_high, b_low], axis=0)
        )
        starts = mat_nt(dz_narrow, fall_start[0]) + mat_nt(dz_narrow, fall_start[1])
        bwd_state = starts
        level = 0
        span = 1
        while span < blocks:
            decay = rows[level : level + 1, :]
            bwd_state = bwd_state + decay * shifted(bwd_state, -span, blocks)
            level += 1
            span *= 2
        state_after = shifted(bwd_state, -1, blocks)
        du_carry = wide_nn(state_after, gain_bwd)
        dz_wide = dz_narrow.astype(jnp.float32)
        du_ref[c] = (du_in + du_carry + gain * dz_wide).astype(du_ref.dtype)
        rise = jnp.exp(lag_ids * rate_row)
        crossed = mat_tn(u_narrow, dz_narrow)
        crossed = jnp.where(upper, crossed, 0.0)
        c_high, c_low = split_pair(crossed)
        weighted = (
            mat_nt(c_high, fall_start[0]) + mat_nt(c_high, fall_start[1]) + mat_nt(c_low, fall_start[0])
        )
        mode_in = jnp.sum(weighted * rise, axis=0, keepdims=True)
        mode_carry = jnp.sum(state_before * starts, axis=0, keepdims=True) * step_row
        mode_ref[c] = mode_in + mode_carry
        skip_ref[c] = jnp.broadcast_to(jnp.sum(u_wide * dz_wide), skip_ref.shape[1:])
        return carry

    lax.fori_loop(0, chans, one_channel, 0, unroll=chans)


def long_conv_tables(rate_rows, weight_rows, gain_rows, width, blocks):
    offsets = jnp.arange(width, dtype=jnp.float32)
    rate = rate_rows[:, :, None]
    weight = weight_rows[:, :, None]
    fall_end = jnp.exp(-rate * (width - 1.0 - offsets))
    fall_start = jnp.exp(-rate * offsets)
    gain_fwd = weight * jnp.exp(-rate * (offsets + 1.0))
    gain_bwd = weight * jnp.exp(-rate * (width - offsets))
    pairs = []
    for table in (fall_end, fall_start, gain_fwd, gain_bwd):
        high = lax.reduce_precision(table, exponent_bits=8, mantissa_bits=7)
        pairs.extend((high.astype(jnp.bfloat16), (table - high).astype(jnp.bfloat16)))
    tabs = jnp.stack(pairs, axis=1)
    levels = []
    span = 1
    while span < blocks:
        levels.append(jnp.exp(-rate_rows * (width * span)))
        span *= 2
    chan_count, modes = rate_rows.shape
    while len(levels) < 5:
        levels.append(jnp.zeros_like(rate_rows))
    levels.append(jnp.exp(-rate_rows))
    levels.append(rate_rows)
    levels.append(jnp.broadcast_to(gain_rows[:, None], (chan_count, modes)))
    lag_kernel = jnp.sum(weight * fall_start, axis=1)
    krow = jnp.stack([lag_kernel, jnp.flip(lag_kernel, axis=1)], axis=1)
    return tabs, jnp.stack(levels, axis=1), krow


def long_conv(u_blocks, dz_blocks, rate_rows, weight_rows, gain_rows, chans_per_step=16):
    chan_count, blocks, width = u_blocks.shape
    modes = rate_rows.shape[1]
    tabs, rows, krow = long_conv_tables(rate_rows, weight_rows, gain_rows, width, blocks)
    step = min(chans_per_step, chan_count)
    data_spec = pl.BlockSpec((step, blocks, width), lambda i: (i, 0, 0))
    side_specs = [
        pl.BlockSpec((step,) + krow.shape[1:], lambda i: (i, 0, 0)),
        pl.BlockSpec((step,) + tabs.shape[1:], lambda i: (i, 0, 0, 0)),
        pl.BlockSpec((step,) + rows.shape[1:], lambda i: (i, 0, 0)),
    ]
    forward = pl.pallas_call(
        partial(long_conv_kernel, False),
        grid=(chan_count // step,),
        in_specs=[data_spec] + side_specs,
        out_specs=data_spec,
        out_shape=jax.ShapeDtypeStruct(u_blocks.shape, jnp.bfloat16),
        cost_estimate=pl.CostEstimate(
            flops=chan_count * 300 * width * width * blocks, transcendentals=0,
            bytes_accessed=chan_count * blocks * width * 4 + tabs.size * 2,
        ),
    )(u_blocks, krow, tabs, rows)
    backward = pl.pallas_call(
        partial(long_conv_kernel, True),
        grid=(chan_count // step,),
        in_specs=[data_spec, data_spec] + side_specs,
        out_specs=[
            data_spec,
            pl.BlockSpec((step, 1, modes), lambda i: (i, 0, 0)),
            pl.BlockSpec((step, 1, 128), lambda i: (i, 0, 0)),
        ],
        out_shape=[
            jax.ShapeDtypeStruct(u_blocks.shape, jnp.bfloat16),
            jax.ShapeDtypeStruct((chan_count, 1, modes), jnp.float32),
            jax.ShapeDtypeStruct((chan_count, 1, 128), jnp.float32),
        ],
        cost_estimate=pl.CostEstimate(
            flops=chan_count * 500 * width * width * blocks, transcendentals=chan_count * width * modes,
            bytes_accessed=chan_count * blocks * width * 6 + tabs.size * 2,
        ),
    )(u_blocks, dz_blocks, krow, tabs, rows)
    return (forward,) + tuple(backward)


def grouped(function, arrays, group_size):
    stacked = tuple(
        (
            item.reshape((item.shape[0] // group_size, group_size) + item.shape[1:])
            for item in arrays
        )
    )
    results = lax.map(function, stacked)
    return tuple(
        (item.reshape((item.shape[0] * item.shape[1],) + item.shape[2:]) for item in results)
    )


def on_device(projected, cotangent, short_filter, residues, decay_rate, skip_gain):
    proj_rows = projected[0]
    token_count = proj_rows.shape[2]
    chans_tp = proj_rows.shape[1]
    rim_width = short_filter.shape[1] - 1
    tp_count = lax.axis_size("tp")
    if tp_count == 2:
        tp_index = lax.axis_index("tp")
        grad_rows = cotangent[0]
        mine = lax.dynamic_slice_in_dim(grad_rows, tp_index * chans_tp, chans_tp, 0)
        other = lax.dynamic_slice_in_dim(grad_rows, (1 - tp_index) * chans_tp, chans_tp, 0)
        theirs = lax.ppermute(other, "tp", [(0, 1), (1, 0)])
        first = jnp.where(tp_index == 0, mine, theirs)
        second = jnp.where(tp_index == 0, theirs, mine)
        grad_out = jnp.concatenate([first, second], axis=1).astype(jnp.float32)
    else:
        grad_out = lax.all_to_all(
            cotangent[0], "tp", split_axis=0, concat_axis=1, tiled=True
        ).astype(jnp.float32)
    prev_rim = from_behind(proj_rows[:, :, token_count - rim_width :], "ctx", 1)
    featured = lax.optimization_barrier(
        causal_short(proj_rows, prev_rim, short_filter).astype(jnp.bfloat16)
    )
    query_feat = featured[0].astype(jnp.float32)
    key_feat = featured[1].astype(jnp.float32)
    value_feat = featured[2].astype(jnp.float32)
    product = (key_feat * value_feat).astype(jnp.bfloat16)
    adjoint = (grad_out * query_feat).astype(jnp.bfloat16)
    ctx_count = lax.axis_size("ctx")
    token_total = token_count * ctx_count * lax.axis_size("dp")
    weight_all = residues * jnp.sqrt(2.0 * decay_rate)
    product_all, adjoint_all = (
        lax.all_to_all(product, "ctx", split_axis=0, concat_axis=1, tiled=True),
        lax.all_to_all(adjoint, "ctx", split_axis=0, concat_axis=1, tiled=True),
    )
    chan_count = chans_tp // ctx_count
    chan_start = lax.axis_index("ctx") * chan_count
    rate_rows = lax.dynamic_slice_in_dim(decay_rate, chan_start, chan_count, 0)
    weight_rows = lax.dynamic_slice_in_dim(weight_all, chan_start, chan_count, 0)
    gain_rows = lax.dynamic_slice_in_dim(skip_gain, chan_start, chan_count, 0)
    rate_rows, weight_rows, gain_rows, product_all = lax.optimization_barrier(
        (rate_rows, weight_rows, gain_rows, product_all)
    )
    length = product_all.shape[1]
    block_len = math.gcd(256, length)
    block_count = length // block_len
    conv_blocks, back_blocks, mode_part, skip_part = long_conv(
        product_all.reshape(chan_count, block_count, block_len),
        adjoint_all.reshape(chan_count, block_count, block_len),
        rate_rows,
        weight_rows,
        gain_rows,
    )
    conv_rows = conv_blocks.reshape(chan_count, length)
    back_rows = back_blocks.reshape(chan_count, length)
    mode_part = mode_part[:, 0, :]
    skip_part = skip_part[:, 0, 0]
    signal, back_signal = (
        lax.all_to_all(conv_rows, "ctx", split_axis=1, concat_axis=0, tiled=True),
        lax.all_to_all(back_rows, "ctx", split_axis=1, concat_axis=0, tiled=True),
    )
    grad_scale = 1.0 / math.sqrt(token_total)
    local_grads = jnp.concatenate(
        [mode_part * jnp.sqrt(2.0 * rate_rows) * grad_scale, skip_part[:, None] * grad_scale], axis=1
    )
    dp_count = lax.axis_size("dp")
    if dp_count & (dp_count - 1) == 0:
        hop = 1
        while hop < dp_count:
            partners = [(i, i ^ hop) for i in range(dp_count)]
            local_grads = local_grads + lax.ppermute(local_grads, "dp", partners)
            hop *= 2
    else:
        local_grads = lax.psum(local_grads, "dp")
    if ctx_count & (ctx_count - 1) == 0:
        ctx_index = lax.axis_index("ctx")
        gathered = local_grads
        hop = 1
        while hop < ctx_count:
            partners = [(i, i ^ hop) for i in range(ctx_count)]
            theirs = lax.ppermute(gathered, "ctx", partners)
            low_side = (ctx_index & hop) == 0
            gathered = jnp.where(
                low_side,
                jnp.concatenate([gathered, theirs], axis=0),
                jnp.concatenate([theirs, gathered], axis=0),
            )
            hop *= 2
    else:
        spread = jnp.broadcast_to(local_grads[None], (ctx_count,) + local_grads.shape)
        gathered = lax.all_to_all(spread, "ctx", split_axis=0, concat_axis=0, tiled=True)
    gathered = gathered.reshape(chans_tp, local_grads.shape[1])
    residue_grad = gathered[:, : mode_part.shape[1]]
    skip_grad = gathered[:, mode_part.shape[1]]
    conv_wide = signal.astype(jnp.float32)
    back_wide = back_signal.astype(jnp.float32)
    hyena_out = (query_feat * conv_wide).astype(jnp.bfloat16)
    feature_grad = jnp.stack(
        [grad_out * conv_wide, back_wide * value_feat, back_wide * key_feat]
    ).astype(jnp.bfloat16)
    next_rim = from_behind(feature_grad[:, :, :rim_width], "ctx", -1)
    input_grad = anticausal_short(feature_grad, next_rim, short_filter).astype(jnp.bfloat16)
    return (hyena_out[None], input_grad[None], residue_grad, skip_grad)


def solution(mesh):
    placed = (
        P("dp", None, "tp", "ctx"),
        P("dp", None, ("ctx", "tp")),
        P(None, None, "tp"),
        P("tp", None),
        P("tp", None),
        P("tp"),
    )
    return jax.shard_map(
        on_device,
        mesh=mesh,
        in_specs=placed,
        out_specs=(P("dp", "tp", "ctx"), P("dp", None, "tp", "ctx"), P("tp", None), P("tp")),
        check_vma=False,
    )
```

```python
from functools import partial
import math

import jax
import jax.numpy as jnp
from jax import lax
from jax.sharding import PartitionSpec as P
from jax.experimental import pallas as pl
from jax.experimental.pallas import tpu as pltpu

exact_mode = lax.Precision.HIGHEST
data_mode = lax.Precision.HIGH


def from_behind(shard, axis, by):
    count = lax.axis_size(axis)
    pairs = [(i, i + by) for i in range(count) if 0 <= i + by < count]
    return lax.ppermute(shard, axis, pairs)


def causal_short(proj_rows, prev_rim, tap_weights):
    rim_width = prev_rim.shape[2]
    token_count = proj_rows.shape[2]
    extended = jnp.concatenate([prev_rim, proj_rows], axis=2).astype(jnp.float32)
    result = tap_weights[:, 0, :, None] * extended[:, :, rim_width : rim_width + token_count]
    for lag_index in range(1, rim_width + 1):
        start_at = rim_width - lag_index
        result = (
            result
            + tap_weights[:, lag_index, :, None] * extended[:, :, start_at : start_at + token_count]
        )
    return result


def anticausal_short(grad_rows, next_rim, tap_weights):
    rim_width = next_rim.shape[2]
    token_count = grad_rows.shape[2]
    extended = jnp.concatenate([grad_rows, next_rim], axis=2).astype(jnp.float32)
    result = tap_weights[:, 0, :, None] * extended[:, :, :token_count]
    for lag_index in range(1, rim_width + 1):
        result = (
            result
            + tap_weights[:, lag_index, :, None]
            * extended[:, :, lag_index : lag_index + token_count]
        )
    return result


def make_tables(rate_rows, block_len):
    offsets = jnp.arange(block_len, dtype=jnp.float32)
    fall_now = jnp.exp(-rate_rows[:, :, None] * offsets)
    rise_now = jnp.exp(rate_rows[:, :, None] * offsets)
    fall_next = jnp.exp(-rate_rows[:, :, None] * (offsets + 1.0))
    fall_tail = jnp.exp(-rate_rows[:, :, None] * (block_len - 1.0 - offsets))
    lower_mask = offsets[:, None] >= offsets[None, :]
    return (fall_now, rise_now, fall_next, fall_tail, lower_mask)


def chain_link(earlier, later):
    return (earlier[0] * later[0], later[0] * earlier[1] + later[1])


def modal_pass(signal, rate_rows, weights, incoming, tables):
    fall_now, rise_now, fall_next, fall_tail, lower_mask = tables
    block_len = fall_now.shape[2]
    chan_count, length = signal.shape
    block_count = length // block_len
    pieces = signal.reshape(chan_count, block_count, block_len)
    kernel = jnp.einsum(
        "cnt,cns->cts", weights[:, :, None] * fall_now, rise_now, precision=exact_mode
    )
    kernel = jnp.where(lower_mask[None], kernel, 0.0)
    inside = jnp.einsum("cts,cbs->cbt", kernel, pieces, precision=data_mode)
    block_ends = jnp.einsum("cns,cbs->cnb", fall_tail, pieces, precision=data_mode)
    span_decay = jnp.exp(-rate_rows * block_len)
    block_mults = jnp.broadcast_to(span_decay[:, :, None], block_ends.shape)
    _, running = lax.associative_scan(chain_link, (block_mults, block_ends), axis=2)
    block_steps = jnp.arange(block_count, dtype=jnp.float32)
    before = jnp.concatenate([jnp.zeros_like(running[:, :, :1]), running[:, :, :-1]], axis=2)
    before = (
        before + jnp.exp(-rate_rows[:, :, None] * block_len * block_steps) * incoming[:, :, None]
    )
    carry_in = jnp.einsum(
        "cnt,cnb->cbt", weights[:, :, None] * fall_next, before, precision=exact_mode
    )
    return ((inside + carry_in).reshape(chan_count, length), before)


def mode_products(signal, adjoint, before, tables):
    fall_now, rise_now, fall_next, fall_tail, lower_mask = tables
    block_len = fall_now.shape[2]
    chan_count, length = signal.shape
    block_count = length // block_len
    pieces = signal.reshape(chan_count, block_count, block_len)
    dual_pieces = adjoint.reshape(chan_count, block_count, block_len)
    crossed = jnp.einsum("cbt,cbs->cts", dual_pieces, pieces, precision=data_mode)
    crossed = jnp.where(lower_mask[None], crossed, 0.0)
    weighted = jnp.einsum("cts,cnt->cns", crossed, fall_now, precision=exact_mode)
    inside = jnp.sum(weighted * rise_now, axis=2)
    carried = jnp.einsum("cbt,cnt->cnb", dual_pieces, fall_next, precision=data_mode)
    return inside + jnp.sum(carried * before, axis=2)


def channel_group(group_items, block_len):
    (
        forward_narrow,
        backward_narrow,
        rate_rows,
        weights,
        gain_rows,
        enter_forward,
        enter_backward,
    ) = group_items
    forward_rows = forward_narrow.astype(jnp.float32)
    backward_rows = backward_narrow.astype(jnp.float32)
    tables = make_tables(rate_rows, block_len)
    carried, before = modal_pass(forward_rows, rate_rows, weights, enter_forward, tables)
    returned, _ = modal_pass(jnp.flip(backward_rows, 1), rate_rows, weights, enter_backward, tables)
    signal = (carried + gain_rows[:, None] * forward_rows).astype(jnp.bfloat16)
    back_signal = (jnp.flip(returned, 1) + gain_rows[:, None] * backward_rows).astype(jnp.bfloat16)
    mode_raw = mode_products(forward_rows, backward_rows, before, tables)
    skip_raw = jnp.sum(backward_rows * forward_rows, axis=1)
    return (signal, back_signal, mode_raw, skip_raw)


def split_pair(values):
    high = values.astype(jnp.bfloat16)
    low = (values - high.astype(jnp.float32)).astype(jnp.bfloat16)
    return high, low


def mat_nn(a, b):
    return jnp.dot(a, b, preferred_element_type=jnp.float32)


def mat_nt(a, b):
    return lax.dot_general(a, b, (((1,), (1,)), ((), ())), preferred_element_type=jnp.float32)


def mat_tn(a, b):
    return lax.dot_general(a, b, (((0,), (0,)), ((), ())), preferred_element_type=jnp.float32)


def wide_nn(a, b_pair):
    a_high, a_low = split_pair(a)
    return mat_nn(a_high, b_pair[0]) + mat_nn(a_high, b_pair[1]) + mat_nn(a_low, b_pair[0])


def shifted(values, by, lanes_rows):
    rows = values.shape[0]
    rolled = pltpu.roll(values, by % rows, 0)
    index = lax.broadcasted_iota(jnp.int32, values.shape, 0)
    keep = (index >= by) if by > 0 else (index < rows + by)
    return jnp.where(keep, rolled, 0.0)


def long_conv_kernel(backward, *refs):
    if backward:
        u_ref, dz_ref, krow_ref, tab_ref, row_ref, du_ref, mode_ref, skip_ref = refs
    else:
        u_ref, krow_ref, tab_ref, row_ref, z_ref = refs
    chans, blocks, width = u_ref.shape
    modes = tab_ref.shape[2]
    col = lax.broadcasted_iota(jnp.int32, (width, width), 1)
    row = lax.broadcasted_iota(jnp.int32, (width, width), 0)
    upper = col >= row
    lower = col <= row
    lag_ids = lax.broadcasted_iota(jnp.int32, (width, modes), 0).astype(jnp.float32)

    def one_channel(c, carry):
        u_narrow = u_ref[c]
        tabs = tab_ref[c]
        rows = row_ref[c]
        krow = krow_ref[c]
        fall_end = (tabs[0], tabs[1])
        fall_start = (tabs[2], tabs[3])
        gain_fwd = (tabs[4], tabs[5])
        gain_bwd = (tabs[6], tabs[7])
        rate_row = rows[6:7, :]
        step_row = rows[5:6, :]
        gain = rows[7:8, 0:1]
        u_wide = u_narrow.astype(jnp.float32)
        ends = mat_nt(u_narrow, fall_end[0]) + mat_nt(u_narrow, fall_end[1])
        fwd_state = ends
        level = 0
        span = 1
        while span < blocks:
            decay = rows[level : level + 1, :]
            fwd_state = fwd_state + decay * shifted(fwd_state, span, blocks)
            level += 1
            span *= 2
        state_before = shifted(fwd_state, 1, blocks)
        if not backward:
            ahead = pltpu.roll(
                jnp.broadcast_to(krow[0:1, :], (width, width)), 0, 1, stride=1, stride_axis=0
            )
            ahead = jnp.where(upper, ahead, 0.0)
            a_high, a_low = split_pair(ahead)
            z_in = mat_nn(
                jnp.concatenate([u_narrow, u_narrow], axis=1), jnp.concatenate([a_high, a_low], axis=0)
            )
            z_carry = wide_nn(state_before, gain_fwd)
            z_ref[c] = (z_in + z_carry + gain * u_wide).astype(z_ref.dtype)
            return carry
        dz_narrow = dz_ref[c]
        behind = pltpu.roll(
            jnp.broadcast_to(krow[1:2, :], (width, width)), 1, 1, stride=1, stride_axis=0
        )
        behind = jnp.where(lower, behind, 0.0)
        b_high, b_low = split_pair(behind)
        du_in = mat_nn(
            jnp.concatenate([dz_narrow, dz_narrow], axis=1), jnp.concatenate([b_high, b_low], axis=0)
        )
        starts = mat_nt(dz_narrow, fall_start[0]) + mat_nt(dz_narrow, fall_start[1])
        bwd_state = starts
        level = 0
        span = 1
        while span < blocks:
            decay = rows[level : level + 1, :]
            bwd_state = bwd_state + decay * shifted(bwd_state, -span, blocks)
            level += 1
            span *= 2
        state_after = shifted(bwd_state, -1, blocks)
        du_carry = wide_nn(state_after, gain_bwd)
        dz_wide = dz_narrow.astype(jnp.float32)
        du_ref[c] = (du_in + du_carry + gain * dz_wide).astype(du_ref.dtype)
        rise = jnp.exp(lag_ids * rate_row)
        crossed = mat_tn(u_narrow, dz_narrow)
        crossed = jnp.where(upper, crossed, 0.0)
        c_high, c_low = split_pair(crossed)
        weighted = (
            mat_nt(c_high, fall_start[0]) + mat_nt(c_high, fall_start[1]) + mat_nt(c_low, fall_start[0])
        )
        mode_in = jnp.sum(weighted * rise, axis=0, keepdims=True)
        mode_carry = jnp.sum(state_before * starts, axis=0, keepdims=True) * step_row
        mode_ref[c] = mode_in + mode_carry
        skip_ref[c] = jnp.broadcast_to(jnp.sum(u_wide * dz_wide), skip_ref.shape[1:])
        return carry

    lax.fori_loop(0, chans, one_channel, 0, unroll=chans)


def long_conv_tables(rate_rows, weight_rows, gain_rows, width, blocks):
    offsets = jnp.arange(width, dtype=jnp.float32)
    rate = rate_rows[:, :, None]
    weight = weight_rows[:, :, None]
    fall_end = jnp.exp(-rate * (width - 1.0 - offsets))
    fall_start = jnp.exp(-rate * offsets)
    gain_fwd = weight * jnp.exp(-rate * (offsets + 1.0))
    gain_bwd = weight * jnp.exp(-rate * (width - offsets))
    pairs = []
    for table in (fall_end, fall_start, gain_fwd, gain_bwd):
        high = lax.reduce_precision(table, exponent_bits=8, mantissa_bits=7)
        pairs.extend((high.astype(jnp.bfloat16), (table - high).astype(jnp.bfloat16)))
    tabs = jnp.stack(pairs, axis=1)
    levels = []
    span = 1
    while span < blocks:
        levels.append(jnp.exp(-rate_rows * (width * span)))
        span *= 2
    chan_count, modes = rate_rows.shape
    while len(levels) < 5:
        levels.append(jnp.zeros_like(rate_rows))
    levels.append(jnp.exp(-rate_rows))
    levels.append(rate_rows)
    levels.append(jnp.broadcast_to(gain_rows[:, None], (chan_count, modes)))
    lag_kernel = jnp.sum(weight * fall_start, axis=1)
    krow = jnp.stack([lag_kernel, jnp.flip(lag_kernel, axis=1)], axis=1)
    return tabs, jnp.stack(levels, axis=1), krow


def long_conv(u_blocks, dz_blocks, rate_rows, weight_rows, gain_rows, chans_per_step=16):
    chan_count, blocks, width = u_blocks.shape
    modes = rate_rows.shape[1]
    tabs, rows, krow = long_conv_tables(rate_rows, weight_rows, gain_rows, width, blocks)
    step = min(chans_per_step, chan_count)
    data_spec = pl.BlockSpec((step, blocks, width), lambda i: (i, 0, 0))
    side_specs = [
        pl.BlockSpec((step,) + krow.shape[1:], lambda i: (i, 0, 0)),
        pl.BlockSpec((step,) + tabs.shape[1:], lambda i: (i, 0, 0, 0)),
        pl.BlockSpec((step,) + rows.shape[1:], lambda i: (i, 0, 0)),
    ]
    forward = pl.pallas_call(
        partial(long_conv_kernel, False),
        grid=(chan_count // step,),
        in_specs=[data_spec] + side_specs,
        out_specs=data_spec,
        out_shape=jax.ShapeDtypeStruct(u_blocks.shape, jnp.bfloat16),
        cost_estimate=pl.CostEstimate(
            flops=chan_count * 300 * width * width * blocks, transcendentals=0,
            bytes_accessed=chan_count * blocks * width * 4 + tabs.size * 2,
        ),
    )(u_blocks, krow, tabs, rows)
    backward = pl.pallas_call(
        partial(long_conv_kernel, True),
        grid=(chan_count // step,),
        in_specs=[data_spec, data_spec] + side_specs,
        out_specs=[
            data_spec,
            pl.BlockSpec((step, 1, modes), lambda i: (i, 0, 0)),
            pl.BlockSpec((step, 1, 128), lambda i: (i, 0, 0)),
        ],
        out_shape=[
            jax.ShapeDtypeStruct(u_blocks.shape, jnp.bfloat16),
            jax.ShapeDtypeStruct((chan_count, 1, modes), jnp.float32),
            jax.ShapeDtypeStruct((chan_count, 1, 128), jnp.float32),
        ],
        cost_estimate=pl.CostEstimate(
            flops=chan_count * 500 * width * width * blocks, transcendentals=chan_count * width * modes,
            bytes_accessed=chan_count * blocks * width * 6 + tabs.size * 2,
        ),
    )(u_blocks, dz_blocks, krow, tabs, rows)
    return (forward,) + tuple(backward)


def grouped(function, arrays, group_size):
    stacked = tuple(
        (
            item.reshape((item.shape[0] // group_size, group_size) + item.shape[1:])
            for item in arrays
        )
    )
    results = lax.map(function, stacked)
    return tuple(
        (item.reshape((item.shape[0] * item.shape[1],) + item.shape[2:]) for item in results)
    )


def on_device(projected, cotangent, short_filter, residues, decay_rate, skip_gain):
    proj_rows = projected[0]
    token_count = proj_rows.shape[2]
    chans_tp = proj_rows.shape[1]
    rim_width = short_filter.shape[1] - 1
    tp_count = lax.axis_size("tp")
    if tp_count == 2:
        tp_index = lax.axis_index("tp")
        grad_rows = cotangent[0]
        mine = lax.dynamic_slice_in_dim(grad_rows, tp_index * chans_tp, chans_tp, 0)
        other = lax.dynamic_slice_in_dim(grad_rows, (1 - tp_index) * chans_tp, chans_tp, 0)
        theirs = lax.ppermute(other, "tp", [(0, 1), (1, 0)])
        first = jnp.where(tp_index == 0, mine, theirs)
        second = jnp.where(tp_index == 0, theirs, mine)
        grad_out = jnp.concatenate([first, second], axis=1).astype(jnp.float32)
    else:
        grad_out = lax.all_to_all(
            cotangent[0], "tp", split_axis=0, concat_axis=1, tiled=True
        ).astype(jnp.float32)
    prev_rim = from_behind(proj_rows[:, :, token_count - rim_width :], "ctx", 1)
    featured = lax.optimization_barrier(
        causal_short(proj_rows, prev_rim, short_filter).astype(jnp.bfloat16)
    )
    query_feat = featured[0].astype(jnp.float32)
    key_feat = featured[1].astype(jnp.float32)
    value_feat = featured[2].astype(jnp.float32)
    product = (key_feat * value_feat).astype(jnp.bfloat16)
    adjoint = (grad_out * query_feat).astype(jnp.bfloat16)
    ctx_count = lax.axis_size("ctx")
    token_total = token_count * ctx_count * lax.axis_size("dp")
    weight_all = residues * jnp.sqrt(2.0 * decay_rate)
    product_all, adjoint_all = (
        lax.all_to_all(product, "ctx", split_axis=0, concat_axis=1, tiled=True),
        lax.all_to_all(adjoint, "ctx", split_axis=0, concat_axis=1, tiled=True),
    )
    chan_count = chans_tp // ctx_count
    chan_start = lax.axis_index("ctx") * chan_count
    rate_rows = lax.dynamic_slice_in_dim(decay_rate, chan_start, chan_count, 0)
    weight_rows = lax.dynamic_slice_in_dim(weight_all, chan_start, chan_count, 0)
    gain_rows = lax.dynamic_slice_in_dim(skip_gain, chan_start, chan_count, 0)
    length = product_all.shape[1]
    block_len = math.gcd(256, length)
    block_count = length // block_len
    conv_blocks, back_blocks, mode_part, skip_part = long_conv(
        product_all.reshape(chan_count, block_count, block_len),
        adjoint_all.reshape(chan_count, block_count, block_len),
        rate_rows,
        weight_rows,
        gain_rows,
    )
    conv_rows = conv_blocks.reshape(chan_count, length)
    back_rows = back_blocks.reshape(chan_count, length)
    mode_part = mode_part[:, 0, :]
    skip_part = skip_part[:, 0, 0]
    signal, back_signal = (
        lax.all_to_all(conv_rows, "ctx", split_axis=1, concat_axis=0, tiled=True),
        lax.all_to_all(back_rows, "ctx", split_axis=1, concat_axis=0, tiled=True),
    )
    grad_scale = 1.0 / math.sqrt(token_total)
    local_grads = jnp.concatenate(
        [mode_part * jnp.sqrt(2.0 * rate_rows) * grad_scale, skip_part[:, None] * grad_scale], axis=1
    )
    dp_count = lax.axis_size("dp")
    if dp_count & (dp_count - 1) == 0:
        hop = 1
        while hop < dp_count:
            partners = [(i, i ^ hop) for i in range(dp_count)]
            local_grads = local_grads + lax.ppermute(local_grads, "dp", partners)
            hop *= 2
    else:
        local_grads = lax.psum(local_grads, "dp")
    if False:
        ctx_index = lax.axis_index("ctx")
        gathered = local_grads
        hop = 1
        while hop < ctx_count:
            partners = [(i, i ^ hop) for i in range(ctx_count)]
            theirs = lax.ppermute(gathered, "ctx", partners)
            low_side = (ctx_index & hop) == 0
            gathered = jnp.where(
                low_side,
                jnp.concatenate([gathered, theirs], axis=0),
                jnp.concatenate([theirs, gathered], axis=0),
            )
            hop *= 2
    else:
        spread = jnp.broadcast_to(local_grads[None], (ctx_count,) + local_grads.shape)
        gathered = lax.all_to_all(spread, "ctx", split_axis=0, concat_axis=0, tiled=True)
    gathered = gathered.reshape(chans_tp, local_grads.shape[1])
    residue_grad = gathered[:, : mode_part.shape[1]]
    skip_grad = gathered[:, mode_part.shape[1]]
    conv_wide = signal.astype(jnp.float32)
    back_wide = back_signal.astype(jnp.float32)
    hyena_out = (query_feat * conv_wide).astype(jnp.bfloat16)
    feature_grad = jnp.stack(
        [grad_out * conv_wide, back_wide * value_feat, back_wide * key_feat]
    ).astype(jnp.bfloat16)
    next_rim = from_behind(feature_grad[:, :, :rim_width], "ctx", -1)
    input_grad = anticausal_short(feature_grad, next_rim, short_filter).astype(jnp.bfloat16)
    return (hyena_out[None], input_grad[None], residue_grad, skip_grad)


def solution(mesh):
    placed = (
        P("dp", None, "tp", "ctx"),
        P("dp", None, ("ctx", "tp")),
        P(None, None, "tp"),
        P("tp", None),
        P("tp", None),
        P("tp"),
    )
    return jax.shard_map(
        on_device,
        mesh=mesh,
        in_specs=placed,
        out_specs=(P("dp", "tp", "ctx"), P("dp", None, "tp", "ctx"), P("tp", None), P("tp")),
        check_vma=False,
    )
```
